32 devices in a mesh: gx: 4 (over x, core), gy: 8 (over z, y).
Axes of the slice: x: 2, y: 2, z: 4, core: 2. Of those that a mesh axis runs over, the one named last changes fastest.
Arguments:
- velocity: float32 [3, 8, 64, 2048], P(None, None, 'gx', 'gy'), may hold values from -6 to 6
- bulk: float32 [8, 64, 2048], P(None, 'gx', 'gy'), may hold values from 0.5 to 4
- prestress: float32 [8, 64, 2048], P(None, 'gx', 'gy'), may hold values from -6 to 6
- node_mass: float32 [8, 64, 2048], P(None, 'gx', 'gy'), may hold values from 0.5 to 2
- slave_pos: float32 [4096, 3, 128], P(('gx', 'gy')), may hold values from -1 to 1
- slave_area: float32 [4096, 128], P(('gx', 'gy')), may hold values from 0.5 to 2
- seg_count: int32 [4096], P(('gx', 'gy')), may hold values from 1 to 128, as said below
- slave_node: int32 [4096, 128], P(('gx', 'gy')), may hold values from 0 to 32767
- pair_owner: int32 [4096, 1], P(('gx', 'gy')), may hold values from 0 to 31; in each aligned block of 128 rows (0 to 127, 128 to 255, ...) at most 5 rows name the same one
- pair_master: int32 [4096], P(('gx', 'gy')), may hold values from 0 to 31
- master_cent: float32 [1024, 3, 128], P(('gx', 'gy')), may hold values from -1 to 1
- master_tilt: float32 [1024, 2, 128], P(('gx', 'gy')), may hold values from -3 to 3
- master_stiff: float32 [1024, 128], P(('gx', 'gy')), may hold values from 0.05 to 0.5
- master_node: int32 [1024, 128], P(('gx', 'gy')), may hold values from 0 to 32767
Outputs:
- velocity_new: float32 [3, 8, 64, 2048], P(None, None, 'gx', 'gy')
- node_rate: float32 [8, 64, 2048], P(None, 'gx', 'gy')
The draws below stay inside these ranges and needn't reach their ends.
Inputs may be any that keep to these rules, and one draw needn't show every extreme that they name: Slots from seg_count on are padding; some block is full. `pair_owner`: owner index is its gx index times 8 plus its gy index. Among the 128 slave blocks of one device no owner is named more than 5 times, a bound that some block reaches.
All inputs are finite; a program needn't handle non-finite values.
Results may differ from the reference program's by a relative error of at most 0.000084.
Values sent between devices are 32-bit elements; how exact they have to be, the bound alone decides.
No kernel may reach another device: no remote copies, remote signals or barrier semaphores. Data moves between devices by JAX's collectives and lax.ppermute only.
A program may use at most 128 MiB of HBM per device.

```python
import math
import jax
import jax.numpy as jnp
import numpy as np
from jax import lax

LZ = 8
CX = 16
CY = 256
NB = 128
NMB = 32
SEG = 128
MOST = 5
NX = 64
NY = 2048
NODES_DEV = 32768
SLAVE_BLOCKS = 4096
MASTER_BLOCKS = 1024
N_GX = 4
N_GY = 8


def draw_seg_count(key, part):
    counts = jax.random.randint(key, (SLAVE_BLOCKS,), 1, SEG + 1, dtype=jnp.int32)
    return counts.at[0].set(SEG)


def touch_ends(entries, own_key, least, top_value):
    extent = entries.shape
    index_at = [jax.random.randint(jax.random.fold_in(own_key, axis), (), 0, extent[axis]) for axis in range(len(extent))]
    entries = entries.at[tuple(index_at)].set(least)
    longest = extent.index(max(extent))
    index_at[longest] = (index_at[longest] + 1) % extent[longest]
    return entries.at[tuple(index_at)].set(top_value)


def block_scale(stream_key, dims, cuts, least, top_value):
    factor_of = 1.0
    for position, parts in cuts:
        steps = jax.random.uniform(jax.random.fold_in(jax.random.fold_in(stream_key, 6), position), (parts,), jnp.float32, least / len(cuts), top_value / len(cuts))
        factor_of = factor_of * jnp.repeat(jnp.exp(steps), dims[position] // parts).reshape((-1,) + (1,) * (len(dims) - 1 - position))
    return factor_of


def deal_out(key, own, number, rows, count, top, bound, skew):
    sequence = jax.random.permutation(key, count)
    heavy_load, usual = portions_of(count, rows * top, bound, skew, True), portions_of(count, rows * top, bound, skew, False)
    places = jnp.arange(count)

    def named(tallies, offset_by):
        used = int((tallies > 0).sum())
        fixed = max(1, used // 4)
        shifted = fixed + (places - fixed + offset_by * (used - fixed)) % max(1, count - fixed)
        return jnp.zeros((count,), jnp.int32).at[sequence[jnp.where(places < fixed, places, shifted)]].set(jnp.asarray(tallies, jnp.int32))

    tallies = jnp.where(number % 4 == 0, named(heavy_load, number // 4), named(usual, number - number // 4 - 1))
    mixed = jax.random.permutation(jax.random.fold_in(own, 3), count)
    donor, sink = mixed[0:count // 2 * 2:2], mixed[1:count // 2 * 2:2]
    margin = jnp.minimum(tallies[donor] - 1, bound - tallies[sink]) // 2
    margin = jnp.where((donor == sequence[0]) | (sink == sequence[0]) | (tallies[sink] == 0), 0, jnp.maximum(margin, 0))
    shifted = jax.random.randint(jax.random.fold_in(own, 4), (count // 2,), 0, 1 << 20) % (margin + 1)
    tallies = tallies.at[donor].add(-shifted).at[sink].add(shifted)
    labels = jnp.searchsorted(jnp.cumsum(tallies), jnp.arange(rows * top), side="right").astype(jnp.int32)
    grid = labels.reshape(top, rows).T
    grid = grid[jax.random.permutation(jax.random.fold_in(own, 1), rows)]
    offset_by = jax.random.randint(jax.random.fold_in(own, 2), (rows, 1), 0, top)
    return jnp.take_along_axis(grid, (jnp.arange(top)[None, :] + offset_by) % top, axis=1)


def portions_of(amount, total, most, slope, full):
    portions = [(1 << 20) // math.isqrt(standing ** slope) + 1 for standing in range(1, amount + 1)]
    largest = most if full else min(most, max(-(-total // amount), total * portions[0] // sum(portions)))
    least = 1 if total - largest >= amount - 1 else 0
    given, surplus = [largest] + [least] * (amount - 1), total - largest - least * (amount - 1)
    while surplus > 0:
        candidates = [i for i in range(1, amount) if given[i] < largest] or [i for i in range(1, amount) if given[i] < most]
        mass, left = sum([portions[i] for i in candidates]), surplus
        for i in candidates:
            extra = min(most - given[i], max(1, left * portions[i] // mass), surplus)
            given[i] = given[i] + extra
            surplus = surplus - extra
    return np.array(given)


def normal_values(stream_key, extent, spread, most, split=(), kind=jnp.bfloat16):
    loudness = block_scale(stream_key, extent, split, -0.22, 0.18) if split else 1.0
    entries = jax.random.normal(stream_key, extent, jnp.float32) * spread * loudness
    return jnp.minimum(jnp.maximum(entries, -most), most).astype(kind)


def setup_inputs(seed: int = 0) -> dict:
    streams_of = jax.random.split(jax.random.key(seed), 15)
    velocity = normal_values(streams_of[0], (3, LZ, NX, NY), 1.0, 6.0, ((2, 4), (3, 8)), jnp.float32)
    bulk = jnp.clip(jnp.exp(math.log(4.0) - 2.0794415 * jax.random.uniform(streams_of[1], (LZ, NX, NY), jnp.float32) ** block_scale(streams_of[1], (LZ, NX, NY), ((1, 4), (2, 8)), -0.2, 0.2)), 0.5, 4.0)
    prestress = normal_values(streams_of[2], (LZ, NX, NY), 1.0, 6.0, ((1, 4), (2, 8)), jnp.float32)
    node_mass = jnp.clip(jnp.exp(math.log(2.0) - 1.3862944 * jax.random.uniform(streams_of[3], (LZ, NX, NY), jnp.float32) ** block_scale(streams_of[3], (LZ, NX, NY), ((1, 4), (2, 8)), -0.2, 0.2)), 0.5, 2.0)
    slave_pos = jnp.clip(jax.random.uniform(streams_of[4], (SLAVE_BLOCKS, 3, SEG), jnp.float32, -1.0, 1.0) * block_scale(streams_of[4], (SLAVE_BLOCKS, 3, SEG), ((0, 32),), -0.4, 0.0), -1.0, 1.0)
    slave_area = jnp.clip(jnp.exp(math.log(2.0) - 1.3862944 * jax.random.uniform(streams_of[5], (SLAVE_BLOCKS, SEG), jnp.float32) ** block_scale(streams_of[5], (SLAVE_BLOCKS, SEG), ((0, 32),), -0.2, 0.2)), 0.5, 2.0)
    seg_count = draw_seg_count(jax.random.fold_in(streams_of[14], 71), 0)
    slave_node = touch_ends(jax.random.randint(streams_of[7], (SLAVE_BLOCKS, SEG), 0, NODES_DEV), jax.random.fold_in(streams_of[7], 1), 0, NODES_DEV - 1).astype(jnp.int32)
    pair_owner_keys = jax.random.split(jax.random.fold_in(streams_of[8], 1), SLAVE_BLOCKS // NB)
    pair_owner_turns = jax.random.permutation(jax.random.fold_in(streams_of[8], 3), SLAVE_BLOCKS // NB)
    pair_owner = jax.vmap(lambda own, number: deal_out(jax.random.fold_in(streams_of[8], 2), own, number, NB, N_GX * N_GY, 1, MOST, 2))(pair_owner_keys, pair_owner_turns).reshape((SLAVE_BLOCKS, 1))
    pair_master = touch_ends(jax.random.randint(streams_of[9], (SLAVE_BLOCKS,), 0, NMB), jax.random.fold_in(streams_of[9], 1), 0, NMB - 1).astype(jnp.int32)
    master_cent = jnp.clip(jax.random.uniform(streams_of[10], (MASTER_BLOCKS, 3, SEG), jnp.float32, -1.0, 1.0) * block_scale(streams_of[10], (MASTER_BLOCKS, 3, SEG), ((0, 32),), -0.4, 0.0), -1.0, 1.0)
    master_tilt = normal_values(streams_of[11], (MASTER_BLOCKS, 2, SEG), 0.5, 3.0, ((0, 32),), jnp.float32)
    master_stiff = jnp.clip(jnp.exp(math.log(0.5) - 2.3025851 * jax.random.uniform(streams_of[12], (MASTER_BLOCKS, SEG), jnp.float32) ** block_scale(streams_of[12], (MASTER_BLOCKS, SEG), ((0, 32),), -0.2, 0.2)), 0.05, 0.5)
    master_node = touch_ends(jax.random.randint(streams_of[13], (MASTER_BLOCKS, SEG), 0, NODES_DEV), jax.random.fold_in(streams_of[13], 1), 0, NODES_DEV - 1).astype(jnp.int32)
    return dict(velocity=velocity, bulk=bulk, prestress=prestress, node_mass=node_mass, slave_pos=slave_pos, slave_area=slave_area, seg_count=seg_count, slave_node=slave_node, pair_owner=pair_owner, pair_master=pair_master, master_cent=master_cent, master_tilt=master_tilt, master_stiff=master_stiff, master_node=master_node)


TIME_STEP = 0.25
VISCOUS = 0.5
SOFT_GAP = 0.2
REACH_SQ = 1.0
DAMPING = 0.5

def pair_mean(values, along):
    length = values.shape[along]
    return 0.5 * (lax.slice_in_dim(values, 0, length - 1, axis=along) + lax.slice_in_dim(values, 1, length, axis=along))

def pair_diff(values, along):
    length = values.shape[along]
    return lax.slice_in_dim(values, 1, length, axis=along) - lax.slice_in_dim(values, 0, length - 1, axis=along)

def pair_prod(values, along):
    length = values.shape[along]
    return lax.slice_in_dim(values, 0, length - 1, axis=along) * lax.slice_in_dim(values, 1, length, axis=along)

def corner_mean(values):
    return pair_mean(pair_mean(pair_mean(values, 0), 1), 2)

def zone_rate(vel):
    rate_x = pair_diff(pair_mean(pair_mean(vel[0], 0), 2), 1)
    rate_y = pair_diff(pair_mean(pair_mean(vel[1], 0), 1), 2)
    rate_z = pair_diff(pair_mean(pair_mean(vel[2], 1), 2), 0)
    return rate_x + rate_y + rate_z

def stress_forces(padded):
    inside = pair_prod(pair_prod(pair_prod(padded[5], 0), 1), 2)
    strain = TIME_STEP * zone_rate(padded[0:3])
    pressure = inside * (corner_mean(padded[4]) + corner_mean(padded[3]) * (VISCOUS * strain * strain - strain))
    framed = jnp.pad(pressure, ((1, 1), (0, 0), (0, 0)))
    force_x = -pair_diff(pair_mean(pair_mean(framed, 0), 2), 1)
    force_y = -pair_diff(pair_mean(pair_mean(framed, 0), 1), 2)
    force_z = -pair_diff(pair_mean(pair_mean(framed, 1), 2), 0)
    return (jnp.stack([force_x, force_y, force_z], axis=0), inside)

def nodal_rate(padded_vel, inside):
    rate = inside * zone_rate(padded_vel)
    framed = jnp.pad(rate, ((1, 1), (0, 0), (0, 0)))
    return pair_mean(pair_mean(pair_mean(framed, 0), 1), 2)

def contact_pairs(slave, master):
    delta_x = slave[:, 0, :, None] - master[:, 0, None, :]
    delta_y = slave[:, 1, :, None] - master[:, 1, None, :]
    delta_z = slave[:, 2, :, None] - master[:, 2, None, :]
    normal_x = master[:, 3, None, :]
    normal_y = master[:, 4, None, :]
    normal_z = master[:, 5, None, :]
    dist_sq = delta_x * delta_x + delta_y * delta_y + delta_z * delta_z
    gap_normal = normal_x * delta_x + normal_y * delta_y + normal_z * delta_z
    closing = normal_x * (slave[:, 3, :, None] - master[:, 6, None, :]) + normal_y * (slave[:, 4, :, None] - master[:, 7, None, :]) + normal_z * (slave[:, 5, :, None] - master[:, 8, None, :])
    weight = jnp.exp(-dist_sq / REACH_SQ)
    depth_soft = SOFT_GAP * jax.nn.softplus(-gap_normal / SOFT_GAP)
    push_force = slave[:, 6, :, None] * master[:, 9, None, :] * weight * depth_soft * (1.0 + DAMPING * jnp.tanh(-closing))
    slave_force = jnp.stack([lax.optimization_barrier(jnp.sum(push_force * normal_x, axis=2)), lax.optimization_barrier(jnp.sum(push_force * normal_y, axis=2)), lax.optimization_barrier(jnp.sum(push_force * normal_z, axis=2))], axis=1)
    reaction = lax.optimization_barrier(jnp.sum(push_force, axis=1))
    return (slave_force, reaction)

def master_normals(master_tilt):
    scale = lax.rsqrt(1.0 + master_tilt[:, 0] * master_tilt[:, 0] + master_tilt[:, 1] * master_tilt[:, 1])
    return jnp.stack([master_tilt[:, 0] * scale, master_tilt[:, 1] * scale, scale], axis=1)

def reference(velocity, bulk, prestress, node_mass, slave_pos, slave_area, seg_count, slave_node, pair_owner, pair_master, master_cent, master_tilt, master_stiff, master_node):
    devices = N_GX * N_GY
    node_total = LZ * CX * CY

    def to_blocks(nodal):
        channels = nodal.shape[0]
        blocked = nodal.reshape(channels, LZ, N_GX, CX, N_GY, CY).transpose(0, 2, 4, 1, 3, 5)
        return blocked.reshape(channels, devices * node_total)

    def from_blocks(flattened):
        channels = flattened.shape[0]
        blocked = flattened.reshape(channels, N_GX, N_GY, LZ, CX, CY).transpose(0, 3, 1, 4, 2, 5)
        return blocked.reshape(channels, LZ, NX, NY)
    vel_flat = to_blocks(velocity)
    slave_gid = (jnp.arange(SLAVE_BLOCKS, dtype=jnp.int32) // NB * node_total)[:, None] + slave_node.astype(jnp.int32)
    master_gid = (jnp.arange(MASTER_BLOCKS, dtype=jnp.int32) // NMB * node_total)[:, None] + master_node.astype(jnp.int32)
    slave_vel = vel_flat[:, slave_gid].transpose(1, 0, 2)
    master_vel = vel_flat[:, master_gid].transpose(1, 0, 2)
    live_mask = jnp.arange(SEG, dtype=jnp.int32)[None, :] < seg_count[:, None]
    area_live = jnp.where(live_mask, slave_area, jnp.zeros_like(slave_area))
    slave = jnp.concatenate([slave_pos + TIME_STEP * slave_vel, slave_vel, area_live[:, None, :]], axis=1)
    normals = master_normals(master_tilt)
    master_data = jnp.concatenate([master_cent + TIME_STEP * master_vel, normals, master_vel, master_stiff[:, None, :]], axis=1)
    target = (pair_owner[:, 0] * NMB + pair_master).astype(jnp.int32)
    paired = master_data[target]

    def per_device(pairing):
        return contact_pairs(pairing[0], pairing[1])
    forces, reaction = lax.map(per_device, (slave.reshape(devices, NB, 7, SEG), paired.reshape(devices, NB, 10, SEG)))
    forces = forces.reshape(SLAVE_BLOCKS, 3, SEG)
    reaction = reaction.reshape(SLAVE_BLOCKS, SEG)
    master_sum = jax.ops.segment_sum(reaction, target, num_segments=MASTER_BLOCKS)
    master_force = -master_sum[:, None, :] * normals
    contact = jnp.zeros((3, devices * node_total), jnp.float32)
    contact = contact.at[:, slave_gid.reshape(-1)].add(forces.transpose(1, 0, 2).reshape(3, -1))
    contact = contact.at[:, master_gid.reshape(-1)].add(master_force.transpose(1, 0, 2).reshape(3, -1))
    contact_field = from_blocks(contact)
    stacked = jnp.concatenate([velocity, bulk[None], prestress[None], jnp.ones_like(bulk)[None]], axis=0)
    padded = jnp.pad(stacked, ((0, 0), (0, 0), (1, 1), (1, 1)))
    stress, inside = stress_forces(padded)
    velocity_new = velocity + TIME_STEP * (stress + contact_field) / node_mass[None]
    padded_new = jnp.pad(velocity_new, ((0, 0), (0, 0), (1, 1), (1, 1)))
    node_rate = nodal_rate(padded_new, inside)
    return (velocity_new, node_rate)
```

```python
import jax
import jax.numpy as jnp
from jax import lax
from jax.sharding import PartitionSpec as P
from jax.experimental import pallas as pl
from jax.experimental.pallas import tpu as pltpu

LANES = 128
TILE = 2048


def split_pieces(values):
    first = values.astype(jnp.bfloat16)
    rest = values - first.astype(jnp.float32)
    second = rest.astype(jnp.bfloat16)
    third = (rest - second.astype(jnp.float32)).astype(jnp.bfloat16)
    return (first, second, third)


def gather_kernel(index_ref, table_ref, out_ref):
    node = index_ref[...]
    width = node.shape[1]
    high_count = table_ref.shape[1]
    channels = out_ref.shape[0]
    onehot = (
        lax.broadcasted_iota(jnp.int32, (high_count, width), 0) == (node >> 7)
    ).astype(jnp.bfloat16)
    gathered = None
    for piece in split_pieces(table_ref[...]):
        part = jnp.dot(piece, onehot, preferred_element_type=jnp.float32)
        gathered = part if gathered is None else gathered + part
    low_hit = lax.broadcasted_iota(jnp.int32, (LANES, width), 0) == (node & (LANES - 1))
    for c in range(channels):
        block = gathered[c * LANES : (c + 1) * LANES]
        out_ref[c : c + 1, :] = jnp.sum(jnp.where(low_hit, block, 0.0), axis=0, keepdims=True)


def scatter_kernel(index_ref, force_ref, out_ref):
    @pl.when(pl.program_id(0) == 0)
    def _():
        out_ref[...] = jnp.zeros_like(out_ref)

    node = index_ref[...]
    width = node.shape[1]
    high_count = out_ref.shape[1]
    channels = force_ref.shape[0]
    onehot = (
        lax.broadcasted_iota(jnp.int32, (high_count, width), 0) == (node >> 7)
    ).astype(jnp.bfloat16)
    low_hit = lax.broadcasted_iota(jnp.int32, (LANES, width), 0) == (node & (LANES - 1))
    total = None
    for piece in split_pieces(force_ref[...]):
        spread = jnp.concatenate(
            [jnp.where(low_hit, piece[c : c + 1, :], jnp.zeros_like(piece[c : c + 1, :])) for c in range(channels)],
            axis=0,
        )
        part = lax.dot_general(
            spread, onehot, (((1,), (1,)), ((), ())), preferred_element_type=jnp.float32
        )
        total = part if total is None else total + part
    out_ref[...] += total


def node_gather(field, nodes):
    channels, node_total = field.shape
    high_count = node_total // LANES
    table = field.reshape(channels, high_count, LANES).transpose(0, 2, 1).reshape(
        channels * LANES, high_count
    )
    count = nodes.shape[0]
    padded_count = -(-count // TILE) * TILE
    nodes = jnp.pad(nodes, (0, padded_count - count))
    return pl.pallas_call(
        gather_kernel,
        grid=(padded_count // TILE,),
        in_specs=[
            pl.BlockSpec((1, TILE), lambda i: (0, i)),
            pl.BlockSpec((channels * LANES, high_count), lambda i: (0, 0)),
        ],
        out_specs=pl.BlockSpec((channels, TILE), lambda i: (0, i)),
        out_shape=jax.ShapeDtypeStruct((channels, padded_count), jnp.float32),
    )(nodes.reshape(1, padded_count), table)[:, :count]


def node_scatter_add(forces, nodes, node_total):
    channels, count = forces.shape
    high_count = node_total // LANES
    padded_count = -(-count // TILE) * TILE
    nodes = jnp.pad(nodes, (0, padded_count - count))
    forces = jnp.pad(forces, ((0, 0), (0, padded_count - count)))
    summed = pl.pallas_call(
        scatter_kernel,
        grid=(padded_count // TILE,),
        in_specs=[
            pl.BlockSpec((1, TILE), lambda i: (0, i)),
            pl.BlockSpec((channels, TILE), lambda i: (0, i)),
        ],
        out_specs=pl.BlockSpec((channels * LANES, high_count), lambda i: (0, 0)),
        out_shape=jax.ShapeDtypeStruct((channels * LANES, high_count), jnp.float32),
    )(nodes.reshape(1, padded_count), forces)
    return summed.reshape(channels, LANES, high_count).transpose(0, 2, 1).reshape(channels, node_total)


TIME_STEP = 0.25
VISCOUS = 0.5
SOFT_GAP = 0.2
REACH_SQ = 1.0
DAMPING = 0.5


def padded_2(block, sides, width):
    for axis, dim in sides:
        count = lax.axis_size(axis)
        forward = [(i, i + 1) for i in range(count - 1)]
        backward = [(target, source) for source, target in forward]
        low = lax.ppermute(
            lax.slice_in_dim(block, block.shape[dim] - width, None, axis=dim), axis, forward
        )
        high = lax.ppermute(lax.slice_in_dim(block, 0, width, axis=dim), axis, backward)
        block = jnp.concatenate([low, block, high], axis=dim)
    return block


def pair_mean(values, along):
    length = values.shape[along]
    return 0.5 * (
        lax.slice_in_dim(values, 0, length - 1, axis=along)
        + lax.slice_in_dim(values, 1, length, axis=along)
    )


def pair_diff(values, along):
    length = values.shape[along]
    return lax.slice_in_dim(values, 1, length, axis=along) - lax.slice_in_dim(
        values, 0, length - 1, axis=along
    )


def pair_prod(values, along):
    length = values.shape[along]
    return lax.slice_in_dim(values, 0, length - 1, axis=along) * lax.slice_in_dim(
        values, 1, length, axis=along
    )


def corner_mean(values):
    return pair_mean(pair_mean(pair_mean(values, 0), 1), 2)


def zone_rate(vel):
    rate_x = pair_diff(pair_mean(pair_mean(vel[0], 0), 2), 1)
    rate_y = pair_diff(pair_mean(pair_mean(vel[1], 0), 1), 2)
    rate_z = pair_diff(pair_mean(pair_mean(vel[2], 1), 2), 0)
    return rate_x + rate_y + rate_z


def stress_forces(padded):
    inside = pair_prod(pair_prod(pair_prod(padded[5], 0), 1), 2)
    strain = TIME_STEP * zone_rate(padded[0:3])
    pressure = inside * (
        corner_mean(padded[4]) + corner_mean(padded[3]) * (VISCOUS * strain * strain - strain)
    )
    framed = jnp.pad(pressure, ((1, 1), (0, 0), (0, 0)))
    force_x = -pair_diff(pair_mean(pair_mean(framed, 0), 2), 1)
    force_y = -pair_diff(pair_mean(pair_mean(framed, 0), 1), 2)
    force_z = -pair_diff(pair_mean(pair_mean(framed, 1), 2), 0)
    return (jnp.stack([force_x, force_y, force_z], axis=0), inside)


def nodal_rate(padded_vel, inside):
    rate = inside * zone_rate(padded_vel)
    framed = jnp.pad(rate, ((1, 1), (0, 0), (0, 0)))
    return pair_mean(pair_mean(pair_mean(framed, 0), 1), 2)


def contact_pairs(slave, master):
    delta_x = slave[:, 0, :, None] - master[:, 0, None, :]
    delta_y = slave[:, 1, :, None] - master[:, 1, None, :]
    delta_z = slave[:, 2, :, None] - master[:, 2, None, :]
    normal_x = master[:, 3, None, :]
    normal_y = master[:, 4, None, :]
    normal_z = master[:, 5, None, :]
    dist_sq = delta_x * delta_x + delta_y * delta_y + delta_z * delta_z
    gap_normal = normal_x * delta_x + normal_y * delta_y + normal_z * delta_z
    closing = (
        normal_x * (slave[:, 3, :, None] - master[:, 6, None, :])
        + normal_y * (slave[:, 4, :, None] - master[:, 7, None, :])
        + normal_z * (slave[:, 5, :, None] - master[:, 8, None, :])
    )
    weight = jnp.exp(-dist_sq / REACH_SQ)
    depth_soft = SOFT_GAP * jax.nn.softplus(-gap_normal / SOFT_GAP)
    push_force = (
        slave[:, 6, :, None]
        * master[:, 9, None, :]
        * weight
        * depth_soft
        * (1.0 + DAMPING * jnp.tanh(-closing))
    )
    slave_force = jnp.stack(
        [
            jnp.sum(push_force * normal_x, axis=2),
            jnp.sum(push_force * normal_y, axis=2),
            jnp.sum(push_force * normal_z, axis=2),
        ],
        axis=1,
    )
    reaction = jnp.sum(push_force, axis=1)
    return (slave_force, reaction)


def master_normals(master_tilt):
    scale = lax.rsqrt(
        1.0 + master_tilt[:, 0] * master_tilt[:, 0] + master_tilt[:, 1] * master_tilt[:, 1]
    )
    return jnp.stack([master_tilt[:, 0] * scale, master_tilt[:, 1] * scale, scale], axis=1)


def on_device(
    velocity,
    bulk,
    prestress,
    node_mass,
    slave_pos,
    slave_area,
    seg_count,
    slave_node,
    pair_owner,
    pair_master,
    master_cent,
    master_tilt,
    master_stiff,
    master_node,
):
    count_gx = lax.axis_size("gx")
    count_gy = lax.axis_size("gy")
    devices = count_gx * count_gy
    layers, row_cells, col_cells = bulk.shape
    node_total = layers * row_cells * col_cells
    block_total, _, seg_width = slave_pos.shape
    master_total = master_cent.shape[0]
    slot_depth = (block_total + devices - 1) // devices + 1
    stacked = jnp.concatenate(
        [velocity, bulk[None], prestress[None], jnp.ones_like(bulk)[None]], axis=0
    )
    padded = padded_2(stacked, (("gx", 2), ("gy", 3)), 1)
    stress, inside = stress_forces(padded)
    vel_flat = velocity.reshape(3, node_total)
    slave_count = block_total * seg_width
    all_nodes = jnp.concatenate([slave_node.reshape(-1), master_node.reshape(-1)])
    picked_vel = node_gather(vel_flat, all_nodes)
    slave_vel = picked_vel[:, :slave_count].reshape(3, block_total, seg_width).transpose(1, 0, 2)
    master_vel = picked_vel[:, slave_count:].reshape(3, master_total, seg_width).transpose(1, 0, 2)
    live_mask = jnp.arange(seg_width, dtype=jnp.int32)[None, :] < seg_count[:, None]
    area_live = jnp.where(live_mask, slave_area, jnp.zeros_like(slave_area))
    slave = jnp.concatenate(
        [slave_pos + TIME_STEP * slave_vel, slave_vel, area_live[:, None, :]], axis=1
    )
    normals = master_normals(master_tilt)
    master_data = jnp.concatenate(
        [master_cent + TIME_STEP * master_vel, normals, master_vel, master_stiff[:, None, :]],
        axis=1,
    )
    owners = pair_owner[:, 0]
    positions = jnp.arange(block_total, dtype=jnp.int32)
    earlier = (owners[:, None] == owners[None, :]) & (positions[None, :] < positions[:, None])
    slot_index = jnp.sum(earlier.astype(jnp.int32), axis=1)
    target_slot = owners * slot_depth + slot_index
    slot_hit = target_slot[None, :] == jnp.arange(devices * slot_depth, dtype=jnp.int32)[:, None]
    source = jnp.sum(jnp.where(slot_hit, positions[None, :], 0), axis=1)
    filled = jnp.any(slot_hit, axis=1)
    outgoing = jnp.where(filled[:, None, None], jnp.take(slave, source, axis=0), 0.0)
    chosen = jnp.where(filled, jnp.take(pair_master, source, axis=0), 0)
    arrived, picked = (
        lax.all_to_all(
            outgoing.reshape(devices, slot_depth, 7, seg_width),
            ("gx", "gy"),
            split_axis=0,
            concat_axis=0,
            tiled=True,
        ),
        lax.all_to_all(
            chosen.reshape(devices, slot_depth),
            ("gx", "gy"),
            split_axis=0,
            concat_axis=0,
            tiled=True,
        ),
    )
    item_total = devices * slot_depth
    arrived = arrived.reshape(item_total, 7, seg_width)
    picked = picked.reshape(item_total)
    paired = jnp.take(master_data, picked, axis=0)
    group_size = 16 * slot_depth

    def per_group(pairing):
        return contact_pairs(pairing[0], pairing[1])

    forces, reaction = lax.map(
        per_group,
        (
            arrived.reshape(item_total // group_size, group_size, 7, seg_width),
            paired.reshape(item_total // group_size, group_size, 10, seg_width),
        ),
    )
    forces = forces.reshape(item_total, 3, seg_width)
    reaction = reaction.reshape(item_total, seg_width)
    onehot = (picked[:, None] == jnp.arange(master_total, dtype=jnp.int32)[None, :]).astype(
        jnp.float32
    )
    master_sum = jnp.dot(onehot.T, reaction, precision=lax.Precision.HIGHEST)
    master_force = -master_sum[:, None, :] * normals
    returned = lax.all_to_all(
        forces.reshape(devices, slot_depth, 3, seg_width),
        ("gx", "gy"),
        split_axis=0,
        concat_axis=0,
        tiled=True,
    )
    slave_force = jnp.take(returned.reshape(item_total, 3, seg_width), target_slot, axis=0)
    all_forces = jnp.concatenate(
        [slave_force.transpose(1, 0, 2).reshape(3, -1), master_force.transpose(1, 0, 2).reshape(3, -1)],
        axis=1,
    )
    contact = node_scatter_add(all_forces, all_nodes, node_total)
    contact_field = contact.reshape(3, layers, row_cells, col_cells)
    velocity_new = velocity + TIME_STEP * (stress + contact_field) / node_mass[None]
    padded_new = padded_2(velocity_new, (("gx", 2), ("gy", 3)), 1)
    node_rate = nodal_rate(padded_new, inside)
    return (velocity_new, node_rate)


def solution(mesh):
    placed = (
        P(None, None, "gx", "gy"),
        P(None, "gx", "gy"),
        P(None, "gx", "gy"),
        P(None, "gx", "gy"),
        P(("gx", "gy"), None, None),
        P(("gx", "gy"), None),
        P(("gx", "gy")),
        P(("gx", "gy"), None),
        P(("gx", "gy"), None),
        P(("gx", "gy")),
        P(("gx", "gy"), None, None),
        P(("gx", "gy"), None, None),
        P(("gx", "gy"), None),
        P(("gx", "gy"), None),
    )
    return jax.shard_map(
        on_device,
        mesh=mesh,
        in_specs=placed,
        out_specs=(P(None, None, "gx", "gy"), P(None, "gx", "gy")),
        check_vma=False,
    )
```

```python
import jax
import jax.numpy as jnp
from jax import lax
from jax.sharding import PartitionSpec as P
from jax.experimental import pallas as pl
from jax.experimental.pallas import tpu as pltpu

LANES = 128
TILE = 2048


def split_pieces(values):
    first = values.astype(jnp.bfloat16)
    rest = values - first.astype(jnp.float32)
    second = rest.astype(jnp.bfloat16)
    third = (rest - second.astype(jnp.float32)).astype(jnp.bfloat16)
    return (first, second, third)


def gather_kernel(index_ref, table_ref, out_ref):
    node = index_ref[...]
    width = node.shape[1]
    high_count = table_ref.shape[1]
    channels = out_ref.shape[0]
    onehot = (
        lax.broadcasted_iota(jnp.int32, (high_count, width), 0) == (node >> 7)
    ).astype(jnp.bfloat16)
    gathered = None
    for piece in split_pieces(table_ref[...]):
        part = jnp.dot(piece, onehot, preferred_element_type=jnp.float32)
        gathered = part if gathered is None else gathered + part
    low_hit = lax.broadcasted_iota(jnp.int32, (LANES, width), 0) == (node & (LANES - 1))
    for c in range(channels):
        block = gathered[c * LANES : (c + 1) * LANES]
        out_ref[c : c + 1, :] = jnp.sum(jnp.where(low_hit, block, 0.0), axis=0, keepdims=True)


def scatter_kernel(index_ref, force_ref, out_ref):
    @pl.when(pl.program_id(0) == 0)
    def _():
        out_ref[...] = jnp.zeros_like(out_ref)

    node = index_ref[...]
    width = node.shape[1]
    high_count = out_ref.shape[1]
    channels = force_ref.shape[0]
    onehot = (
        lax.broadcasted_iota(jnp.int32, (high_count, width), 0) == (node >> 7)
    ).astype(jnp.bfloat16)
    low_hit = lax.broadcasted_iota(jnp.int32, (LANES, width), 0) == (node & (LANES - 1))
    total = None
    for piece in split_pieces(force_ref[...])[:2]:
        spread = jnp.concatenate(
            [jnp.where(low_hit, piece[c : c + 1, :], jnp.zeros_like(piece[c : c + 1, :])) for c in range(channels)],
            axis=0,
        )
        part = lax.dot_general(
            spread, onehot, (((1,), (1,)), ((), ())), preferred_element_type=jnp.float32
        )
        total = part if total is None else total + part
    out_ref[...] += total


def node_gather(field, nodes):
    channels, node_total = field.shape
    high_count = node_total // LANES
    table = field.reshape(channels, high_count, LANES).transpose(0, 2, 1).reshape(
        channels * LANES, high_count
    )
    count = nodes.shape[0]
    padded_count = -(-count // TILE) * TILE
    nodes = jnp.pad(nodes, (0, padded_count - count))
    return pl.pallas_call(
        gather_kernel,
        grid=(padded_count // TILE,),
        in_specs=[
            pl.BlockSpec((1, TILE), lambda i: (0, i)),
            pl.BlockSpec((channels * LANES, high_count), lambda i: (0, 0)),
        ],
        out_specs=pl.BlockSpec((channels, TILE), lambda i: (0, i)),
        out_shape=jax.ShapeDtypeStruct((channels, padded_count), jnp.float32),
    )(nodes.reshape(1, padded_count), table)[:, :count]


def node_scatter_add(forces, nodes, node_total):
    channels, count = forces.shape
    high_count = node_total // LANES
    padded_count = -(-count // TILE) * TILE
    nodes = jnp.pad(nodes, (0, padded_count - count))
    forces = jnp.pad(forces, ((0, 0), (0, padded_count - count)))
    summed = pl.pallas_call(
        scatter_kernel,
        grid=(padded_count // TILE,),
        in_specs=[
            pl.BlockSpec((1, TILE), lambda i: (0, i)),
            pl.BlockSpec((channels, TILE), lambda i: (0, i)),
        ],
        out_specs=pl.BlockSpec((channels * LANES, high_count), lambda i: (0, 0)),
        out_shape=jax.ShapeDtypeStruct((channels * LANES, high_count), jnp.float32),
    )(nodes.reshape(1, padded_count), forces)
    return summed.reshape(channels, LANES, high_count).transpose(0, 2, 1).reshape(channels, node_total)


TIME_STEP = 0.25
VISCOUS = 0.5
SOFT_GAP = 0.2
REACH_SQ = 1.0
DAMPING = 0.5


def halo_pad(block):
    count_x = lax.axis_size("gx")
    count_y = lax.axis_size("gy")
    down_x = [(i, i + 1) for i in range(count_x - 1)]
    up_x = [(i + 1, i) for i in range(count_x - 1)]
    down_y = [(j, j + 1) for j in range(count_y - 1)]
    up_y = [(j + 1, j) for j in range(count_y - 1)]

    def diagonal(step_x, step_y):
        pairs = []
        for i in range(count_x):
            for j in range(count_y):
                ti, tj = i + step_x, j + step_y
                if 0 <= ti < count_x and 0 <= tj < count_y:
                    pairs.append((i * count_y + j, ti * count_y + tj))
        return pairs

    last_row = block[..., -1:, :]
    first_row = block[..., :1, :]
    top = lax.ppermute(last_row, "gx", down_x)
    bottom = lax.ppermute(first_row, "gx", up_x)
    left = lax.ppermute(block[..., :, -1:], "gy", down_y)
    right = lax.ppermute(block[..., :, :1], "gy", up_y)
    both = ("gx", "gy")
    top_left = lax.ppermute(last_row[..., -1:], both, diagonal(1, 1))
    top_right = lax.ppermute(last_row[..., :1], both, diagonal(1, -1))
    bottom_left = lax.ppermute(first_row[..., -1:], both, diagonal(-1, 1))
    bottom_right = lax.ppermute(first_row[..., :1], both, diagonal(-1, -1))
    upper = jnp.concatenate([top_left, top, top_right], axis=-1)
    middle = jnp.concatenate([left, block, right], axis=-1)
    lower = jnp.concatenate([bottom_left, bottom, bottom_right], axis=-1)
    return jnp.concatenate([upper, middle, lower], axis=-2)


def pair_mean(values, along):
    length = values.shape[along]
    return 0.5 * (
        lax.slice_in_dim(values, 0, length - 1, axis=along)
        + lax.slice_in_dim(values, 1, length, axis=along)
    )


def pair_diff(values, along):
    length = values.shape[along]
    return lax.slice_in_dim(values, 1, length, axis=along) - lax.slice_in_dim(
        values, 0, length - 1, axis=along
    )


def pair_prod(values, along):
    length = values.shape[along]
    return lax.slice_in_dim(values, 0, length - 1, axis=along) * lax.slice_in_dim(
        values, 1, length, axis=along
    )


def corner_mean(values):
    return pair_mean(pair_mean(pair_mean(values, 0), 1), 2)


def zone_rate(vel):
    rate_x = pair_diff(pair_mean(pair_mean(vel[0], 0), 2), 1)
    rate_y = pair_diff(pair_mean(pair_mean(vel[1], 0), 1), 2)
    rate_z = pair_diff(pair_mean(pair_mean(vel[2], 1), 2), 0)
    return rate_x + rate_y + rate_z


def stress_forces(padded):
    inside = pair_prod(pair_prod(pair_prod(padded[5], 0), 1), 2)
    strain = TIME_STEP * zone_rate(padded[0:3])
    pressure = inside * (
        corner_mean(padded[4]) + corner_mean(padded[3]) * (VISCOUS * strain * strain - strain)
    )
    framed = jnp.pad(pressure, ((1, 1), (0, 0), (0, 0)))
    force_x = -pair_diff(pair_mean(pair_mean(framed, 0), 2), 1)
    force_y = -pair_diff(pair_mean(pair_mean(framed, 0), 1), 2)
    force_z = -pair_diff(pair_mean(pair_mean(framed, 1), 2), 0)
    return (jnp.stack([force_x, force_y, force_z], axis=0), inside)


def nodal_rate(padded_vel, inside):
    rate = inside * zone_rate(padded_vel)
    framed = jnp.pad(rate, ((1, 1), (0, 0), (0, 0)))
    return pair_mean(pair_mean(pair_mean(framed, 0), 1), 2)


def contact_pairs(slave, master):
    delta_x = slave[:, 0, :, None] - master[:, 0, None, :]
    delta_y = slave[:, 1, :, None] - master[:, 1, None, :]
    delta_z = slave[:, 2, :, None] - master[:, 2, None, :]
    normal_x = master[:, 3, None, :]
    normal_y = master[:, 4, None, :]
    normal_z = master[:, 5, None, :]
    dist_sq = delta_x * delta_x + delta_y * delta_y + delta_z * delta_z
    gap_normal = normal_x * delta_x + normal_y * delta_y + normal_z * delta_z
    closing = (
        normal_x * (slave[:, 3, :, None] - master[:, 6, None, :])
        + normal_y * (slave[:, 4, :, None] - master[:, 7, None, :])
        + normal_z * (slave[:, 5, :, None] - master[:, 8, None, :])
    )
    weight = jnp.exp(-dist_sq / REACH_SQ)
    depth_soft = SOFT_GAP * jax.nn.softplus(-gap_normal / SOFT_GAP)
    push_force = (
        slave[:, 6, :, None]
        * master[:, 9, None, :]
        * weight
        * depth_soft
        * (1.0 + DAMPING * jnp.tanh(-closing))
    )
    slave_force = jnp.stack(
        [
            jnp.sum(push_force * normal_x, axis=2),
            jnp.sum(push_force * normal_y, axis=2),
            jnp.sum(push_force * normal_z, axis=2),
        ],
        axis=1,
    )
    reaction = jnp.sum(push_force, axis=1)
    return (slave_force, reaction)


def master_normals(master_tilt):
    scale = lax.rsqrt(
        1.0 + master_tilt[:, 0] * master_tilt[:, 0] + master_tilt[:, 1] * master_tilt[:, 1]
    )
    return jnp.stack([master_tilt[:, 0] * scale, master_tilt[:, 1] * scale, scale], axis=1)


def on_device(
    velocity,
    bulk,
    prestress,
    node_mass,
    slave_pos,
    slave_area,
    seg_count,
    slave_node,
    pair_owner,
    pair_master,
    master_cent,
    master_tilt,
    master_stiff,
    master_node,
):
    count_gx = lax.axis_size("gx")
    count_gy = lax.axis_size("gy")
    devices = count_gx * count_gy
    layers, row_cells, col_cells = bulk.shape
    node_total = layers * row_cells * col_cells
    block_total, _, seg_width = slave_pos.shape
    master_total = master_cent.shape[0]
    slot_depth = (block_total + devices - 1) // devices + 1
    stacked = jnp.concatenate(
        [velocity, bulk[None], prestress[None], jnp.ones_like(bulk)[None]], axis=0
    )
    padded = halo_pad(stacked)
    stress, inside = stress_forces(padded)
    vel_flat = velocity.reshape(3, node_total)
    slave_count = block_total * seg_width
    all_nodes = jnp.concatenate([slave_node.reshape(-1), master_node.reshape(-1)])
    picked_vel = node_gather(vel_flat, all_nodes)
    slave_vel = picked_vel[:, :slave_count].reshape(3, block_total, seg_width).transpose(1, 0, 2)
    master_vel = picked_vel[:, slave_count:].reshape(3, master_total, seg_width).transpose(1, 0, 2)
    live_mask = jnp.arange(seg_width, dtype=jnp.int32)[None, :] < seg_count[:, None]
    area_live = jnp.where(live_mask, slave_area, jnp.zeros_like(slave_area))
    slave = jnp.concatenate(
        [slave_pos + TIME_STEP * slave_vel, slave_vel, area_live[:, None, :]], axis=1
    )
    normals = master_normals(master_tilt)
    master_data = jnp.concatenate(
        [master_cent + TIME_STEP * master_vel, normals, master_vel, master_stiff[:, None, :]],
        axis=1,
    )
    owners = pair_owner[:, 0]
    positions = jnp.arange(block_total, dtype=jnp.int32)
    earlier = (owners[:, None] == owners[None, :]) & (positions[None, :] < positions[:, None])
    slot_index = jnp.sum(earlier.astype(jnp.int32), axis=1)
    target_slot = owners * slot_depth + slot_index
    slot_hit = target_slot[None, :] == jnp.arange(devices * slot_depth, dtype=jnp.int32)[:, None]
    source = jnp.sum(jnp.where(slot_hit, positions[None, :], 0), axis=1)
    filled = jnp.any(slot_hit, axis=1)
    tagged = jnp.concatenate(
        [
            slave,
            jnp.broadcast_to(pair_master.astype(jnp.float32)[:, None, None], (block_total, 1, seg_width)),
        ],
        axis=1,
    )
    outgoing = jnp.where(filled[:, None, None], jnp.take(tagged, source, axis=0), 0.0)
    arrived = lax.all_to_all(
        outgoing.reshape(devices, slot_depth, 8, seg_width),
        ("gx", "gy"),
        split_axis=0,
        concat_axis=0,
        tiled=True,
    )
    item_total = devices * slot_depth
    arrived = arrived.reshape(item_total, 8, seg_width)
    picked = arrived[:, 7, 0].astype(jnp.int32)
    arrived = arrived[:, :7]
    paired = jnp.take(master_data, picked, axis=0)
    group_size = 16 * slot_depth

    def per_group(pairing):
        return contact_pairs(pairing[0], pairing[1])

    forces, reaction = lax.map(
        per_group,
        (
            arrived.reshape(item_total // group_size, group_size, 7, seg_width),
            paired.reshape(item_total // group_size, group_size, 10, seg_width),
        ),
    )
    forces = forces.reshape(item_total, 3, seg_width)
    reaction = reaction.reshape(item_total, seg_width)
    onehot = (picked[:, None] == jnp.arange(master_total, dtype=jnp.int32)[None, :]).astype(
        jnp.float32
    )
    master_sum = jnp.dot(onehot.T, reaction, precision=lax.Precision.HIGHEST)
    master_force = -master_sum[:, None, :] * normals
    returned = lax.all_to_all(
        forces.reshape(devices, slot_depth, 3, seg_width),
        ("gx", "gy"),
        split_axis=0,
        concat_axis=0,
        tiled=True,
    )
    slave_force = jnp.take(returned.reshape(item_total, 3, seg_width), target_slot, axis=0)
    all_forces = jnp.concatenate(
        [slave_force.transpose(1, 0, 2).reshape(3, -1), master_force.transpose(1, 0, 2).reshape(3, -1)],
        axis=1,
    )
    contact = node_scatter_add(all_forces, all_nodes, node_total)
    contact_field = contact.reshape(3, layers, row_cells, col_cells)
    velocity_new = velocity + TIME_STEP * (stress + contact_field) / node_mass[None]
    padded_new = halo_pad(velocity_new)
    node_rate = nodal_rate(padded_new, inside)
    return (velocity_new, node_rate)


def solution(mesh):
    placed = (
        P(None, None, "gx", "gy"),
        P(None, "gx", "gy"),
        P(None, "gx", "gy"),
        P(None, "gx", "gy"),
        P(("gx", "gy"), None, None),
        P(("gx", "gy"), None),
        P(("gx", "gy")),
        P(("gx", "gy"), None),
        P(("gx", "gy"), None),
        P(("gx", "gy")),
        P(("gx", "gy"), None, None),
        P(("gx", "gy"), None, None),
        P(("gx", "gy"), None),
        P(("gx", "gy"), None),
    )
    return jax.shard_map(
        on_device,
        mesh=mesh,
        in_specs=placed,
        out_specs=(P(None, None, "gx", "gy"), P(None, "gx", "gy")),
        check_vma=False,
    )
```

```python
import jax
import jax.numpy as jnp
from jax import lax
from jax.sharding import PartitionSpec as P
from jax.experimental import pallas as pl
from jax.experimental.pallas import tpu as pltpu

LANES = 128
TILE = 2048


def split_pieces(values):
    first = values.astype(jnp.bfloat16)
    rest = values - first.astype(jnp.float32)
    second = rest.astype(jnp.bfloat16)
    third = (rest - second.astype(jnp.float32)).astype(jnp.bfloat16)
    return (first, second, third)


def gather_kernel(index_ref, table_ref, out_ref):
    node = index_ref[...]
    width = node.shape[1]
    high_count = table_ref.shape[1]
    channels = out_ref.shape[0]
    onehot = (
        lax.broadcasted_iota(jnp.int32, (high_count, width), 0) == (node >> 7)
    ).astype(jnp.bfloat16)
    gathered = None
    for piece in split_pieces(table_ref[...]):
        part = jnp.dot(piece, onehot, preferred_element_type=jnp.float32)
        gathered = part if gathered is None else gathered + part
    low_hit = lax.broadcasted_iota(jnp.int32, (LANES, width), 0) == (node & (LANES - 1))
    for c in range(channels):
        block = gathered[c * LANES : (c + 1) * LANES]
        out_ref[c : c + 1, :] = jnp.sum(jnp.where(low_hit, block, 0.0), axis=0, keepdims=True)


def scatter_kernel(index_ref, force_ref, out_ref):
    @pl.when(pl.program_id(0) == 0)
    def _():
        out_ref[...] = jnp.zeros_like(out_ref)

    node = index_ref[...]
    width = node.shape[1]
    high_count = out_ref.shape[1]
    channels = force_ref.shape[0]
    onehot = (
        lax.broadcasted_iota(jnp.int32, (high_count, width), 0) == (node >> 7)
    ).astype(jnp.bfloat16)
    low_hit = lax.broadcasted_iota(jnp.int32, (LANES, width), 0) == (node & (LANES - 1))
    total = None
    for piece in split_pieces(force_ref[...])[:2]:
        spread = jnp.concatenate(
            [jnp.where(low_hit, piece[c : c + 1, :], jnp.zeros_like(piece[c : c + 1, :])) for c in range(channels)],
            axis=0,
        )
        part = lax.dot_general(
            spread, onehot, (((1,), (1,)), ((), ())), preferred_element_type=jnp.float32
        )
        total = part if total is None else total + part
    out_ref[...] += total


def node_gather(field, nodes):
    channels, node_total = field.shape
    high_count = node_total // LANES
    table = field.reshape(channels, high_count, LANES).transpose(0, 2, 1).reshape(
        channels * LANES, high_count
    )
    count = nodes.shape[0]
    padded_count = -(-count // TILE) * TILE
    nodes = jnp.pad(nodes, (0, padded_count - count))
    return pl.pallas_call(
        gather_kernel,
        grid=(padded_count // TILE,),
        in_specs=[
            pl.BlockSpec((1, TILE), lambda i: (0, i)),
            pl.BlockSpec((channels * LANES, high_count), lambda i: (0, 0)),
        ],
        out_specs=pl.BlockSpec((channels, TILE), lambda i: (0, i)),
        out_shape=jax.ShapeDtypeStruct((channels, padded_count), jnp.float32),
    )(nodes.reshape(1, padded_count), table)[:, :count]


def node_scatter_add(forces, nodes, node_total):
    channels, count = forces.shape
    high_count = node_total // LANES
    padded_count = -(-count // TILE) * TILE
    nodes = jnp.pad(nodes, (0, padded_count - count))
    forces = jnp.pad(forces, ((0, 0), (0, padded_count - count)))
    summed = pl.pallas_call(
        scatter_kernel,
        grid=(padded_count // TILE,),
        in_specs=[
            pl.BlockSpec((1, TILE), lambda i: (0, i)),
            pl.BlockSpec((channels, TILE), lambda i: (0, i)),
        ],
        out_specs=pl.BlockSpec((channels * LANES, high_count), lambda i: (0, 0)),
        out_shape=jax.ShapeDtypeStruct((channels * LANES, high_count), jnp.float32),
    )(nodes.reshape(1, padded_count), forces)
    return summed.reshape(channels, LANES, high_count).transpose(0, 2, 1).reshape(channels, node_total)


TIME_STEP = 0.25
VISCOUS = 0.5
SOFT_GAP = 0.2
REACH_SQ = 1.0
DAMPING = 0.5


def padded_2(block, sides, width):
    for axis, dim in sides:
        count = lax.axis_size(axis)
        forward = [(i, i + 1) for i in range(count - 1)]
        backward = [(target, source) for source, target in forward]
        low = lax.ppermute(
            lax.slice_in_dim(block, block.shape[dim] - width, None, axis=dim), axis, forward
        )
        high = lax.ppermute(lax.slice_in_dim(block, 0, width, axis=dim), axis, backward)
        block = jnp.concatenate([low, block, high], axis=dim)
    return block


def pair_mean(values, along):
    length = values.shape[along]
    return 0.5 * (
        lax.slice_in_dim(values, 0, length - 1, axis=along)
        + lax.slice_in_dim(values, 1, length, axis=along)
    )


def pair_diff(values, along):
    length = values.shape[along]
    return lax.slice_in_dim(values, 1, length, axis=along) - lax.slice_in_dim(
        values, 0, length - 1, axis=along
    )


def pair_prod(values, along):
    length = values.shape[along]
    return lax.slice_in_dim(values, 0, length - 1, axis=along) * lax.slice_in_dim(
        values, 1, length, axis=along
    )


def corner_mean(values):
    return pair_mean(pair_mean(pair_mean(values, 0), 1), 2)


def zone_rate(vel):
    rate_x = pair_diff(pair_mean(pair_mean(vel[0], 0), 2), 1)
    rate_y = pair_diff(pair_mean(pair_mean(vel[1], 0), 1), 2)
    rate_z = pair_diff(pair_mean(pair_mean(vel[2], 1), 2), 0)
    return rate_x + rate_y + rate_z


def stress_forces(padded):
    inside = pair_prod(pair_prod(pair_prod(padded[5], 0), 1), 2)
    strain = TIME_STEP * zone_rate(padded[0:3])
    pressure = inside * (
        corner_mean(padded[4]) + corner_mean(padded[3]) * (VISCOUS * strain * strain - strain)
    )
    framed = jnp.pad(pressure, ((1, 1), (0, 0), (0, 0)))
    force_x = -pair_diff(pair_mean(pair_mean(framed, 0), 2), 1)
    force_y = -pair_diff(pair_mean(pair_mean(framed, 0), 1), 2)
    force_z = -pair_diff(pair_mean(pair_mean(framed, 1), 2), 0)
    return (jnp.stack([force_x, force_y, force_z], axis=0), inside)


def nodal_rate(padded_vel, inside):
    rate = inside * zone_rate(padded_vel)
    framed = jnp.pad(rate, ((1, 1), (0, 0), (0, 0)))
    return pair_mean(pair_mean(pair_mean(framed, 0), 1), 2)


def contact_pairs(slave, master):
    delta_x = slave[:, 0, :, None] - master[:, 0, None, :]
    delta_y = slave[:, 1, :, None] - master[:, 1, None, :]
    delta_z = slave[:, 2, :, None] - master[:, 2, None, :]
    normal_x = master[:, 3, None, :]
    normal_y = master[:, 4, None, :]
    normal_z = master[:, 5, None, :]
    dist_sq = delta_x * delta_x + delta_y * delta_y + delta_z * delta_z
    gap_normal = normal_x * delta_x + normal_y * delta_y + normal_z * delta_z
    closing = (
        normal_x * (slave[:, 3, :, None] - master[:, 6, None, :])
        + normal_y * (slave[:, 4, :, None] - master[:, 7, None, :])
        + normal_z * (slave[:, 5, :, None] - master[:, 8, None, :])
    )
    weight = jnp.exp(-dist_sq / REACH_SQ)
    depth_soft = SOFT_GAP * jax.nn.softplus(-gap_normal / SOFT_GAP)
    push_force = (
        slave[:, 6, :, None]
        * master[:, 9, None, :]
        * weight
        * depth_soft
        * (1.0 + DAMPING * jnp.tanh(-closing))
    )
    slave_force = jnp.stack(
        [
            jnp.sum(push_force * normal_x, axis=2),
            jnp.sum(push_force * normal_y, axis=2),
            jnp.sum(push_force * normal_z, axis=2),
        ],
        axis=1,
    )
    reaction = jnp.sum(push_force, axis=1)
    return (slave_force, reaction)


def master_normals(master_tilt):
    scale = lax.rsqrt(
        1.0 + master_tilt[:, 0] * master_tilt[:, 0] + master_tilt[:, 1] * master_tilt[:, 1]
    )
    return jnp.stack([master_tilt[:, 0] * scale, master_tilt[:, 1] * scale, scale], axis=1)


def on_device(
    velocity,
    bulk,
    prestress,
    node_mass,
    slave_pos,
    slave_area,
    seg_count,
    slave_node,
    pair_owner,
    pair_master,
    master_cent,
    master_tilt,
    master_stiff,
    master_node,
):
    count_gx = lax.axis_size("gx")
    count_gy = lax.axis_size("gy")
    devices = count_gx * count_gy
    layers, row_cells, col_cells = bulk.shape
    node_total = layers * row_cells * col_cells
    block_total, _, seg_width = slave_pos.shape
    master_total = master_cent.shape[0]
    slot_depth = (block_total + devices - 1) // devices + 1
    stacked = jnp.concatenate(
        [velocity, bulk[None], prestress[None], jnp.ones_like(bulk)[None]], axis=0
    )
    padded = padded_2(stacked, (("gx", 2), ("gy", 3)), 1)
    stress, inside = stress_forces(padded)
    vel_flat = velocity.reshape(3, node_total)
    slave_count = block_total * seg_width
    all_nodes = jnp.concatenate([slave_node.reshape(-1), master_node.reshape(-1)])
    picked_vel = node_gather(vel_flat, all_nodes)
    slave_vel = picked_vel[:, :slave_count].reshape(3, block_total, seg_width).transpose(1, 0, 2)
    master_vel = picked_vel[:, slave_count:].reshape(3, master_total, seg_width).transpose(1, 0, 2)
    live_mask = jnp.arange(seg_width, dtype=jnp.int32)[None, :] < seg_count[:, None]
    area_live = jnp.where(live_mask, slave_area, jnp.zeros_like(slave_area))
    slave = jnp.concatenate(
        [slave_pos + TIME_STEP * slave_vel, slave_vel, area_live[:, None, :]], axis=1
    )
    normals = master_normals(master_tilt)
    master_data = jnp.concatenate(
        [master_cent + TIME_STEP * master_vel, normals, master_vel, master_stiff[:, None, :]],
        axis=1,
    )
    owners = pair_owner[:, 0]
    positions = jnp.arange(block_total, dtype=jnp.int32)
    earlier = (owners[:, None] == owners[None, :]) & (positions[None, :] < positions[:, None])
    slot_index = jnp.sum(earlier.astype(jnp.int32), axis=1)
    target_slot = owners * slot_depth + slot_index
    slot_hit = target_slot[None, :] == jnp.arange(devices * slot_depth, dtype=jnp.int32)[:, None]
    source = jnp.sum(jnp.where(slot_hit, positions[None, :], 0), axis=1)
    filled = jnp.any(slot_hit, axis=1)
    tagged = jnp.concatenate(
        [
            slave,
            jnp.broadcast_to(pair_master.astype(jnp.float32)[:, None, None], (block_total, 1, seg_width)),
        ],
        axis=1,
    )
    outgoing = jnp.where(filled[:, None, None], jnp.take(tagged, source, axis=0), 0.0)
    arrived = lax.all_to_all(
        outgoing.reshape(devices, slot_depth, 8, seg_width),
        ("gx", "gy"),
        split_axis=0,
        concat_axis=0,
        tiled=True,
    )
    item_total = devices * slot_depth
    arrived = arrived.reshape(item_total, 8, seg_width)
    picked = arrived[:, 7, 0].astype(jnp.int32)
    arrived = arrived[:, :7]
    paired = jnp.take(master_data, picked, axis=0)
    group_size = 16 * slot_depth

    def per_group(pairing):
        return contact_pairs(pairing[0], pairing[1])

    forces, reaction = lax.map(
        per_group,
        (
            arrived.reshape(item_total // group_size, group_size, 7, seg_width),
            paired.reshape(item_total // group_size, group_size, 10, seg_width),
        ),
    )
    forces = forces.reshape(item_total, 3, seg_width)
    reaction = reaction.reshape(item_total, seg_width)
    onehot = (picked[:, None] == jnp.arange(master_total, dtype=jnp.int32)[None, :]).astype(
        jnp.float32
    )
    master_sum = jnp.dot(onehot.T, reaction, precision=lax.Precision.HIGHEST)
    master_force = -master_sum[:, None, :] * normals
    returned = lax.all_to_all(
        forces.reshape(devices, slot_depth, 3, seg_width),
        ("gx", "gy"),
        split_axis=0,
        concat_axis=0,
        tiled=True,
    )
    slave_force = jnp.take(returned.reshape(item_total, 3, seg_width), target_slot, axis=0)
    all_forces = jnp.concatenate(
        [slave_force.transpose(1, 0, 2).reshape(3, -1), master_force.transpose(1, 0, 2).reshape(3, -1)],
        axis=1,
    )
    contact = node_scatter_add(all_forces, all_nodes, node_total)
    contact_field = contact.reshape(3, layers, row_cells, col_cells)
    velocity_new = velocity + TIME_STEP * (stress + contact_field) / node_mass[None]
    padded_new = padded_2(velocity_new, (("gx", 2), ("gy", 3)), 1)
    node_rate = nodal_rate(padded_new, inside)
    return (velocity_new, node_rate)


def solution(mesh):
    placed = (
        P(None, None, "gx", "gy"),
        P(None, "gx", "gy"),
        P(None, "gx", "gy"),
        P(None, "gx", "gy"),
        P(("gx", "gy"), None, None),
        P(("gx", "gy"), None),
        P(("gx", "gy")),
        P(("gx", "gy"), None),
        P(("gx", "gy"), None),
        P(("gx", "gy")),
        P(("gx", "gy"), None, None),
        P(("gx", "gy"), None, None),
        P(("gx", "gy"), None),
        P(("gx", "gy"), None),
    )
    return jax.shard_map(
        on_device,
        mesh=mesh,
        in_specs=placed,
        out_specs=(P(None, None, "gx", "gy"), P(None, "gx", "gy")),
        check_vma=False,
    )
```

```python
import math

import jax
import jax.numpy as jnp
from jax import lax
from jax.sharding import PartitionSpec as P
from jax.experimental import pallas as pl
from jax.experimental.pallas import tpu as pltpu

LANES = 128
TILE = 2048


def split_pieces(values):
    first = values.astype(jnp.bfloat16)
    rest = values - first.astype(jnp.float32)
    second = rest.astype(jnp.bfloat16)
    third = (rest - second.astype(jnp.float32)).astype(jnp.bfloat16)
    return (first, second, third)


def gather_kernel(index_ref, table_ref, out_ref):
    node = index_ref[...]
    width = node.shape[1]
    high_count = table_ref.shape[1]
    channels = out_ref.shape[0]
    onehot = (
        lax.broadcasted_iota(jnp.int32, (high_count, width), 0) == (node >> 7)
    ).astype(jnp.bfloat16)
    gathered = None
    for piece in split_pieces(table_ref[...]):
        part = jnp.dot(piece, onehot, preferred_element_type=jnp.float32)
        gathered = part if gathered is None else gathered + part
    low_hit = lax.broadcasted_iota(jnp.int32, (LANES, width), 0) == (node & (LANES - 1))
    for c in range(channels):
        block = gathered[c * LANES : (c + 1) * LANES]
        out_ref[c : c + 1, :] = jnp.sum(jnp.where(low_hit, block, 0.0), axis=0, keepdims=True)


def scatter_kernel(index_ref, force_ref, out_ref):
    @pl.when(pl.program_id(0) == 0)
    def _():
        out_ref[...] = jnp.zeros_like(out_ref)

    node = index_ref[...]
    width = node.shape[1]
    high_count = out_ref.shape[1]
    channels = force_ref.shape[0]
    onehot = (
        lax.broadcasted_iota(jnp.int32, (high_count, width), 0) == (node >> 7)
    ).astype(jnp.bfloat16)
    low_hit = lax.broadcasted_iota(jnp.int32, (LANES, width), 0) == (node & (LANES - 1))
    total = None
    for piece in split_pieces(force_ref[...])[:2]:
        spread = jnp.concatenate(
            [jnp.where(low_hit, piece[c : c + 1, :], jnp.zeros_like(piece[c : c + 1, :])) for c in range(channels)],
            axis=0,
        )
        part = lax.dot_general(
            spread, onehot, (((1,), (1,)), ((), ())), preferred_element_type=jnp.float32
        )
        total = part if total is None else total + part
    out_ref[...] += total


def contact_kernel(picked_ref, live_ref, slave_ref, master_ref, force_ref, react_ref, acc_ref):
    step = pl.program_id(0)
    group = slave_ref.shape[0]
    width = slave_ref.shape[2]

    @pl.when(step == 0)
    def _():
        acc_ref[...] = jnp.zeros_like(acc_ref)

    lane = lax.broadcasted_iota(jnp.int32, acc_ref.shape, 1)

    def body(k, carry):
        item = step * group + k

        @pl.when(live_ref[item] > 0)
        def _():
            s = slave_ref[k]
            m = master_ref[picked_ref[item]]
            delta_x = s[0:1] - m[:, 0:1]
            delta_y = s[1:2] - m[:, 1:2]
            delta_z = s[2:3] - m[:, 2:3]
            normal_x = m[:, 3:4]
            normal_y = m[:, 4:5]
            normal_z = m[:, 5:6]
            dist_sq = delta_x * delta_x + delta_y * delta_y + delta_z * delta_z
            gap_normal = normal_x * delta_x + normal_y * delta_y + normal_z * delta_z
            closing = (normal_x * s[3:4] + normal_y * s[4:5] + normal_z * s[5:6]) - m[:, 6:7]
            weight = jnp.exp(-dist_sq)
            soft = gap_normal * (-1.0 / SOFT_GAP)
            depth_soft = SOFT_GAP * (
                jnp.maximum(soft, 0.0) + jnp.log1p(jnp.exp(-jnp.abs(soft)))
            )
            push = (
                (s[6:7] * m[:, 7:8])
                * weight
                * depth_soft
                * (1.0 + DAMPING * jnp.tanh(-closing))
            )
            force_ref[k] = jnp.concatenate(
                [
                    jnp.sum(push * normal_x, axis=0, keepdims=True),
                    jnp.sum(push * normal_y, axis=0, keepdims=True),
                    jnp.sum(push * normal_z, axis=0, keepdims=True),
                ],
                axis=0,
            )
            reaction = jnp.sum(push, axis=1, keepdims=True)
            acc_ref[...] += jnp.where(lane == picked_ref[item], reaction, 0.0)

        @pl.when(live_ref[item] == 0)
        def _():
            force_ref[k] = jnp.zeros((3, width), jnp.float32)

        return carry

    lax.fori_loop(0, group, body, 0)

    @pl.when(step == pl.num_programs(0) - 1)
    def _():
        react_ref[...] = acc_ref[...].T


def contact_forces(arrived, picked, live, master_cols):
    item_total, _, width = arrived.shape
    group = math.gcd(item_total, 16)
    master_total = master_cols.shape[0]
    grid_spec = pltpu.PrefetchScalarGridSpec(
        num_scalar_prefetch=2,
        grid=(item_total // group,),
        in_specs=[
            pl.BlockSpec((group,) + arrived.shape[1:], lambda i, p, l: (i, 0, 0)),
            pl.BlockSpec(master_cols.shape, lambda i, p, l: (0, 0, 0)),
        ],
        out_specs=[
            pl.BlockSpec((group, 3, width), lambda i, p, l: (i, 0, 0)),
            pl.BlockSpec((width, width), lambda i, p, l: (0, 0)),
        ],
        scratch_shapes=[pltpu.VMEM((width, width), jnp.float32)],
    )
    forces, react = pl.pallas_call(
        contact_kernel,
        grid_spec=grid_spec,
        out_shape=[
            jax.ShapeDtypeStruct((item_total, 3, width), jnp.float32),
            jax.ShapeDtypeStruct((width, width), jnp.float32),
        ],
    )(picked, live, arrived, master_cols)
    return forces, react[:master_total]


def node_gather(field, nodes):
    channels, node_total = field.shape
    high_count = node_total // LANES
    table = field.reshape(channels, high_count, LANES).transpose(0, 2, 1).reshape(
        channels * LANES, high_count
    )
    count = nodes.shape[0]
    padded_count = -(-count // TILE) * TILE
    nodes = jnp.pad(nodes, (0, padded_count - count))
    return pl.pallas_call(
        gather_kernel,
        grid=(padded_count // TILE,),
        in_specs=[
            pl.BlockSpec((1, TILE), lambda i: (0, i)),
            pl.BlockSpec((channels * LANES, high_count), lambda i: (0, 0)),
        ],
        out_specs=pl.BlockSpec((channels, TILE), lambda i: (0, i)),
        out_shape=jax.ShapeDtypeStruct((channels, padded_count), jnp.float32),
    )(nodes.reshape(1, padded_count), table)[:, :count]


def node_scatter_add(forces, nodes, node_total):
    channels, count = forces.shape
    high_count = node_total // LANES
    padded_count = -(-count // TILE) * TILE
    nodes = jnp.pad(nodes, (0, padded_count - count))
    forces = jnp.pad(forces, ((0, 0), (0, padded_count - count)))
    summed = pl.pallas_call(
        scatter_kernel,
        grid=(padded_count // TILE,),
        in_specs=[
            pl.BlockSpec((1, TILE), lambda i: (0, i)),
            pl.BlockSpec((channels, TILE), lambda i: (0, i)),
        ],
        out_specs=pl.BlockSpec((channels * LANES, high_count), lambda i: (0, 0)),
        out_shape=jax.ShapeDtypeStruct((channels * LANES, high_count), jnp.float32),
    )(nodes.reshape(1, padded_count), forces)
    return summed.reshape(channels, LANES, high_count).transpose(0, 2, 1).reshape(channels, node_total)


TIME_STEP = 0.25
VISCOUS = 0.5
SOFT_GAP = 0.2
REACH_SQ = 1.0
DAMPING = 0.5


def padded_2(block, sides, width):
    for axis, dim in sides:
        count = lax.axis_size(axis)
        forward = [(i, i + 1) for i in range(count - 1)]
        backward = [(target, source) for source, target in forward]
        low = lax.ppermute(
            lax.slice_in_dim(block, block.shape[dim] - width, None, axis=dim), axis, forward
        )
        high = lax.ppermute(lax.slice_in_dim(block, 0, width, axis=dim), axis, backward)
        block = jnp.concatenate([low, block, high], axis=dim)
    return block


def pair_mean(values, along):
    length = values.shape[along]
    return 0.5 * (
        lax.slice_in_dim(values, 0, length - 1, axis=along)
        + lax.slice_in_dim(values, 1, length, axis=along)
    )


def pair_diff(values, along):
    length = values.shape[along]
    return lax.slice_in_dim(values, 1, length, axis=along) - lax.slice_in_dim(
        values, 0, length - 1, axis=along
    )


def pair_prod(values, along):
    length = values.shape[along]
    return lax.slice_in_dim(values, 0, length - 1, axis=along) * lax.slice_in_dim(
        values, 1, length, axis=along
    )


def corner_mean(values):
    return pair_mean(pair_mean(pair_mean(values, 0), 1), 2)


def zone_rate(vel):
    rate_x = pair_diff(pair_mean(pair_mean(vel[0], 0), 2), 1)
    rate_y = pair_diff(pair_mean(pair_mean(vel[1], 0), 1), 2)
    rate_z = pair_diff(pair_mean(pair_mean(vel[2], 1), 2), 0)
    return rate_x + rate_y + rate_z


def stress_forces(padded):
    inside = pair_prod(pair_prod(pair_prod(padded[5], 0), 1), 2)
    strain = TIME_STEP * zone_rate(padded[0:3])
    pressure = inside * (
        corner_mean(padded[4]) + corner_mean(padded[3]) * (VISCOUS * strain * strain - strain)
    )
    framed = jnp.pad(pressure, ((1, 1), (0, 0), (0, 0)))
    force_x = -pair_diff(pair_mean(pair_mean(framed, 0), 2), 1)
    force_y = -pair_diff(pair_mean(pair_mean(framed, 0), 1), 2)
    force_z = -pair_diff(pair_mean(pair_mean(framed, 1), 2), 0)
    return (jnp.stack([force_x, force_y, force_z], axis=0), inside)


def nodal_rate(padded_vel, inside):
    rate = inside * zone_rate(padded_vel)
    framed = jnp.pad(rate, ((1, 1), (0, 0), (0, 0)))
    return pair_mean(pair_mean(pair_mean(framed, 0), 1), 2)


def contact_pairs(slave, master):
    delta_x = slave[:, 0, :, None] - master[:, 0, None, :]
    delta_y = slave[:, 1, :, None] - master[:, 1, None, :]
    delta_z = slave[:, 2, :, None] - master[:, 2, None, :]
    normal_x = master[:, 3, None, :]
    normal_y = master[:, 4, None, :]
    normal_z = master[:, 5, None, :]
    dist_sq = delta_x * delta_x + delta_y * delta_y + delta_z * delta_z
    gap_normal = normal_x * delta_x + normal_y * delta_y + normal_z * delta_z
    closing = (
        normal_x * (slave[:, 3, :, None] - master[:, 6, None, :])
        + normal_y * (slave[:, 4, :, None] - master[:, 7, None, :])
        + normal_z * (slave[:, 5, :, None] - master[:, 8, None, :])
    )
    weight = jnp.exp(-dist_sq / REACH_SQ)
    depth_soft = SOFT_GAP * jax.nn.softplus(-gap_normal / SOFT_GAP)
    push_force = (
        slave[:, 6, :, None]
        * master[:, 9, None, :]
        * weight
        * depth_soft
        * (1.0 + DAMPING * jnp.tanh(-closing))
    )
    slave_force = jnp.stack(
        [
            jnp.sum(push_force * normal_x, axis=2),
            jnp.sum(push_force * normal_y, axis=2),
            jnp.sum(push_force * normal_z, axis=2),
        ],
        axis=1,
    )
    reaction = jnp.sum(push_force, axis=1)
    return (slave_force, reaction)


def master_normals(master_tilt):
    scale = lax.rsqrt(
        1.0 + master_tilt[:, 0] * master_tilt[:, 0] + master_tilt[:, 1] * master_tilt[:, 1]
    )
    return jnp.stack([master_tilt[:, 0] * scale, master_tilt[:, 1] * scale, scale], axis=1)


def on_device(
    velocity,
    bulk,
    prestress,
    node_mass,
    slave_pos,
    slave_area,
    seg_count,
    slave_node,
    pair_owner,
    pair_master,
    master_cent,
    master_tilt,
    master_stiff,
    master_node,
):
    count_gx = lax.axis_size("gx")
    count_gy = lax.axis_size("gy")
    devices = count_gx * count_gy
    layers, row_cells, col_cells = bulk.shape
    node_total = layers * row_cells * col_cells
    block_total, _, seg_width = slave_pos.shape
    master_total = master_cent.shape[0]
    slot_depth = (block_total + devices - 1) // devices + 1
    stacked = jnp.concatenate(
        [velocity, bulk[None], prestress[None], jnp.ones_like(bulk)[None]], axis=0
    )
    padded = padded_2(stacked, (("gx", 2), ("gy", 3)), 1)
    stress, inside = stress_forces(padded)
    vel_flat = velocity.reshape(3, node_total)
    slave_count = block_total * seg_width
    all_nodes = jnp.concatenate([slave_node.reshape(-1), master_node.reshape(-1)])
    picked_vel = node_gather(vel_flat, all_nodes)
    slave_vel = picked_vel[:, :slave_count].reshape(3, block_total, seg_width).transpose(1, 0, 2)
    master_vel = picked_vel[:, slave_count:].reshape(3, master_total, seg_width).transpose(1, 0, 2)
    live_mask = jnp.arange(seg_width, dtype=jnp.int32)[None, :] < seg_count[:, None]
    area_live = jnp.where(live_mask, slave_area, jnp.zeros_like(slave_area))
    slave = jnp.concatenate(
        [slave_pos + TIME_STEP * slave_vel, slave_vel, area_live[:, None, :]], axis=1
    )
    normals = master_normals(master_tilt)
    master_data = jnp.concatenate(
        [master_cent + TIME_STEP * master_vel, normals, master_vel, master_stiff[:, None, :]],
        axis=1,
    )
    owners = pair_owner[:, 0]
    positions = jnp.arange(block_total, dtype=jnp.int32)
    earlier = (owners[:, None] == owners[None, :]) & (positions[None, :] < positions[:, None])
    slot_index = jnp.sum(earlier.astype(jnp.int32), axis=1)
    target_slot = owners * slot_depth + slot_index
    slot_hit = target_slot[None, :] == jnp.arange(devices * slot_depth, dtype=jnp.int32)[:, None]
    source = jnp.sum(jnp.where(slot_hit, positions[None, :], 0), axis=1)
    filled = jnp.any(slot_hit, axis=1)
    tagged = jnp.concatenate(
        [
            slave,
            jnp.broadcast_to(
                jnp.where(
                    jnp.arange(seg_width)[None, :] == 0,
                    pair_master.astype(jnp.float32)[:, None],
                    1.0,
                )[:, None, :],
                (block_total, 1, seg_width),
            ),
        ],
        axis=1,
    )
    outgoing = jnp.where(filled[:, None, None], jnp.take(tagged, source, axis=0), 0.0)
    arrived = lax.all_to_all(
        outgoing.reshape(devices, slot_depth, 8, seg_width),
        ("gx", "gy"),
        split_axis=0,
        concat_axis=0,
        tiled=True,
    )
    item_total = devices * slot_depth
    arrived = arrived.reshape(item_total, 8, seg_width)
    picked = jnp.clip(arrived[:, 7, 0].astype(jnp.int32), 0, master_total - 1)
    live = (arrived[:, 7, 1] > 0.5).astype(jnp.int32)
    master_vel_normal = jnp.sum(normals * master_vel, axis=1, keepdims=True)
    master_rows = jnp.concatenate(
        [
            master_cent + TIME_STEP * master_vel,
            normals,
            master_vel_normal,
            master_stiff[:, None, :],
        ],
        axis=1,
    )
    master_cols = master_rows.transpose(0, 2, 1)
    forces, master_sum = contact_forces(arrived, picked, live, master_cols)
    master_force = -master_sum[:, None, :] * normals
    returned = lax.all_to_all(
        forces.reshape(devices, slot_depth, 3, seg_width),
        ("gx", "gy"),
        split_axis=0,
        concat_axis=0,
        tiled=True,
    )
    slave_force = jnp.take(returned.reshape(item_total, 3, seg_width), target_slot, axis=0)
    all_forces = jnp.concatenate(
        [slave_force.transpose(1, 0, 2).reshape(3, -1), master_force.transpose(1, 0, 2).reshape(3, -1)],
        axis=1,
    )
    contact = node_scatter_add(all_forces, all_nodes, node_total)
    contact_field = contact.reshape(3, layers, row_cells, col_cells)
    velocity_new = velocity + TIME_STEP * (stress + contact_field) / node_mass[None]
    padded_new = padded_2(velocity_new, (("gx", 2), ("gy", 3)), 1)
    node_rate = nodal_rate(padded_new, inside)
    return (velocity_new, node_rate)


def solution(mesh):
    placed = (
        P(None, None, "gx", "gy"),
        P(None, "gx", "gy"),
        P(None, "gx", "gy"),
        P(None, "gx", "gy"),
        P(("gx", "gy"), None, None),
        P(("gx", "gy"), None),
        P(("gx", "gy")),
        P(("gx", "gy"), None),
        P(("gx", "gy"), None),
        P(("gx", "gy")),
        P(("gx", "gy"), None, None),
        P(("gx", "gy"), None, None),
        P(("gx", "gy"), None),
        P(("gx", "gy"), None),
    )
    return jax.shard_map(
        on_device,
        mesh=mesh,
        in_specs=placed,
        out_specs=(P(None, None, "gx", "gy"), P(None, "gx", "gy")),
        check_vma=False,
    )
```

```python
import jax
import jax.numpy as jnp
from jax import lax
from jax.sharding import PartitionSpec as P
from jax.experimental import pallas as pl
from jax.experimental.pallas import tpu as pltpu

LANES = 128
TILE = 2048


def split_pieces(values):
    first = values.astype(jnp.bfloat16)
    rest = values - first.astype(jnp.float32)
    second = rest.astype(jnp.bfloat16)
    third = (rest - second.astype(jnp.float32)).astype(jnp.bfloat16)
    return (first, second, third)


def gather_kernel(index_ref, table_ref, out_ref):
    node = index_ref[...]
    width = node.shape[1]
    high_count = table_ref.shape[1]
    channels = out_ref.shape[0]
    onehot = (
        lax.broadcasted_iota(jnp.int32, (high_count, width), 0) == (node >> 7)
    ).astype(jnp.bfloat16)
    gathered = None
    for piece in split_pieces(table_ref[...]):
        part = jnp.dot(piece, onehot, preferred_element_type=jnp.float32)
        gathered = part if gathered is None else gathered + part
    low_hit = lax.broadcasted_iota(jnp.int32, (LANES, width), 0) == (node & (LANES - 1))
    for c in range(channels):
        block = gathered[c * LANES : (c + 1) * LANES]
        out_ref[c : c + 1, :] = jnp.sum(jnp.where(low_hit, block, 0.0), axis=0, keepdims=True)


def scatter_kernel(index_ref, force_ref, out_ref):
    @pl.when(pl.program_id(0) == 0)
    def _():
        out_ref[...] = jnp.zeros_like(out_ref)

    node = index_ref[...]
    width = node.shape[1]
    high_count = out_ref.shape[1]
    channels = force_ref.shape[0]
    onehot = (
        lax.broadcasted_iota(jnp.int32, (high_count, width), 0) == (node >> 7)
    ).astype(jnp.bfloat16)
    low_hit = lax.broadcasted_iota(jnp.int32, (LANES, width), 0) == (node & (LANES - 1))
    total = None
    for piece in split_pieces(force_ref[...])[:2]:
        spread = jnp.concatenate(
            [jnp.where(low_hit, piece[c : c + 1, :], jnp.zeros_like(piece[c : c + 1, :])) for c in range(channels)],
            axis=0,
        )
        part = lax.dot_general(
            spread, onehot, (((1,), (1,)), ((), ())), preferred_element_type=jnp.float32
        )
        total = part if total is None else total + part
    out_ref[...] += total


def node_gather(field, nodes):
    channels, node_total = field.shape
    high_count = node_total // LANES
    table = field.reshape(channels, high_count, LANES).transpose(0, 2, 1).reshape(
        channels * LANES, high_count
    )
    count = nodes.shape[0]
    padded_count = -(-count // TILE) * TILE
    nodes = jnp.pad(nodes, (0, padded_count - count))
    return pl.pallas_call(
        gather_kernel,
        grid=(padded_count // TILE,),
        in_specs=[
            pl.BlockSpec((1, TILE), lambda i: (0, i)),
            pl.BlockSpec((channels * LANES, high_count), lambda i: (0, 0)),
        ],
        out_specs=pl.BlockSpec((channels, TILE), lambda i: (0, i)),
        out_shape=jax.ShapeDtypeStruct((channels, padded_count), jnp.float32),
    )(nodes.reshape(1, padded_count), table)[:, :count]


def node_scatter_add(forces, nodes, node_total):
    channels, count = forces.shape
    high_count = node_total // LANES
    padded_count = -(-count // TILE) * TILE
    nodes = jnp.pad(nodes, (0, padded_count - count))
    forces = jnp.pad(forces, ((0, 0), (0, padded_count - count)))
    summed = pl.pallas_call(
        scatter_kernel,
        grid=(padded_count // TILE,),
        in_specs=[
            pl.BlockSpec((1, TILE), lambda i: (0, i)),
            pl.BlockSpec((channels, TILE), lambda i: (0, i)),
        ],
        out_specs=pl.BlockSpec((channels * LANES, high_count), lambda i: (0, 0)),
        out_shape=jax.ShapeDtypeStruct((channels * LANES, high_count), jnp.float32),
    )(nodes.reshape(1, padded_count), forces)
    return summed.reshape(channels, LANES, high_count).transpose(0, 2, 1).reshape(channels, node_total)


TIME_STEP = 0.25
VISCOUS = 0.5
SOFT_GAP = 0.2
REACH_SQ = 1.0
DAMPING = 0.5


def padded_2(block, sides, width):
    for axis, dim in sides:
        count = lax.axis_size(axis)
        forward = [(i, i + 1) for i in range(count - 1)]
        backward = [(target, source) for source, target in forward]
        low = lax.ppermute(
            lax.index_in_dim(block, block.shape[dim] - 1, axis=dim, keepdims=False), axis, forward
        )
        high = lax.ppermute(lax.index_in_dim(block, 0, axis=dim, keepdims=False), axis, backward)
        block = jnp.concatenate(
            [jnp.expand_dims(low, dim), block, jnp.expand_dims(high, dim)], axis=dim
        )
    return block


def pair_mean(values, along):
    length = values.shape[along]
    return 0.5 * (
        lax.slice_in_dim(values, 0, length - 1, axis=along)
        + lax.slice_in_dim(values, 1, length, axis=along)
    )


def pair_diff(values, along):
    length = values.shape[along]
    return lax.slice_in_dim(values, 1, length, axis=along) - lax.slice_in_dim(
        values, 0, length - 1, axis=along
    )


def pair_prod(values, along):
    length = values.shape[along]
    return lax.slice_in_dim(values, 0, length - 1, axis=along) * lax.slice_in_dim(
        values, 1, length, axis=along
    )


def corner_mean(values):
    return pair_mean(pair_mean(pair_mean(values, 0), 1), 2)


def zone_rate(vel):
    rate_x = pair_diff(pair_mean(pair_mean(vel[0], 0), 2), 1)
    rate_y = pair_diff(pair_mean(pair_mean(vel[1], 0), 1), 2)
    rate_z = pair_diff(pair_mean(pair_mean(vel[2], 1), 2), 0)
    return rate_x + rate_y + rate_z


def stress_forces(padded):
    inside = pair_prod(pair_prod(pair_prod(padded[5], 0), 1), 2)
    strain = TIME_STEP * zone_rate(padded[0:3])
    pressure = inside * (
        corner_mean(padded[4]) + corner_mean(padded[3]) * (VISCOUS * strain * strain - strain)
    )
    framed = jnp.pad(pressure, ((1, 1), (0, 0), (0, 0)))
    force_x = -pair_diff(pair_mean(pair_mean(framed, 0), 2), 1)
    force_y = -pair_diff(pair_mean(pair_mean(framed, 0), 1), 2)
    force_z = -pair_diff(pair_mean(pair_mean(framed, 1), 2), 0)
    return (jnp.stack([force_x, force_y, force_z], axis=0), inside)


def nodal_rate(padded_vel, inside):
    rate = inside * zone_rate(padded_vel)
    framed = jnp.pad(rate, ((1, 1), (0, 0), (0, 0)))
    return pair_mean(pair_mean(pair_mean(framed, 0), 1), 2)


def contact_pairs(slave, master):
    delta_x = slave[:, 0, :, None] - master[:, 0, None, :]
    delta_y = slave[:, 1, :, None] - master[:, 1, None, :]
    delta_z = slave[:, 2, :, None] - master[:, 2, None, :]
    normal_x = master[:, 3, None, :]
    normal_y = master[:, 4, None, :]
    normal_z = master[:, 5, None, :]
    dist_sq = delta_x * delta_x + delta_y * delta_y + delta_z * delta_z
    gap_normal = normal_x * delta_x + normal_y * delta_y + normal_z * delta_z
    closing = (
        normal_x * (slave[:, 3, :, None] - master[:, 6, None, :])
        + normal_y * (slave[:, 4, :, None] - master[:, 7, None, :])
        + normal_z * (slave[:, 5, :, None] - master[:, 8, None, :])
    )
    weight = jnp.exp(-dist_sq / REACH_SQ)
    depth_soft = SOFT_GAP * jax.nn.softplus(-gap_normal / SOFT_GAP)
    push_force = (
        slave[:, 6, :, None]
        * master[:, 9, None, :]
        * weight
        * depth_soft
        * (1.0 + DAMPING * jnp.tanh(-closing))
    )
    slave_force = jnp.stack(
        [
            jnp.sum(push_force * normal_x, axis=2),
            jnp.sum(push_force * normal_y, axis=2),
            jnp.sum(push_force * normal_z, axis=2),
        ],
        axis=1,
    )
    reaction = jnp.sum(push_force, axis=1)
    return (slave_force, reaction)


def master_normals(master_tilt):
    scale = lax.rsqrt(
        1.0 + master_tilt[:, 0] * master_tilt[:, 0] + master_tilt[:, 1] * master_tilt[:, 1]
    )
    return jnp.stack([master_tilt[:, 0] * scale, master_tilt[:, 1] * scale, scale], axis=1)


def on_device(
    velocity,
    bulk,
    prestress,
    node_mass,
    slave_pos,
    slave_area,
    seg_count,
    slave_node,
    pair_owner,
    pair_master,
    master_cent,
    master_tilt,
    master_stiff,
    master_node,
):
    count_gx = lax.axis_size("gx")
    count_gy = lax.axis_size("gy")
    devices = count_gx * count_gy
    layers, row_cells, col_cells = bulk.shape
    node_total = layers * row_cells * col_cells
    block_total, _, seg_width = slave_pos.shape
    master_total = master_cent.shape[0]
    slot_depth = (block_total + devices - 1) // devices + 1
    stacked = jnp.concatenate(
        [velocity, bulk[None], prestress[None], jnp.ones_like(bulk)[None]], axis=0
    )
    padded = padded_2(stacked, (("gx", 2), ("gy", 3)), 1)
    stress, inside = stress_forces(padded)
    vel_flat = velocity.reshape(3, node_total)
    slave_count = block_total * seg_width
    all_nodes = jnp.concatenate([slave_node.reshape(-1), master_node.reshape(-1)])
    slave_vel = (
        node_gather(vel_flat, slave_node.reshape(-1))
        .reshape(3, block_total, seg_width)
        .transpose(1, 0, 2)
    )
    master_vel = (
        node_gather(vel_flat, master_node.reshape(-1))
        .reshape(3, master_total, seg_width)
        .transpose(1, 0, 2)
    )
    live_mask = jnp.arange(seg_width, dtype=jnp.int32)[None, :] < seg_count[:, None]
    area_live = jnp.where(live_mask, slave_area, jnp.zeros_like(slave_area))
    slave = jnp.concatenate(
        [slave_pos + TIME_STEP * slave_vel, slave_vel, area_live[:, None, :]], axis=1
    )
    normals = master_normals(master_tilt)
    master_data = jnp.concatenate(
        [master_cent + TIME_STEP * master_vel, normals, master_vel, master_stiff[:, None, :]],
        axis=1,
    )
    owners = pair_owner[:, 0]
    positions = jnp.arange(block_total, dtype=jnp.int32)
    earlier = (owners[:, None] == owners[None, :]) & (positions[None, :] < positions[:, None])
    slot_index = jnp.sum(earlier.astype(jnp.int32), axis=1)
    target_slot = owners * slot_depth + slot_index
    slot_hit = target_slot[None, :] == jnp.arange(devices * slot_depth, dtype=jnp.int32)[:, None]
    source = jnp.sum(jnp.where(slot_hit, positions[None, :], 0), axis=1)
    filled = jnp.any(slot_hit, axis=1)
    tagged = jnp.concatenate(
        [
            slave,
            jnp.broadcast_to(pair_master.astype(jnp.float32)[:, None, None], (block_total, 1, seg_width)),
        ],
        axis=1,
    )
    outgoing = jnp.where(filled[:, None, None], jnp.take(tagged, source, axis=0), 0.0)
    arrived = lax.all_to_all(
        outgoing.reshape(devices, slot_depth, 8, seg_width),
        ("gx", "gy"),
        split_axis=0,
        concat_axis=0,
        tiled=True,
    )
    item_total = devices * slot_depth
    arrived = arrived.reshape(item_total, 8, seg_width)
    picked = arrived[:, 7, 0].astype(jnp.int32)
    arrived = arrived[:, :7]
    paired = jnp.take(master_data, picked, axis=0)
    group_size = 16 * slot_depth

    def per_group(pairing):
        return contact_pairs(pairing[0], pairing[1])

    forces, reaction = lax.map(
        per_group,
        (
            arrived.reshape(item_total // group_size, group_size, 7, seg_width),
            paired.reshape(item_total // group_size, group_size, 10, seg_width),
        ),
    )
    forces = forces.reshape(item_total, 3, seg_width)
    reaction = reaction.reshape(item_total, seg_width)
    onehot = (picked[:, None] == jnp.arange(master_total, dtype=jnp.int32)[None, :]).astype(
        jnp.float32
    )
    master_sum = jnp.dot(onehot.T, reaction, precision=lax.Precision.HIGHEST)
    master_force = -master_sum[:, None, :] * normals
    returned = lax.all_to_all(
        forces.reshape(devices, slot_depth, 3, seg_width),
        ("gx", "gy"),
        split_axis=0,
        concat_axis=0,
        tiled=True,
    )
    slave_force = jnp.take(returned.reshape(item_total, 3, seg_width), target_slot, axis=0)
    all_forces = jnp.concatenate(
        [slave_force.transpose(1, 0, 2).reshape(3, -1), master_force.transpose(1, 0, 2).reshape(3, -1)],
        axis=1,
    )
    contact = node_scatter_add(all_forces, all_nodes, node_total)
    contact_field = contact.reshape(3, layers, row_cells, col_cells)
    velocity_new = velocity + TIME_STEP * (stress + contact_field) / node_mass[None]
    padded_new = padded_2(velocity_new, (("gx", 2), ("gy", 3)), 1)
    node_rate = nodal_rate(padded_new, inside)
    return (velocity_new, node_rate)


def solution(mesh):
    placed = (
        P(None, None, "gx", "gy"),
        P(None, "gx", "gy"),
        P(None, "gx", "gy"),
        P(None, "gx", "gy"),
        P(("gx", "gy"), None, None),
        P(("gx", "gy"), None),
        P(("gx", "gy")),
        P(("gx", "gy"), None),
        P(("gx", "gy"), None),
        P(("gx", "gy")),
        P(("gx", "gy"), None, None),
        P(("gx", "gy"), None, None),
        P(("gx", "gy"), None),
        P(("gx", "gy"), None),
    )
    return jax.shard_map(
        on_device,
        mesh=mesh,
        in_specs=placed,
        out_specs=(P(None, None, "gx", "gy"), P(None, "gx", "gy")),
        check_vma=False,
    )
```

```python
import jax
import jax.numpy as jnp
from jax import lax
from jax.sharding import PartitionSpec as P
from jax.experimental import pallas as pl
from jax.experimental.pallas import tpu as pltpu

LANES = 128
TILE = 2048


def split_pieces(values):
    first = values.astype(jnp.bfloat16)
    rest = values - first.astype(jnp.float32)
    second = rest.astype(jnp.bfloat16)
    third = (rest - second.astype(jnp.float32)).astype(jnp.bfloat16)
    return (first, second, third)


def gather_kernel(index_ref, table_ref, out_ref):
    node = index_ref[...]
    width = node.shape[1]
    high_count = table_ref.shape[1]
    channels = out_ref.shape[0]
    onehot = (
        lax.broadcasted_iota(jnp.int32, (high_count, width), 0) == (node >> 7)
    ).astype(jnp.bfloat16)
    gathered = None
    for piece in split_pieces(table_ref[...]):
        part = jnp.dot(piece, onehot, preferred_element_type=jnp.float32)
        gathered = part if gathered is None else gathered + part
    low_hit = lax.broadcasted_iota(jnp.int32, (LANES, width), 0) == (node & (LANES - 1))
    for c in range(channels):
        block = gathered[c * LANES : (c + 1) * LANES]
        out_ref[c : c + 1, :] = jnp.sum(jnp.where(low_hit, block, 0.0), axis=0, keepdims=True)


def scatter_kernel(index_ref, force_ref, out_ref):
    @pl.when(pl.program_id(0) == 0)
    def _():
        out_ref[...] = jnp.zeros_like(out_ref)

    node = index_ref[...]
    width = node.shape[1]
    high_count = out_ref.shape[1]
    channels = force_ref.shape[0]
    onehot = (
        lax.broadcasted_iota(jnp.int32, (high_count, width), 0) == (node >> 7)
    ).astype(jnp.bfloat16)
    low_hit = lax.broadcasted_iota(jnp.int32, (LANES, width), 0) == (node & (LANES - 1))
    total = None
    for piece in split_pieces(force_ref[...])[:2]:
        spread = jnp.concatenate(
            [jnp.where(low_hit, piece[c : c + 1, :], jnp.zeros_like(piece[c : c + 1, :])) for c in range(channels)],
            axis=0,
        )
        part = lax.dot_general(
            spread, onehot, (((1,), (1,)), ((), ())), preferred_element_type=jnp.float32
        )
        total = part if total is None else total + part
    out_ref[...] += total


def node_gather(field, nodes):
    channels, node_total = field.shape
    high_count = node_total // LANES
    table = field.reshape(channels, high_count, LANES).transpose(0, 2, 1).reshape(
        channels * LANES, high_count
    )
    count = nodes.shape[0]
    padded_count = -(-count // TILE) * TILE
    nodes = jnp.pad(nodes, (0, padded_count - count))
    return pl.pallas_call(
        gather_kernel,
        grid=(padded_count // TILE,),
        in_specs=[
            pl.BlockSpec((1, TILE), lambda i: (0, i)),
            pl.BlockSpec((channels * LANES, high_count), lambda i: (0, 0)),
        ],
        out_specs=pl.BlockSpec((channels, TILE), lambda i: (0, i)),
        out_shape=jax.ShapeDtypeStruct((channels, padded_count), jnp.float32),
    )(nodes.reshape(1, padded_count), table)[:, :count]


def node_scatter_add(forces, nodes, node_total):
    channels, count = forces.shape
    high_count = node_total // LANES
    padded_count = -(-count // TILE) * TILE
    nodes = jnp.pad(nodes, (0, padded_count - count))
    forces = jnp.pad(forces, ((0, 0), (0, padded_count - count)))
    summed = pl.pallas_call(
        scatter_kernel,
        grid=(padded_count // TILE,),
        in_specs=[
            pl.BlockSpec((1, TILE), lambda i: (0, i)),
            pl.BlockSpec((channels, TILE), lambda i: (0, i)),
        ],
        out_specs=pl.BlockSpec((channels * LANES, high_count), lambda i: (0, 0)),
        out_shape=jax.ShapeDtypeStruct((channels * LANES, high_count), jnp.float32),
    )(nodes.reshape(1, padded_count), forces)
    return summed.reshape(channels, LANES, high_count).transpose(0, 2, 1).reshape(channels, node_total)


TIME_STEP = 0.25
VISCOUS = 0.5
SOFT_GAP = 0.2
REACH_SQ = 1.0
DAMPING = 0.5


def padded_2(block, sides, width):
    for axis, dim in sides:
        count = lax.axis_size(axis)
        forward = [(i, i + 1) for i in range(count - 1)]
        backward = [(target, source) for source, target in forward]
        low = lax.ppermute(
            lax.index_in_dim(block, block.shape[dim] - 1, axis=dim, keepdims=False), axis, forward
        )
        high = lax.ppermute(lax.index_in_dim(block, 0, axis=dim, keepdims=False), axis, backward)
        block = jnp.concatenate(
            [jnp.expand_dims(low, dim), block, jnp.expand_dims(high, dim)], axis=dim
        )
    return block


def pair_mean(values, along):
    length = values.shape[along]
    return 0.5 * (
        lax.slice_in_dim(values, 0, length - 1, axis=along)
        + lax.slice_in_dim(values, 1, length, axis=along)
    )


def pair_diff(values, along):
    length = values.shape[along]
    return lax.slice_in_dim(values, 1, length, axis=along) - lax.slice_in_dim(
        values, 0, length - 1, axis=along
    )


def pair_prod(values, along):
    length = values.shape[along]
    return lax.slice_in_dim(values, 0, length - 1, axis=along) * lax.slice_in_dim(
        values, 1, length, axis=along
    )


def corner_mean(values):
    return pair_mean(pair_mean(pair_mean(values, 0), 1), 2)


def zone_rate(vel):
    rate_x = pair_diff(pair_mean(pair_mean(vel[0], 0), 2), 1)
    rate_y = pair_diff(pair_mean(pair_mean(vel[1], 0), 1), 2)
    rate_z = pair_diff(pair_mean(pair_mean(vel[2], 1), 2), 0)
    return rate_x + rate_y + rate_z


def stress_forces(padded):
    inside = pair_prod(pair_prod(pair_prod(padded[5], 0), 1), 2)
    strain = TIME_STEP * zone_rate(padded[0:3])
    pressure = inside * (
        corner_mean(padded[4]) + corner_mean(padded[3]) * (VISCOUS * strain * strain - strain)
    )
    framed = jnp.pad(pressure, ((1, 1), (0, 0), (0, 0)))
    force_x = -pair_diff(pair_mean(pair_mean(framed, 0), 2), 1)
    force_y = -pair_diff(pair_mean(pair_mean(framed, 0), 1), 2)
    force_z = -pair_diff(pair_mean(pair_mean(framed, 1), 2), 0)
    return (jnp.stack([force_x, force_y, force_z], axis=0), inside)


def nodal_rate(padded_vel, inside):
    rate = inside * zone_rate(padded_vel)
    framed = jnp.pad(rate, ((1, 1), (0, 0), (0, 0)))
    return pair_mean(pair_mean(pair_mean(framed, 0), 1), 2)


def contact_pairs(slave, master):
    delta_x = slave[:, 0, :, None] - master[:, 0, None, :]
    delta_y = slave[:, 1, :, None] - master[:, 1, None, :]
    delta_z = slave[:, 2, :, None] - master[:, 2, None, :]
    normal_x = master[:, 3, None, :]
    normal_y = master[:, 4, None, :]
    normal_z = master[:, 5, None, :]
    dist_sq = delta_x * delta_x + delta_y * delta_y + delta_z * delta_z
    gap_normal = normal_x * delta_x + normal_y * delta_y + normal_z * delta_z
    closing = (
        normal_x * slave[:, 3, :, None]
        + normal_y * slave[:, 4, :, None]
        + normal_z * slave[:, 5, :, None]
    ) - master[:, 6, None, :]
    weight = jnp.exp(-dist_sq / REACH_SQ)
    depth_soft = SOFT_GAP * jax.nn.softplus(-gap_normal / SOFT_GAP)
    push_force = (
        slave[:, 6, :, None]
        * master[:, 7, None, :]
        * weight
        * depth_soft
        * (1.0 + DAMPING * jnp.tanh(-closing))
    )
    slave_force = jnp.stack(
        [
            jnp.sum(push_force * normal_x, axis=2),
            jnp.sum(push_force * normal_y, axis=2),
            jnp.sum(push_force * normal_z, axis=2),
        ],
        axis=1,
    )
    reaction = jnp.sum(push_force, axis=1)
    return (slave_force, reaction)


def master_normals(master_tilt):
    scale = lax.rsqrt(
        1.0 + master_tilt[:, 0] * master_tilt[:, 0] + master_tilt[:, 1] * master_tilt[:, 1]
    )
    return jnp.stack([master_tilt[:, 0] * scale, master_tilt[:, 1] * scale, scale], axis=1)


def on_device(
    velocity,
    bulk,
    prestress,
    node_mass,
    slave_pos,
    slave_area,
    seg_count,
    slave_node,
    pair_owner,
    pair_master,
    master_cent,
    master_tilt,
    master_stiff,
    master_node,
):
    count_gx = lax.axis_size("gx")
    count_gy = lax.axis_size("gy")
    devices = count_gx * count_gy
    layers, row_cells, col_cells = bulk.shape
    node_total = layers * row_cells * col_cells
    block_total, _, seg_width = slave_pos.shape
    master_total = master_cent.shape[0]
    slot_depth = (block_total + devices - 1) // devices + 1
    stacked = jnp.concatenate(
        [velocity, bulk[None], prestress[None], jnp.ones_like(bulk)[None]], axis=0
    )
    padded = padded_2(stacked, (("gx", 2), ("gy", 3)), 1)
    stress, inside = stress_forces(padded)
    vel_flat = velocity.reshape(3, node_total)
    slave_count = block_total * seg_width
    slave_vel = (
        node_gather(vel_flat, slave_node.reshape(-1))
        .reshape(3, block_total, seg_width)
        .transpose(1, 0, 2)
    )
    master_vel = (
        node_gather(vel_flat, master_node.reshape(-1))
        .reshape(3, master_total, seg_width)
        .transpose(1, 0, 2)
    )
    live_mask = jnp.arange(seg_width, dtype=jnp.int32)[None, :] < seg_count[:, None]
    area_live = jnp.where(live_mask, slave_area, jnp.zeros_like(slave_area))
    slave = jnp.concatenate(
        [slave_pos + TIME_STEP * slave_vel, slave_vel, area_live[:, None, :]], axis=1
    )
    normals = master_normals(master_tilt)
    master_rows = jnp.concatenate(
        [
            master_cent + TIME_STEP * master_vel,
            normals,
            jnp.sum(normals * master_vel, axis=1, keepdims=True),
            master_stiff[:, None, :],
        ],
        axis=1,
    )
    all_master = lax.all_gather(master_rows, ("gx", "gy"), axis=0, tiled=True)
    target = pair_owner[:, 0] * master_total + pair_master
    paired = jnp.take(all_master, target, axis=0)
    group_size = block_total // 2 if block_total % 2 == 0 else block_total

    def per_group(pairing):
        return contact_pairs(pairing[0], pairing[1])

    forces, reaction = lax.map(
        per_group,
        (
            slave.reshape(block_total // group_size, group_size, 7, seg_width),
            paired.reshape(block_total // group_size, group_size, 8, seg_width),
        ),
    )
    slave_force = forces.reshape(block_total, 3, seg_width)
    reaction = reaction.reshape(block_total, seg_width)
    onehot = (
        target[None, :] == jnp.arange(devices * master_total, dtype=jnp.int32)[:, None]
    ).astype(jnp.float32)
    partial = jnp.dot(onehot, reaction, precision=lax.Precision.HIGHEST)
    master_sum = lax.psum_scatter(partial, ("gx", "gy"), scatter_dimension=0, tiled=True)
    master_force = -master_sum[:, None, :] * normals
    contact = node_scatter_add(
        slave_force.transpose(1, 0, 2).reshape(3, -1), slave_node.reshape(-1), node_total
    ) + node_scatter_add(
        master_force.transpose(1, 0, 2).reshape(3, -1), master_node.reshape(-1), node_total
    )
    contact_field = contact.reshape(3, layers, row_cells, col_cells)
    velocity_new = velocity + TIME_STEP * (stress + contact_field) / node_mass[None]
    padded_new = padded_2(velocity_new, (("gx", 2), ("gy", 3)), 1)
    node_rate = nodal_rate(padded_new, inside)
    return (velocity_new, node_rate)


def solution(mesh):
    placed = (
        P(None, None, "gx", "gy"),
        P(None, "gx", "gy"),
        P(None, "gx", "gy"),
        P(None, "gx", "gy"),
        P(("gx", "gy"), None, None),
        P(("gx", "gy"), None),
        P(("gx", "gy")),
        P(("gx", "gy"), None),
        P(("gx", "gy"), None),
        P(("gx", "gy")),
        P(("gx", "gy"), None, None),
        P(("gx", "gy"), None, None),
        P(("gx", "gy"), None),
        P(("gx", "gy"), None),
    )
    return jax.shard_map(
        on_device,
        mesh=mesh,
        in_specs=placed,
        out_specs=(P(None, None, "gx", "gy"), P(None, "gx", "gy")),
        check_vma=False,
    )
```

```python
import jax
import jax.numpy as jnp
from jax import lax
from jax.sharding import PartitionSpec as P
from jax.experimental import pallas as pl
from jax.experimental.pallas import tpu as pltpu

LANES = 128
TILE = 2048


def split_pieces(values):
    first = values.astype(jnp.bfloat16)
    rest = values - first.astype(jnp.float32)
    second = rest.astype(jnp.bfloat16)
    third = (rest - second.astype(jnp.float32)).astype(jnp.bfloat16)
    return (first, second, third)


def gather_kernel(index_ref, table_ref, out_ref):
    node = index_ref[...]
    width = node.shape[1]
    high_count = table_ref.shape[1]
    channels = out_ref.shape[0]
    onehot = (
        lax.broadcasted_iota(jnp.int32, (high_count, width), 0) == (node >> 7)
    ).astype(jnp.bfloat16)
    gathered = None
    for piece in split_pieces(table_ref[...]):
        part = jnp.dot(piece, onehot, preferred_element_type=jnp.float32)
        gathered = part if gathered is None else gathered + part
    low_hit = lax.broadcasted_iota(jnp.int32, (LANES, width), 0) == (node & (LANES - 1))
    for c in range(channels):
        block = gathered[c * LANES : (c + 1) * LANES]
        out_ref[c : c + 1, :] = jnp.sum(jnp.where(low_hit, block, 0.0), axis=0, keepdims=True)


def scatter_kernel(index_ref, force_ref, out_ref):
    @pl.when(pl.program_id(0) == 0)
    def _():
        out_ref[...] = jnp.zeros_like(out_ref)

    node = index_ref[...]
    width = node.shape[1]
    high_count = out_ref.shape[1]
    channels = force_ref.shape[0]
    onehot = (
        lax.broadcasted_iota(jnp.int32, (high_count, width), 0) == (node >> 7)
    ).astype(jnp.bfloat16)
    low_hit = lax.broadcasted_iota(jnp.int32, (LANES, width), 0) == (node & (LANES - 1))
    total = None
    for piece in split_pieces(force_ref[...])[:2]:
        spread = jnp.concatenate(
            [jnp.where(low_hit, piece[c : c + 1, :], jnp.zeros_like(piece[c : c + 1, :])) for c in range(channels)],
            axis=0,
        )
        part = lax.dot_general(
            spread, onehot, (((1,), (1,)), ((), ())), preferred_element_type=jnp.float32
        )
        total = part if total is None else total + part
    out_ref[...] += total


def node_gather(field, nodes):
    channels, node_total = field.shape
    high_count = node_total // LANES
    table = field.reshape(channels, high_count, LANES).transpose(0, 2, 1).reshape(
        channels * LANES, high_count
    )
    count = nodes.shape[0]
    padded_count = -(-count // TILE) * TILE
    nodes = jnp.pad(nodes, (0, padded_count - count))
    return pl.pallas_call(
        gather_kernel,
        grid=(padded_count // TILE,),
        in_specs=[
            pl.BlockSpec((1, TILE), lambda i: (0, i)),
            pl.BlockSpec((channels * LANES, high_count), lambda i: (0, 0)),
        ],
        out_specs=pl.BlockSpec((channels, TILE), lambda i: (0, i)),
        out_shape=jax.ShapeDtypeStruct((channels, padded_count), jnp.float32),
    )(nodes.reshape(1, padded_count), table)[:, :count]


def node_scatter_add(forces, nodes, node_total):
    channels, count = forces.shape
    high_count = node_total // LANES
    padded_count = -(-count // TILE) * TILE
    nodes = jnp.pad(nodes, (0, padded_count - count))
    forces = jnp.pad(forces, ((0, 0), (0, padded_count - count)))
    summed = pl.pallas_call(
        scatter_kernel,
        grid=(padded_count // TILE,),
        in_specs=[
            pl.BlockSpec((1, TILE), lambda i: (0, i)),
            pl.BlockSpec((channels, TILE), lambda i: (0, i)),
        ],
        out_specs=pl.BlockSpec((channels * LANES, high_count), lambda i: (0, 0)),
        out_shape=jax.ShapeDtypeStruct((channels * LANES, high_count), jnp.float32),
    )(nodes.reshape(1, padded_count), forces)
    return summed.reshape(channels, LANES, high_count).transpose(0, 2, 1).reshape(channels, node_total)


TIME_STEP = 0.25
VISCOUS = 0.5
SOFT_GAP = 0.2
REACH_SQ = 1.0
DAMPING = 0.5


def padded_2(block, sides, width):
    for axis, dim in sides:
        count = lax.axis_size(axis)
        forward = [(i, i + 1) for i in range(count - 1)]
        backward = [(target, source) for source, target in forward]
        low = lax.ppermute(
            lax.index_in_dim(block, block.shape[dim] - 1, axis=dim, keepdims=False), axis, forward
        )
        high = lax.ppermute(lax.index_in_dim(block, 0, axis=dim, keepdims=False), axis, backward)
        block = jnp.concatenate(
            [jnp.expand_dims(low, dim), block, jnp.expand_dims(high, dim)], axis=dim
        )
    return block


def pair_mean(values, along):
    length = values.shape[along]
    return 0.5 * (
        lax.slice_in_dim(values, 0, length - 1, axis=along)
        + lax.slice_in_dim(values, 1, length, axis=along)
    )


def pair_diff(values, along):
    length = values.shape[along]
    return lax.slice_in_dim(values, 1, length, axis=along) - lax.slice_in_dim(
        values, 0, length - 1, axis=along
    )


def pair_prod(values, along):
    length = values.shape[along]
    return lax.slice_in_dim(values, 0, length - 1, axis=along) * lax.slice_in_dim(
        values, 1, length, axis=along
    )


def corner_mean(values):
    return pair_mean(pair_mean(pair_mean(values, 0), 1), 2)


def zone_rate(vel):
    rate_x = pair_diff(pair_mean(pair_mean(vel[0], 0), 2), 1)
    rate_y = pair_diff(pair_mean(pair_mean(vel[1], 0), 1), 2)
    rate_z = pair_diff(pair_mean(pair_mean(vel[2], 1), 2), 0)
    return rate_x + rate_y + rate_z


def stress_forces(padded):
    inside = pair_prod(pair_prod(pair_prod(padded[5], 0), 1), 2)
    strain = TIME_STEP * zone_rate(padded[0:3])
    pressure = inside * (
        corner_mean(padded[4]) + corner_mean(padded[3]) * (VISCOUS * strain * strain - strain)
    )
    framed = jnp.pad(pressure, ((1, 1), (0, 0), (0, 0)))
    force_x = -pair_diff(pair_mean(pair_mean(framed, 0), 2), 1)
    force_y = -pair_diff(pair_mean(pair_mean(framed, 0), 1), 2)
    force_z = -pair_diff(pair_mean(pair_mean(framed, 1), 2), 0)
    return (jnp.stack([force_x, force_y, force_z], axis=0), inside)


def nodal_rate(padded_vel, inside):
    rate = inside * zone_rate(padded_vel)
    framed = jnp.pad(rate, ((1, 1), (0, 0), (0, 0)))
    return pair_mean(pair_mean(pair_mean(framed, 0), 1), 2)


def contact_pairs(slave, master):
    delta_x = slave[:, 0, :, None] - master[:, 0, None, :]
    delta_y = slave[:, 1, :, None] - master[:, 1, None, :]
    delta_z = slave[:, 2, :, None] - master[:, 2, None, :]
    normal_x = master[:, 3, None, :]
    normal_y = master[:, 4, None, :]
    normal_z = master[:, 5, None, :]
    dist_sq = delta_x * delta_x + delta_y * delta_y + delta_z * delta_z
    gap_normal = normal_x * delta_x + normal_y * delta_y + normal_z * delta_z
    master_along = (
        master[:, 3] * master[:, 6] + master[:, 4] * master[:, 7] + master[:, 5] * master[:, 8]
    )
    closing = (
        normal_x * slave[:, 3, :, None]
        + normal_y * slave[:, 4, :, None]
        + normal_z * slave[:, 5, :, None]
    ) - master_along[:, None, :]
    weight = jnp.exp(-dist_sq / REACH_SQ)
    soft = gap_normal * (-1.0 / SOFT_GAP)
    depth_soft = SOFT_GAP * (jnp.maximum(soft, 0.0) + jnp.log1p(jnp.exp(-jnp.abs(soft))))
    push_force = (
        slave[:, 6, :, None]
        * master[:, 9, None, :]
        * weight
        * depth_soft
        * (1.0 + DAMPING * jnp.tanh(-closing))
    )
    slave_force = jnp.stack(
        [
            jnp.sum(push_force * normal_x, axis=2),
            jnp.sum(push_force * normal_y, axis=2),
            jnp.sum(push_force * normal_z, axis=2),
        ],
        axis=1,
    )
    reaction = jnp.sum(push_force, axis=1)
    return (slave_force, reaction)


def master_normals(master_tilt):
    scale = lax.rsqrt(
        1.0 + master_tilt[:, 0] * master_tilt[:, 0] + master_tilt[:, 1] * master_tilt[:, 1]
    )
    return jnp.stack([master_tilt[:, 0] * scale, master_tilt[:, 1] * scale, scale], axis=1)


def on_device(
    velocity,
    bulk,
    prestress,
    node_mass,
    slave_pos,
    slave_area,
    seg_count,
    slave_node,
    pair_owner,
    pair_master,
    master_cent,
    master_tilt,
    master_stiff,
    master_node,
):
    count_gx = lax.axis_size("gx")
    count_gy = lax.axis_size("gy")
    devices = count_gx * count_gy
    layers, row_cells, col_cells = bulk.shape
    node_total = layers * row_cells * col_cells
    block_total, _, seg_width = slave_pos.shape
    master_total = master_cent.shape[0]
    slot_depth = (block_total + devices - 1) // devices + 1
    stacked = jnp.concatenate(
        [velocity, bulk[None], prestress[None], jnp.ones_like(bulk)[None]], axis=0
    )
    padded = padded_2(stacked, (("gx", 2), ("gy", 3)), 1)
    stress, inside = stress_forces(padded)
    vel_flat = velocity.reshape(3, node_total)
    slave_count = block_total * seg_width
    slave_vel = (
        node_gather(vel_flat, slave_node.reshape(-1))
        .reshape(3, block_total, seg_width)
        .transpose(1, 0, 2)
    )
    master_vel = (
        node_gather(vel_flat, master_node.reshape(-1))
        .reshape(3, master_total, seg_width)
        .transpose(1, 0, 2)
    )
    live_mask = jnp.arange(seg_width, dtype=jnp.int32)[None, :] < seg_count[:, None]
    area_live = jnp.where(live_mask, slave_area, jnp.zeros_like(slave_area))
    slave = jnp.concatenate(
        [slave_pos + TIME_STEP * slave_vel, slave_vel, area_live[:, None, :]], axis=1
    )
    normals = master_normals(master_tilt)
    master_data = jnp.concatenate(
        [master_cent + TIME_STEP * master_vel, normals, master_vel, master_stiff[:, None, :]],
        axis=1,
    )
    owners = pair_owner[:, 0]
    positions = jnp.arange(block_total, dtype=jnp.int32)
    earlier = (owners[:, None] == owners[None, :]) & (positions[None, :] < positions[:, None])
    slot_index = jnp.sum(earlier.astype(jnp.int32), axis=1)
    target_slot = owners * slot_depth + slot_index
    slot_hit = target_slot[None, :] == jnp.arange(devices * slot_depth, dtype=jnp.int32)[:, None]
    source = jnp.sum(jnp.where(slot_hit, positions[None, :], 0), axis=1)
    filled = jnp.any(slot_hit, axis=1)
    tagged = jnp.concatenate(
        [
            slave,
            jnp.broadcast_to(pair_master.astype(jnp.float32)[:, None, None], (block_total, 1, seg_width)),
        ],
        axis=1,
    )
    outgoing = jnp.where(filled[:, None, None], jnp.take(tagged, source, axis=0), 0.0)
    arrived = lax.all_to_all(
        outgoing.reshape(devices, slot_depth, 8, seg_width),
        ("gx", "gy"),
        split_axis=0,
        concat_axis=0,
        tiled=True,
    )
    item_total = devices * slot_depth
    arrived = arrived.reshape(item_total, 8, seg_width)
    picked = arrived[:, 7, 0].astype(jnp.int32)
    arrived = arrived[:, :7]
    paired = jnp.take(master_data, picked, axis=0)
    group_size = 16 * slot_depth

    def per_group(pairing):
        return contact_pairs(pairing[0], pairing[1])

    forces, reaction = lax.map(
        per_group,
        (
            arrived.reshape(item_total // group_size, group_size, 7, seg_width),
            paired.reshape(item_total // group_size, group_size, 10, seg_width),
        ),
    )
    forces = forces.reshape(item_total, 3, seg_width)
    reaction = reaction.reshape(item_total, seg_width)
    onehot = (picked[:, None] == jnp.arange(master_total, dtype=jnp.int32)[None, :]).astype(
        jnp.float32
    )
    master_sum = jnp.dot(onehot.T, reaction, precision=lax.Precision.HIGHEST)
    master_force = -master_sum[:, None, :] * normals
    master_contact = node_scatter_add(
        master_force.transpose(1, 0, 2).reshape(3, -1), master_node.reshape(-1), node_total
    )
    returned = lax.all_to_all(
        forces.reshape(devices, slot_depth, 3, seg_width),
        ("gx", "gy"),
        split_axis=0,
        concat_axis=0,
        tiled=True,
    )
    slave_force = jnp.take(returned.reshape(item_total, 3, seg_width), target_slot, axis=0)
    contact = master_contact + node_scatter_add(
        slave_force.transpose(1, 0, 2).reshape(3, -1), slave_node.reshape(-1), node_total
    )
    contact_field = contact.reshape(3, layers, row_cells, col_cells)
    velocity_new = velocity + TIME_STEP * (stress + contact_field) / node_mass[None]
    padded_new = padded_2(velocity_new, (("gx", 2), ("gy", 3)), 1)
    node_rate = nodal_rate(padded_new, inside)
    return (velocity_new, node_rate)


def solution(mesh):
    placed = (
        P(None, None, "gx", "gy"),
        P(None, "gx", "gy"),
        P(None, "gx", "gy"),
        P(None, "gx", "gy"),
        P(("gx", "gy"), None, None),
        P(("gx", "gy"), None),
        P(("gx", "gy")),
        P(("gx", "gy"), None),
        P(("gx", "gy"), None),
        P(("gx", "gy")),
        P(("gx", "gy"), None, None),
        P(("gx", "gy"), None, None),
        P(("gx", "gy"), None),
        P(("gx", "gy"), None),
    )
    return jax.shard_map(
        on_device,
        mesh=mesh,
        in_specs=placed,
        out_specs=(P(None, None, "gx", "gy"), P(None, "gx", "gy")),
        check_vma=False,
    )
```

```python
import jax
import jax.numpy as jnp
from jax import lax
from jax.sharding import PartitionSpec as P
from jax.experimental import pallas as pl
from jax.experimental.pallas import tpu as pltpu

LANES = 128
TILE = 2048


def split_pieces(values):
    first = values.astype(jnp.bfloat16)
    rest = values - first.astype(jnp.float32)
    second = rest.astype(jnp.bfloat16)
    third = (rest - second.astype(jnp.float32)).astype(jnp.bfloat16)
    return (first, second, third)


def gather_kernel(index_ref, table_ref, out_ref):
    node = index_ref[...]
    width = node.shape[1]
    high_count = table_ref.shape[1]
    channels = out_ref.shape[0]
    onehot = (
        lax.broadcasted_iota(jnp.int32, (high_count, width), 0) == (node >> 7)
    ).astype(jnp.bfloat16)
    gathered = None
    for piece in split_pieces(table_ref[...]):
        part = jnp.dot(piece, onehot, preferred_element_type=jnp.float32)
        gathered = part if gathered is None else gathered + part
    low_hit = lax.broadcasted_iota(jnp.int32, (LANES, width), 0) == (node & (LANES - 1))
    for c in range(channels):
        block = gathered[c * LANES : (c + 1) * LANES]
        out_ref[c : c + 1, :] = jnp.sum(jnp.where(low_hit, block, 0.0), axis=0, keepdims=True)


def scatter_kernel(index_ref, force_ref, out_ref):
    @pl.when(pl.program_id(0) == 0)
    def _():
        out_ref[...] = jnp.zeros_like(out_ref)

    node = index_ref[...]
    width = node.shape[1]
    high_count = out_ref.shape[1]
    channels = force_ref.shape[0]
    onehot = (
        lax.broadcasted_iota(jnp.int32, (high_count, width), 0) == (node >> 7)
    ).astype(jnp.bfloat16)
    low_hit = lax.broadcasted_iota(jnp.int32, (LANES, width), 0) == (node & (LANES - 1))
    total = None
    for piece in split_pieces(force_ref[...])[:2]:
        spread = jnp.concatenate(
            [jnp.where(low_hit, piece[c : c + 1, :], jnp.zeros_like(piece[c : c + 1, :])) for c in range(channels)],
            axis=0,
        )
        part = lax.dot_general(
            spread, onehot, (((1,), (1,)), ((), ())), preferred_element_type=jnp.float32
        )
        total = part if total is None else total + part
    out_ref[...] += total


def node_gather(field, nodes):
    channels, node_total = field.shape
    high_count = node_total // LANES
    table = field.reshape(channels, high_count, LANES).transpose(0, 2, 1).reshape(
        channels * LANES, high_count
    )
    count = nodes.shape[0]
    padded_count = -(-count // TILE) * TILE
    nodes = jnp.pad(nodes, (0, padded_count - count))
    return pl.pallas_call(
        gather_kernel,
        grid=(padded_count // TILE,),
        in_specs=[
            pl.BlockSpec((1, TILE), lambda i: (0, i)),
            pl.BlockSpec((channels * LANES, high_count), lambda i: (0, 0)),
        ],
        out_specs=pl.BlockSpec((channels, TILE), lambda i: (0, i)),
        out_shape=jax.ShapeDtypeStruct((channels, padded_count), jnp.float32),
    )(nodes.reshape(1, padded_count), table)[:, :count]


def node_scatter_add(forces, nodes, node_total):
    channels, count = forces.shape
    high_count = node_total // LANES
    padded_count = -(-count // TILE) * TILE
    nodes = jnp.pad(nodes, (0, padded_count - count))
    forces = jnp.pad(forces, ((0, 0), (0, padded_count - count)))
    summed = pl.pallas_call(
        scatter_kernel,
        grid=(padded_count // TILE,),
        in_specs=[
            pl.BlockSpec((1, TILE), lambda i: (0, i)),
            pl.BlockSpec((channels, TILE), lambda i: (0, i)),
        ],
        out_specs=pl.BlockSpec((channels * LANES, high_count), lambda i: (0, 0)),
        out_shape=jax.ShapeDtypeStruct((channels * LANES, high_count), jnp.float32),
    )(nodes.reshape(1, padded_count), forces)
    return summed.reshape(channels, LANES, high_count).transpose(0, 2, 1).reshape(channels, node_total)


TIME_STEP = 0.25
VISCOUS = 0.5
SOFT_GAP = 0.2
REACH_SQ = 1.0
DAMPING = 0.5


def padded_2(block, sides, width):
    for axis, dim in sides:
        count = lax.axis_size(axis)
        forward = [(i, i + 1) for i in range(count - 1)]
        backward = [(target, source) for source, target in forward]
        low = lax.ppermute(
            lax.index_in_dim(block, block.shape[dim] - 1, axis=dim, keepdims=False), axis, forward
        )
        high = lax.ppermute(lax.index_in_dim(block, 0, axis=dim, keepdims=False), axis, backward)
        block = jnp.concatenate(
            [jnp.expand_dims(low, dim), block, jnp.expand_dims(high, dim)], axis=dim
        )
    return block


def pair_mean(values, along):
    length = values.shape[along]
    return 0.5 * (
        lax.slice_in_dim(values, 0, length - 1, axis=along)
        + lax.slice_in_dim(values, 1, length, axis=along)
    )


def pair_diff(values, along):
    length = values.shape[along]
    return lax.slice_in_dim(values, 1, length, axis=along) - lax.slice_in_dim(
        values, 0, length - 1, axis=along
    )


def pair_prod(values, along):
    length = values.shape[along]
    return lax.slice_in_dim(values, 0, length - 1, axis=along) * lax.slice_in_dim(
        values, 1, length, axis=along
    )


def corner_mean(values):
    return pair_mean(pair_mean(pair_mean(values, 0), 1), 2)


def zone_rate(vel):
    rate_x = pair_diff(pair_mean(pair_mean(vel[0], 0), 2), 1)
    rate_y = pair_diff(pair_mean(pair_mean(vel[1], 0), 1), 2)
    rate_z = pair_diff(pair_mean(pair_mean(vel[2], 1), 2), 0)
    return rate_x + rate_y + rate_z


def stress_forces(padded):
    inside = pair_prod(pair_prod(pair_prod(padded[5], 0), 1), 2)
    strain = TIME_STEP * zone_rate(padded[0:3])
    pressure = inside * (
        corner_mean(padded[4]) + corner_mean(padded[3]) * (VISCOUS * strain * strain - strain)
    )
    framed = jnp.pad(pressure, ((1, 1), (0, 0), (0, 0)))
    force_x = -pair_diff(pair_mean(pair_mean(framed, 0), 2), 1)
    force_y = -pair_diff(pair_mean(pair_mean(framed, 0), 1), 2)
    force_z = -pair_diff(pair_mean(pair_mean(framed, 1), 2), 0)
    return (jnp.stack([force_x, force_y, force_z], axis=0), inside)


def nodal_rate(padded_vel, inside):
    rate = inside * zone_rate(padded_vel)
    framed = jnp.pad(rate, ((1, 1), (0, 0), (0, 0)))
    return pair_mean(pair_mean(pair_mean(framed, 0), 1), 2)


def contact_pairs(slave, master):
    delta_x = slave[:, 0, :, None] - master[:, 0, None, :]
    delta_y = slave[:, 1, :, None] - master[:, 1, None, :]
    delta_z = slave[:, 2, :, None] - master[:, 2, None, :]
    normal_x = master[:, 3, None, :]
    normal_y = master[:, 4, None, :]
    normal_z = master[:, 5, None, :]
    dist_sq = delta_x * delta_x + delta_y * delta_y + delta_z * delta_z
    gap_normal = normal_x * delta_x + normal_y * delta_y + normal_z * delta_z
    master_along = (
        master[:, 3] * master[:, 6] + master[:, 4] * master[:, 7] + master[:, 5] * master[:, 8]
    )
    closing = (
        normal_x * slave[:, 3, :, None]
        + normal_y * slave[:, 4, :, None]
        + normal_z * slave[:, 5, :, None]
    ) - master_along[:, None, :]
    weight = jnp.exp(-dist_sq / REACH_SQ)
    soft = gap_normal * (-1.0 / SOFT_GAP)
    depth_soft = SOFT_GAP * jnp.log(1.0 + jnp.exp(soft))
    push_force = (
        slave[:, 6, :, None]
        * master[:, 9, None, :]
        * weight
        * depth_soft
        * ((1.0 - DAMPING) + (2.0 * DAMPING) / (1.0 + jnp.exp(2.0 * closing)))
    )
    slave_force = jnp.stack(
        [
            jnp.sum(push_force * normal_x, axis=2),
            jnp.sum(push_force * normal_y, axis=2),
            jnp.sum(push_force * normal_z, axis=2),
        ],
        axis=1,
    )
    reaction = jnp.sum(push_force, axis=1)
    return (slave_force, reaction)


def master_normals(master_tilt):
    scale = lax.rsqrt(
        1.0 + master_tilt[:, 0] * master_tilt[:, 0] + master_tilt[:, 1] * master_tilt[:, 1]
    )
    return jnp.stack([master_tilt[:, 0] * scale, master_tilt[:, 1] * scale, scale], axis=1)


def on_device(
    velocity,
    bulk,
    prestress,
    node_mass,
    slave_pos,
    slave_area,
    seg_count,
    slave_node,
    pair_owner,
    pair_master,
    master_cent,
    master_tilt,
    master_stiff,
    master_node,
):
    count_gx = lax.axis_size("gx")
    count_gy = lax.axis_size("gy")
    devices = count_gx * count_gy
    layers, row_cells, col_cells = bulk.shape
    node_total = layers * row_cells * col_cells
    block_total, _, seg_width = slave_pos.shape
    master_total = master_cent.shape[0]
    slot_depth = (block_total + devices - 1) // devices + 1
    stacked = jnp.concatenate(
        [velocity, bulk[None], prestress[None], jnp.ones_like(bulk)[None]], axis=0
    )
    padded = padded_2(stacked, (("gx", 2), ("gy", 3)), 1)
    stress, inside = stress_forces(padded)
    vel_flat = velocity.reshape(3, node_total)
    slave_count = block_total * seg_width
    slave_vel = (
        node_gather(vel_flat, slave_node.reshape(-1))
        .reshape(3, block_total, seg_width)
        .transpose(1, 0, 2)
    )
    master_vel = (
        node_gather(vel_flat, master_node.reshape(-1))
        .reshape(3, master_total, seg_width)
        .transpose(1, 0, 2)
    )
    live_mask = jnp.arange(seg_width, dtype=jnp.int32)[None, :] < seg_count[:, None]
    area_live = jnp.where(live_mask, slave_area, jnp.zeros_like(slave_area))
    slave = jnp.concatenate(
        [slave_pos + TIME_STEP * slave_vel, slave_vel, area_live[:, None, :]], axis=1
    )
    normals = master_normals(master_tilt)
    master_data = jnp.concatenate(
        [master_cent + TIME_STEP * master_vel, normals, master_vel, master_stiff[:, None, :]],
        axis=1,
    )
    owners = pair_owner[:, 0]
    positions = jnp.arange(block_total, dtype=jnp.int32)
    earlier = (owners[:, None] == owners[None, :]) & (positions[None, :] < positions[:, None])
    slot_index = jnp.sum(earlier.astype(jnp.int32), axis=1)
    target_slot = owners * slot_depth + slot_index
    slot_hit = target_slot[None, :] == jnp.arange(devices * slot_depth, dtype=jnp.int32)[:, None]
    source = jnp.sum(jnp.where(slot_hit, positions[None, :], 0), axis=1)
    filled = jnp.any(slot_hit, axis=1)
    tagged = jnp.concatenate(
        [
            slave,
            jnp.broadcast_to(pair_master.astype(jnp.float32)[:, None, None], (block_total, 1, seg_width)),
        ],
        axis=1,
    )
    outgoing = jnp.where(filled[:, None, None], jnp.take(tagged, source, axis=0), 0.0)
    arrived = lax.all_to_all(
        outgoing.reshape(devices, slot_depth, 8, seg_width),
        ("gx", "gy"),
        split_axis=0,
        concat_axis=0,
        tiled=True,
    )
    item_total = devices * slot_depth
    arrived = arrived.reshape(item_total, 8, seg_width)
    picked = arrived[:, 7, 0].astype(jnp.int32)
    arrived = arrived[:, :7]
    paired = jnp.take(master_data, picked, axis=0)
    group_size = 16 * slot_depth

    def per_group(pairing):
        return contact_pairs(pairing[0], pairing[1])

    forces, reaction = lax.map(
        per_group,
        (
            arrived.reshape(item_total // group_size, group_size, 7, seg_width),
            paired.reshape(item_total // group_size, group_size, 10, seg_width),
        ),
    )
    forces = forces.reshape(item_total, 3, seg_width)
    reaction = reaction.reshape(item_total, seg_width)
    onehot = (picked[:, None] == jnp.arange(master_total, dtype=jnp.int32)[None, :]).astype(
        jnp.float32
    )
    master_sum = jnp.dot(onehot.T, reaction, precision=lax.Precision.HIGHEST)
    master_force = -master_sum[:, None, :] * normals
    master_contact = node_scatter_add(
        master_force.transpose(1, 0, 2).reshape(3, -1), master_node.reshape(-1), node_total
    )
    returned = lax.all_to_all(
        forces.reshape(devices, slot_depth, 3, seg_width),
        ("gx", "gy"),
        split_axis=0,
        concat_axis=0,
        tiled=True,
    )
    slave_force = jnp.take(returned.reshape(item_total, 3, seg_width), target_slot, axis=0)
    contact = master_contact + node_scatter_add(
        slave_force.transpose(1, 0, 2).reshape(3, -1), slave_node.reshape(-1), node_total
    )
    contact_field = contact.reshape(3, layers, row_cells, col_cells)
    velocity_new = velocity + TIME_STEP * (stress + contact_field) / node_mass[None]
    padded_new = padded_2(velocity_new, (("gx", 2), ("gy", 3)), 1)
    node_rate = nodal_rate(padded_new, inside)
    return (velocity_new, node_rate)


def solution(mesh):
    placed = (
        P(None, None, "gx", "gy"),
        P(None, "gx", "gy"),
        P(None, "gx", "gy"),
        P(None, "gx", "gy"),
        P(("gx", "gy"), None, None),
        P(("gx", "gy"), None),
        P(("gx", "gy")),
        P(("gx", "gy"), None),
        P(("gx", "gy"), None),
        P(("gx", "gy")),
        P(("gx", "gy"), None, None),
        P(("gx", "gy"), None, None),
        P(("gx", "gy"), None),
        P(("gx", "gy"), None),
    )
    return jax.shard_map(
        on_device,
        mesh=mesh,
        in_specs=placed,
        out_specs=(P(None, None, "gx", "gy"), P(None, "gx", "gy")),
        check_vma=False,
    )
```

```python
import jax
import jax.numpy as jnp
from jax import lax
from jax.sharding import PartitionSpec as P
from jax.experimental import pallas as pl
from jax.experimental.pallas import tpu as pltpu

LANES = 128
TILE = 2048


def split_pieces(values):
    first = values.astype(jnp.bfloat16)
    rest = values - first.astype(jnp.float32)
    second = rest.astype(jnp.bfloat16)
    third = (rest - second.astype(jnp.float32)).astype(jnp.bfloat16)
    return (first, second, third)


def gather_kernel(index_ref, table_ref, out_ref):
    node = index_ref[...]
    width = node.shape[1]
    high_count = table_ref.shape[1]
    channels = out_ref.shape[0]
    onehot = (
        lax.broadcasted_iota(jnp.int32, (high_count, width), 0) == (node >> 7)
    ).astype(jnp.bfloat16)
    gathered = None
    for piece in split_pieces(table_ref[...]):
        part = jnp.dot(piece, onehot, preferred_element_type=jnp.float32)
        gathered = part if gathered is None else gathered + part
    low_hit = lax.broadcasted_iota(jnp.int32, (LANES, width), 0) == (node & (LANES - 1))
    for c in range(channels):
        block = gathered[c * LANES : (c + 1) * LANES]
        out_ref[c : c + 1, :] = jnp.sum(jnp.where(low_hit, block, 0.0), axis=0, keepdims=True)


def scatter_kernel(index_ref, force_ref, out_ref):
    @pl.when(pl.program_id(0) == 0)
    def _():
        out_ref[...] = jnp.zeros_like(out_ref)

    node = index_ref[...]
    width = node.shape[1]
    high_count = out_ref.shape[1]
    channels = force_ref.shape[0]
    onehot = (
        lax.broadcasted_iota(jnp.int32, (high_count, width), 0) == (node >> 7)
    ).astype(jnp.bfloat16)
    low_hit = lax.broadcasted_iota(jnp.int32, (LANES, width), 0) == (node & (LANES - 1))
    total = None
    for piece in split_pieces(force_ref[...])[:2]:
        spread = jnp.concatenate(
            [jnp.where(low_hit, piece[c : c + 1, :], jnp.zeros_like(piece[c : c + 1, :])) for c in range(channels)],
            axis=0,
        )
        part = lax.dot_general(
            spread, onehot, (((1,), (1,)), ((), ())), preferred_element_type=jnp.float32
        )
        total = part if total is None else total + part
    out_ref[...] += total


def node_gather(field, nodes):
    channels, node_total = field.shape
    high_count = node_total // LANES
    table = field.reshape(channels, high_count, LANES).transpose(0, 2, 1).reshape(
        channels * LANES, high_count
    )
    count = nodes.shape[0]
    padded_count = -(-count // TILE) * TILE
    nodes = jnp.pad(nodes, (0, padded_count - count))
    return pl.pallas_call(
        gather_kernel,
        grid=(padded_count // TILE,),
        in_specs=[
            pl.BlockSpec((1, TILE), lambda i: (0, i)),
            pl.BlockSpec((channels * LANES, high_count), lambda i: (0, 0)),
        ],
        out_specs=pl.BlockSpec((channels, TILE), lambda i: (0, i)),
        out_shape=jax.ShapeDtypeStruct((channels, padded_count), jnp.float32),
    )(nodes.reshape(1, padded_count), table)[:, :count]


def node_scatter_add(forces, nodes, node_total):
    channels, count = forces.shape
    high_count = node_total // LANES
    padded_count = -(-count // TILE) * TILE
    nodes = jnp.pad(nodes, (0, padded_count - count))
    forces = jnp.pad(forces, ((0, 0), (0, padded_count - count)))
    summed = pl.pallas_call(
        scatter_kernel,
        grid=(padded_count // TILE,),
        in_specs=[
            pl.BlockSpec((1, TILE), lambda i: (0, i)),
            pl.BlockSpec((channels, TILE), lambda i: (0, i)),
        ],
        out_specs=pl.BlockSpec((channels * LANES, high_count), lambda i: (0, 0)),
        out_shape=jax.ShapeDtypeStruct((channels * LANES, high_count), jnp.float32),
    )(nodes.reshape(1, padded_count), forces)
    return summed.reshape(channels, LANES, high_count).transpose(0, 2, 1).reshape(channels, node_total)


TIME_STEP = 0.25
VISCOUS = 0.5
SOFT_GAP = 0.2
REACH_SQ = 1.0
DAMPING = 0.5


def padded_2(block, sides, width):
    for axis, dim in sides:
        count = lax.axis_size(axis)
        forward = [(i, i + 1) for i in range(count - 1)]
        backward = [(target, source) for source, target in forward]
        low = lax.ppermute(
            lax.index_in_dim(block, block.shape[dim] - 1, axis=dim, keepdims=False), axis, forward
        )
        high = lax.ppermute(lax.index_in_dim(block, 0, axis=dim, keepdims=False), axis, backward)
        block = jnp.concatenate(
            [jnp.expand_dims(low, dim), block, jnp.expand_dims(high, dim)], axis=dim
        )
    return block


def pair_mean(values, along):
    length = values.shape[along]
    return 0.5 * (
        lax.slice_in_dim(values, 0, length - 1, axis=along)
        + lax.slice_in_dim(values, 1, length, axis=along)
    )


def pair_diff(values, along):
    length = values.shape[along]
    return lax.slice_in_dim(values, 1, length, axis=along) - lax.slice_in_dim(
        values, 0, length - 1, axis=along
    )


def pair_prod(values, along):
    length = values.shape[along]
    return lax.slice_in_dim(values, 0, length - 1, axis=along) * lax.slice_in_dim(
        values, 1, length, axis=along
    )


def corner_mean(values):
    return pair_mean(pair_mean(pair_mean(values, 0), 1), 2)


def zone_rate(vel):
    rate_x = pair_diff(pair_mean(pair_mean(vel[0], 0), 2), 1)
    rate_y = pair_diff(pair_mean(pair_mean(vel[1], 0), 1), 2)
    rate_z = pair_diff(pair_mean(pair_mean(vel[2], 1), 2), 0)
    return rate_x + rate_y + rate_z


def stress_forces(padded):
    inside = pair_prod(pair_prod(pair_prod(padded[5], 0), 1), 2)
    strain = TIME_STEP * zone_rate(padded[0:3])
    pressure = inside * (
        corner_mean(padded[4]) + corner_mean(padded[3]) * (VISCOUS * strain * strain - strain)
    )
    framed = jnp.pad(pressure, ((1, 1), (0, 0), (0, 0)))
    force_x = -pair_diff(pair_mean(pair_mean(framed, 0), 2), 1)
    force_y = -pair_diff(pair_mean(pair_mean(framed, 0), 1), 2)
    force_z = -pair_diff(pair_mean(pair_mean(framed, 1), 2), 0)
    return (jnp.stack([force_x, force_y, force_z], axis=0), inside)


def nodal_rate(padded_vel, inside):
    rate = inside * zone_rate(padded_vel)
    framed = jnp.pad(rate, ((1, 1), (0, 0), (0, 0)))
    return pair_mean(pair_mean(pair_mean(framed, 0), 1), 2)


def contact_pairs(slave, master):
    delta_x = slave[:, 0, :, None] - master[:, 0, None, :]
    delta_y = slave[:, 1, :, None] - master[:, 1, None, :]
    delta_z = slave[:, 2, :, None] - master[:, 2, None, :]
    normal_x = master[:, 3, None, :]
    normal_y = master[:, 4, None, :]
    normal_z = master[:, 5, None, :]
    dist_sq = delta_x * delta_x + delta_y * delta_y + delta_z * delta_z
    gap_normal = normal_x * delta_x + normal_y * delta_y + normal_z * delta_z
    master_along = (
        master[:, 3] * master[:, 6] + master[:, 4] * master[:, 7] + master[:, 5] * master[:, 8]
    )
    closing = (
        normal_x * slave[:, 3, :, None]
        + normal_y * slave[:, 4, :, None]
        + normal_z * slave[:, 5, :, None]
    ) - master_along[:, None, :]
    weight = jnp.exp(-dist_sq / REACH_SQ)
    soft = gap_normal * (-1.0 / SOFT_GAP)
    depth_soft = SOFT_GAP * (jnp.maximum(soft, 0.0) + jnp.log1p(jnp.exp(-jnp.abs(soft))))
    push_force = (
        slave[:, 6, :, None]
        * master[:, 9, None, :]
        * weight
        * depth_soft
        * (1.0 + DAMPING * jnp.tanh(-closing))
    )
    slave_force = jnp.stack(
        [
            jnp.sum(push_force * normal_x, axis=2),
            jnp.sum(push_force * normal_y, axis=2),
            jnp.sum(push_force * normal_z, axis=2),
        ],
        axis=1,
    )
    reaction = jnp.sum(push_force, axis=1)
    return (slave_force, reaction)


def master_normals(master_tilt):
    scale = lax.rsqrt(
        1.0 + master_tilt[:, 0] * master_tilt[:, 0] + master_tilt[:, 1] * master_tilt[:, 1]
    )
    return jnp.stack([master_tilt[:, 0] * scale, master_tilt[:, 1] * scale, scale], axis=1)


def on_device(
    velocity,
    bulk,
    prestress,
    node_mass,
    slave_pos,
    slave_area,
    seg_count,
    slave_node,
    pair_owner,
    pair_master,
    master_cent,
    master_tilt,
    master_stiff,
    master_node,
):
    count_gx = lax.axis_size("gx")
    count_gy = lax.axis_size("gy")
    devices = count_gx * count_gy
    layers, row_cells, col_cells = bulk.shape
    node_total = layers * row_cells * col_cells
    block_total, _, seg_width = slave_pos.shape
    master_total = master_cent.shape[0]
    slot_depth = (block_total + devices - 1) // devices + 1
    stacked = jnp.concatenate(
        [velocity, bulk[None], prestress[None], jnp.ones_like(bulk)[None]], axis=0
    )
    padded = padded_2(stacked, (("gx", 2), ("gy", 3)), 1)
    stress, inside = stress_forces(padded)
    vel_flat = velocity.reshape(3, node_total)
    slave_count = block_total * seg_width
    slave_vel = (
        node_gather(vel_flat, slave_node.reshape(-1))
        .reshape(3, block_total, seg_width)
        .transpose(1, 0, 2)
    )
    master_vel = (
        node_gather(vel_flat, master_node.reshape(-1))
        .reshape(3, master_total, seg_width)
        .transpose(1, 0, 2)
    )
    live_mask = jnp.arange(seg_width, dtype=jnp.int32)[None, :] < seg_count[:, None]
    area_live = jnp.where(live_mask, slave_area, jnp.zeros_like(slave_area))
    slave = jnp.concatenate(
        [slave_pos + TIME_STEP * slave_vel, slave_vel, area_live[:, None, :]], axis=1
    )
    owners = pair_owner[:, 0]
    positions = jnp.arange(block_total, dtype=jnp.int32)
    earlier = (owners[:, None] == owners[None, :]) & (positions[None, :] < positions[:, None])
    slot_index = jnp.sum(earlier.astype(jnp.int32), axis=1)
    target_slot = owners * slot_depth + slot_index
    item_total = devices * slot_depth
    slot_hit = target_slot[None, :] == jnp.arange(item_total, dtype=jnp.int32)[:, None]
    source = jnp.sum(jnp.where(slot_hit, positions[None, :], 0), axis=1)
    filled = jnp.any(slot_hit, axis=1)
    request = jnp.where(filled, jnp.take(pair_master, source, axis=0), 0)
    asked = lax.all_to_all(
        request.reshape(devices, slot_depth),
        ("gx", "gy"),
        split_axis=0,
        concat_axis=0,
        tiled=True,
    ).reshape(item_total)
    normals = master_normals(master_tilt)
    master_data = jnp.concatenate(
        [master_cent + TIME_STEP * master_vel, normals, master_vel, master_stiff[:, None, :]],
        axis=1,
    )
    reply = lax.all_to_all(
        jnp.take(master_data, asked, axis=0).reshape(devices, slot_depth, 10, seg_width),
        ("gx", "gy"),
        split_axis=0,
        concat_axis=0,
        tiled=True,
    )
    paired = jnp.take(reply.reshape(item_total, 10, seg_width), target_slot, axis=0)
    group_size = block_total // 2 if block_total % 2 == 0 else block_total

    def per_group(pairing):
        return contact_pairs(pairing[0], pairing[1])

    forces, reaction = lax.map(
        per_group,
        (
            slave.reshape(block_total // group_size, group_size, 7, seg_width),
            paired.reshape(block_total // group_size, group_size, 10, seg_width),
        ),
    )
    slave_force = forces.reshape(block_total, 3, seg_width)
    reaction = reaction.reshape(block_total, seg_width)
    back = lax.all_to_all(
        jnp.where(filled[:, None], jnp.take(reaction, source, axis=0), 0.0).reshape(
            devices, slot_depth, seg_width
        ),
        ("gx", "gy"),
        split_axis=0,
        concat_axis=0,
        tiled=True,
    ).reshape(item_total, seg_width)
    slave_contact = node_scatter_add(
        slave_force.transpose(1, 0, 2).reshape(3, -1), slave_node.reshape(-1), node_total
    )
    onehot = (asked[:, None] == jnp.arange(master_total, dtype=jnp.int32)[None, :]).astype(
        jnp.float32
    )
    master_sum = jnp.dot(onehot.T, back, precision=lax.Precision.HIGHEST)
    master_force = -master_sum[:, None, :] * normals
    contact = slave_contact + node_scatter_add(
        master_force.transpose(1, 0, 2).reshape(3, -1), master_node.reshape(-1), node_total
    )
    contact_field = contact.reshape(3, layers, row_cells, col_cells)
    velocity_new = velocity + TIME_STEP * (stress + contact_field) / node_mass[None]
    padded_new = padded_2(velocity_new, (("gx", 2), ("gy", 3)), 1)
    node_rate = nodal_rate(padded_new, inside)
    return (velocity_new, node_rate)


def solution(mesh):
    placed = (
        P(None, None, "gx", "gy"),
        P(None, "gx", "gy"),
        P(None, "gx", "gy"),
        P(None, "gx", "gy"),
        P(("gx", "gy"), None, None),
        P(("gx", "gy"), None),
        P(("gx", "gy")),
        P(("gx", "gy"), None),
        P(("gx", "gy"), None),
        P(("gx", "gy")),
        P(("gx", "gy"), None, None),
        P(("gx", "gy"), None, None),
        P(("gx", "gy"), None),
        P(("gx", "gy"), None),
    )
    return jax.shard_map(
        on_device,
        mesh=mesh,
        in_specs=placed,
        out_specs=(P(None, None, "gx", "gy"), P(None, "gx", "gy")),
        check_vma=False,
    )
```

```python
import jax
import jax.numpy as jnp
from jax import lax
from jax.sharding import PartitionSpec as P
from jax.experimental import pallas as pl
from jax.experimental.pallas import tpu as pltpu

LANES = 128
TILE = 2048


def split_pieces(values):
    first = values.astype(jnp.bfloat16)
    rest = values - first.astype(jnp.float32)
    second = rest.astype(jnp.bfloat16)
    third = (rest - second.astype(jnp.float32)).astype(jnp.bfloat16)
    return (first, second, third)


def gather_kernel(index_ref, table_ref, out_ref):
    node = index_ref[...]
    width = node.shape[1]
    high_count = table_ref.shape[1]
    channels = out_ref.shape[0]
    onehot = (
        lax.broadcasted_iota(jnp.int32, (high_count, width), 0) == (node >> 7)
    ).astype(jnp.bfloat16)
    gathered = None
    for piece in split_pieces(table_ref[...])[:2]:
        part = jnp.dot(piece, onehot, preferred_element_type=jnp.float32)
        gathered = part if gathered is None else gathered + part
    low_hit = lax.broadcasted_iota(jnp.int32, (LANES, width), 0) == (node & (LANES - 1))
    for c in range(channels):
        block = gathered[c * LANES : (c + 1) * LANES]
        out_ref[c : c + 1, :] = jnp.sum(jnp.where(low_hit, block, 0.0), axis=0, keepdims=True)


def scatter_kernel(index_ref, force_ref, out_ref):
    @pl.when(pl.program_id(0) == 0)
    def _():
        out_ref[...] = jnp.zeros_like(out_ref)

    node = index_ref[...]
    width = node.shape[1]
    high_count = out_ref.shape[1]
    channels = force_ref.shape[0]
    onehot = (
        lax.broadcasted_iota(jnp.int32, (high_count, width), 0) == (node >> 7)
    ).astype(jnp.bfloat16)
    low_hit = lax.broadcasted_iota(jnp.int32, (LANES, width), 0) == (node & (LANES - 1))
    total = None
    for piece in split_pieces(force_ref[...])[:2]:
        spread = jnp.concatenate(
            [jnp.where(low_hit, piece[c : c + 1, :], jnp.zeros_like(piece[c : c + 1, :])) for c in range(channels)],
            axis=0,
        )
        part = lax.dot_general(
            spread, onehot, (((1,), (1,)), ((), ())), preferred_element_type=jnp.float32
        )
        total = part if total is None else total + part
    out_ref[...] += total


def node_gather(field, nodes):
    channels, node_total = field.shape
    high_count = node_total // LANES
    table = field.reshape(channels, high_count, LANES).transpose(0, 2, 1).reshape(
        channels * LANES, high_count
    )
    count = nodes.shape[0]
    padded_count = -(-count // TILE) * TILE
    nodes = jnp.pad(nodes, (0, padded_count - count))
    return pl.pallas_call(
        gather_kernel,
        grid=(padded_count // TILE,),
        in_specs=[
            pl.BlockSpec((1, TILE), lambda i: (0, i)),
            pl.BlockSpec((channels * LANES, high_count), lambda i: (0, 0)),
        ],
        out_specs=pl.BlockSpec((channels, TILE), lambda i: (0, i)),
        out_shape=jax.ShapeDtypeStruct((channels, padded_count), jnp.float32),
    )(nodes.reshape(1, padded_count), table)[:, :count]


def node_scatter_add(forces, nodes, node_total):
    channels, count = forces.shape
    high_count = node_total // LANES
    padded_count = -(-count // TILE) * TILE
    nodes = jnp.pad(nodes, (0, padded_count - count))
    forces = jnp.pad(forces, ((0, 0), (0, padded_count - count)))
    summed = pl.pallas_call(
        scatter_kernel,
        grid=(padded_count // TILE,),
        in_specs=[
            pl.BlockSpec((1, TILE), lambda i: (0, i)),
            pl.BlockSpec((channels, TILE), lambda i: (0, i)),
        ],
        out_specs=pl.BlockSpec((channels * LANES, high_count), lambda i: (0, 0)),
        out_shape=jax.ShapeDtypeStruct((channels * LANES, high_count), jnp.float32),
    )(nodes.reshape(1, padded_count), forces)
    return summed.reshape(channels, LANES, high_count).transpose(0, 2, 1).reshape(channels, node_total)


TIME_STEP = 0.25
VISCOUS = 0.5
SOFT_GAP = 0.2
REACH_SQ = 1.0
DAMPING = 0.5


def padded_2(block, sides, width):
    for axis, dim in sides:
        count = lax.axis_size(axis)
        forward = [(i, i + 1) for i in range(count - 1)]
        backward = [(target, source) for source, target in forward]
        low = lax.ppermute(
            lax.index_in_dim(block, block.shape[dim] - 1, axis=dim, keepdims=False), axis, forward
        )
        high = lax.ppermute(lax.index_in_dim(block, 0, axis=dim, keepdims=False), axis, backward)
        block = jnp.concatenate(
            [jnp.expand_dims(low, dim), block, jnp.expand_dims(high, dim)], axis=dim
        )
    return block


def pair_mean(values, along):
    length = values.shape[along]
    return 0.5 * (
        lax.slice_in_dim(values, 0, length - 1, axis=along)
        + lax.slice_in_dim(values, 1, length, axis=along)
    )


def pair_diff(values, along):
    length = values.shape[along]
    return lax.slice_in_dim(values, 1, length, axis=along) - lax.slice_in_dim(
        values, 0, length - 1, axis=along
    )


def pair_prod(values, along):
    length = values.shape[along]
    return lax.slice_in_dim(values, 0, length - 1, axis=along) * lax.slice_in_dim(
        values, 1, length, axis=along
    )


def corner_mean(values):
    return pair_mean(pair_mean(pair_mean(values, 0), 1), 2)


def zone_rate(vel):
    rate_x = pair_diff(pair_mean(pair_mean(vel[0], 0), 2), 1)
    rate_y = pair_diff(pair_mean(pair_mean(vel[1], 0), 1), 2)
    rate_z = pair_diff(pair_mean(pair_mean(vel[2], 1), 2), 0)
    return rate_x + rate_y + rate_z


def stress_forces(padded):
    inside = pair_prod(pair_prod(pair_prod(padded[5], 0), 1), 2)
    strain = TIME_STEP * zone_rate(padded[0:3])
    pressure = inside * (
        corner_mean(padded[4]) + corner_mean(padded[3]) * (VISCOUS * strain * strain - strain)
    )
    framed = jnp.pad(pressure, ((1, 1), (0, 0), (0, 0)))
    force_x = -pair_diff(pair_mean(pair_mean(framed, 0), 2), 1)
    force_y = -pair_diff(pair_mean(pair_mean(framed, 0), 1), 2)
    force_z = -pair_diff(pair_mean(pair_mean(framed, 1), 2), 0)
    return (jnp.stack([force_x, force_y, force_z], axis=0), inside)


def nodal_rate(padded_vel, inside):
    rate = inside * zone_rate(padded_vel)
    framed = jnp.pad(rate, ((1, 1), (0, 0), (0, 0)))
    return pair_mean(pair_mean(pair_mean(framed, 0), 1), 2)


def contact_pairs(slave, master):
    delta_x = slave[:, 0, :, None] - master[:, 0, None, :]
    delta_y = slave[:, 1, :, None] - master[:, 1, None, :]
    delta_z = slave[:, 2, :, None] - master[:, 2, None, :]
    normal_x = master[:, 3, None, :]
    normal_y = master[:, 4, None, :]
    normal_z = master[:, 5, None, :]
    dist_sq = delta_x * delta_x + delta_y * delta_y + delta_z * delta_z
    gap_normal = normal_x * delta_x + normal_y * delta_y + normal_z * delta_z
    master_along = (
        master[:, 3] * master[:, 6] + master[:, 4] * master[:, 7] + master[:, 5] * master[:, 8]
    )
    closing = (
        normal_x * slave[:, 3, :, None]
        + normal_y * slave[:, 4, :, None]
        + normal_z * slave[:, 5, :, None]
    ) - master_along[:, None, :]
    weight = jnp.exp(-dist_sq / REACH_SQ)
    soft = gap_normal * (-1.0 / SOFT_GAP)
    depth_soft = SOFT_GAP * (jnp.maximum(soft, 0.0) + jnp.log1p(jnp.exp(-jnp.abs(soft))))
    push_force = (
        slave[:, 6, :, None]
        * master[:, 9, None, :]
        * weight
        * depth_soft
        * (1.0 + DAMPING * jnp.tanh(-closing))
    )
    slave_force = jnp.stack(
        [
            jnp.sum(push_force * normal_x, axis=2),
            jnp.sum(push_force * normal_y, axis=2),
            jnp.sum(push_force * normal_z, axis=2),
        ],
        axis=1,
    )
    reaction = jnp.sum(push_force, axis=1)
    return (slave_force, reaction)


def master_normals(master_tilt):
    scale = lax.rsqrt(
        1.0 + master_tilt[:, 0] * master_tilt[:, 0] + master_tilt[:, 1] * master_tilt[:, 1]
    )
    return jnp.stack([master_tilt[:, 0] * scale, master_tilt[:, 1] * scale, scale], axis=1)


def on_device(
    velocity,
    bulk,
    prestress,
    node_mass,
    slave_pos,
    slave_area,
    seg_count,
    slave_node,
    pair_owner,
    pair_master,
    master_cent,
    master_tilt,
    master_stiff,
    master_node,
):
    count_gx = lax.axis_size("gx")
    count_gy = lax.axis_size("gy")
    devices = count_gx * count_gy
    layers, row_cells, col_cells = bulk.shape
    node_total = layers * row_cells * col_cells
    block_total, _, seg_width = slave_pos.shape
    master_total = master_cent.shape[0]
    slot_depth = (block_total + devices - 1) // devices + 1
    stacked = jnp.concatenate(
        [velocity, bulk[None], prestress[None], jnp.ones_like(bulk)[None]], axis=0
    )
    padded = padded_2(stacked, (("gx", 2), ("gy", 3)), 1)
    stress, inside = stress_forces(padded)
    vel_flat = velocity.reshape(3, node_total)
    slave_count = block_total * seg_width
    slave_vel = (
        node_gather(vel_flat, slave_node.reshape(-1))
        .reshape(3, block_total, seg_width)
        .transpose(1, 0, 2)
    )
    master_vel = (
        node_gather(vel_flat, master_node.reshape(-1))
        .reshape(3, master_total, seg_width)
        .transpose(1, 0, 2)
    )
    live_mask = jnp.arange(seg_width, dtype=jnp.int32)[None, :] < seg_count[:, None]
    area_live = jnp.where(live_mask, slave_area, jnp.zeros_like(slave_area))
    slave = jnp.concatenate(
        [slave_pos + TIME_STEP * slave_vel, slave_vel, area_live[:, None, :]], axis=1
    )
    normals = master_normals(master_tilt)
    master_data = jnp.concatenate(
        [master_cent + TIME_STEP * master_vel, normals, master_vel, master_stiff[:, None, :]],
        axis=1,
    )
    owners = pair_owner[:, 0]
    positions = jnp.arange(block_total, dtype=jnp.int32)
    earlier = (owners[:, None] == owners[None, :]) & (positions[None, :] < positions[:, None])
    slot_index = jnp.sum(earlier.astype(jnp.int32), axis=1)
    target_slot = owners * slot_depth + slot_index
    slot_hit = target_slot[None, :] == jnp.arange(devices * slot_depth, dtype=jnp.int32)[:, None]
    source = jnp.sum(jnp.where(slot_hit, positions[None, :], 0), axis=1)
    filled = jnp.any(slot_hit, axis=1)
    tagged = jnp.concatenate(
        [
            slave,
            jnp.broadcast_to(pair_master.astype(jnp.float32)[:, None, None], (block_total, 1, seg_width)),
        ],
        axis=1,
    )
    outgoing = jnp.where(filled[:, None, None], jnp.take(tagged, source, axis=0), 0.0)
    arrived = lax.all_to_all(
        outgoing.reshape(devices, slot_depth, 8, seg_width),
        ("gx", "gy"),
        split_axis=0,
        concat_axis=0,
        tiled=True,
    )
    item_total = devices * slot_depth
    arrived = arrived.reshape(item_total, 8, seg_width)
    picked = arrived[:, 7, 0].astype(jnp.int32)
    arrived = arrived[:, :7]
    paired = jnp.take(master_data, picked, axis=0)
    group_size = 16 * slot_depth

    def per_group(pairing):
        return contact_pairs(pairing[0], pairing[1])

    forces, reaction = lax.map(
        per_group,
        (
            arrived.reshape(item_total // group_size, group_size, 7, seg_width),
            paired.reshape(item_total // group_size, group_size, 10, seg_width),
        ),
    )
    forces = forces.reshape(item_total, 3, seg_width)
    reaction = reaction.reshape(item_total, seg_width)
    onehot = (picked[:, None] == jnp.arange(master_total, dtype=jnp.int32)[None, :]).astype(
        jnp.float32
    )
    master_sum = jnp.dot(onehot.T, reaction, precision=lax.Precision.HIGHEST)
    master_force = -master_sum[:, None, :] * normals
    master_contact = node_scatter_add(
        master_force.transpose(1, 0, 2).reshape(3, -1), master_node.reshape(-1), node_total
    )
    returned = lax.all_to_all(
        forces.reshape(devices, slot_depth, 3, seg_width),
        ("gx", "gy"),
        split_axis=0,
        concat_axis=0,
        tiled=True,
    )
    slave_force = jnp.take(returned.reshape(item_total, 3, seg_width), target_slot, axis=0)
    contact = master_contact + node_scatter_add(
        slave_force.transpose(1, 0, 2).reshape(3, -1), slave_node.reshape(-1), node_total
    )
    contact_field = contact.reshape(3, layers, row_cells, col_cells)
    velocity_new = velocity + TIME_STEP * (stress + contact_field) / node_mass[None]
    padded_new = padded_2(velocity_new, (("gx", 2), ("gy", 3)), 1)
    node_rate = nodal_rate(padded_new, inside)
    return (velocity_new, node_rate)


def solution(mesh):
    placed = (
        P(None, None, "gx", "gy"),
        P(None, "gx", "gy"),
        P(None, "gx", "gy"),
        P(None, "gx", "gy"),
        P(("gx", "gy"), None, None),
        P(("gx", "gy"), None),
        P(("gx", "gy")),
        P(("gx", "gy"), None),
        P(("gx", "gy"), None),
        P(("gx", "gy")),
        P(("gx", "gy"), None, None),
        P(("gx", "gy"), None, None),
        P(("gx", "gy"), None),
        P(("gx", "gy"), None),
    )
    return jax.shard_map(
        on_device,
        mesh=mesh,
        in_specs=placed,
        out_specs=(P(None, None, "gx", "gy"), P(None, "gx", "gy")),
        check_vma=False,
    )
```

```python
import jax
import jax.numpy as jnp
from jax import lax
from jax.sharding import PartitionSpec as P
from jax.experimental import pallas as pl
from jax.experimental.pallas import tpu as pltpu

LANES = 128
TILE = 2048


def split_pieces(values):
    first = values.astype(jnp.bfloat16)
    rest = values - first.astype(jnp.float32)
    second = rest.astype(jnp.bfloat16)
    third = (rest - second.astype(jnp.float32)).astype(jnp.bfloat16)
    return (first, second, third)


def gather_kernel(index_ref, table_ref, out_ref):
    node = index_ref[...]
    width = node.shape[1]
    high_count = table_ref.shape[1]
    channels = out_ref.shape[0]
    onehot = (
        lax.broadcasted_iota(jnp.int32, (high_count, width), 0) == (node >> 7)
    ).astype(jnp.bfloat16)
    gathered = None
    for piece in split_pieces(table_ref[...])[:2]:
        part = jnp.dot(piece, onehot, preferred_element_type=jnp.float32)
        gathered = part if gathered is None else gathered + part
    low_hit = lax.broadcasted_iota(jnp.int32, (LANES, width), 0) == (node & (LANES - 1))
    for c in range(channels):
        block = gathered[c * LANES : (c + 1) * LANES]
        out_ref[c : c + 1, :] = jnp.sum(jnp.where(low_hit, block, 0.0), axis=0, keepdims=True)


def scatter_kernel(index_ref, force_ref, out_ref):
    @pl.when(pl.program_id(0) == 0)
    def _():
        out_ref[...] = jnp.zeros_like(out_ref)

    node = index_ref[...]
    width = node.shape[1]
    high_count = out_ref.shape[1]
    channels = force_ref.shape[0]
    onehot = (
        lax.broadcasted_iota(jnp.int32, (high_count, width), 0) == (node >> 7)
    ).astype(jnp.bfloat16)
    low_hit = lax.broadcasted_iota(jnp.int32, (LANES, width), 0) == (node & (LANES - 1))
    total = None
    for piece in split_pieces(force_ref[...])[:2]:
        spread = jnp.concatenate(
            [jnp.where(low_hit, piece[c : c + 1, :], jnp.zeros_like(piece[c : c + 1, :])) for c in range(channels)],
            axis=0,
        )
        part = lax.dot_general(
            spread, onehot, (((1,), (1,)), ((), ())), preferred_element_type=jnp.float32
        )
        total = part if total is None else total + part
    out_ref[...] += total


def node_gather(field, nodes):
    channels, node_total = field.shape
    high_count = node_total // LANES
    table = field.reshape(channels, high_count, LANES).transpose(0, 2, 1).reshape(
        channels * LANES, high_count
    )
    count = nodes.shape[0]
    padded_count = -(-count // TILE) * TILE
    nodes = jnp.pad(nodes, (0, padded_count - count))
    return pl.pallas_call(
        gather_kernel,
        grid=(padded_count // TILE,),
        in_specs=[
            pl.BlockSpec((1, TILE), lambda i: (0, i)),
            pl.BlockSpec((channels * LANES, high_count), lambda i: (0, 0)),
        ],
        out_specs=pl.BlockSpec((channels, TILE), lambda i: (0, i)),
        out_shape=jax.ShapeDtypeStruct((channels, padded_count), jnp.float32),
    )(nodes.reshape(1, padded_count), table)[:, :count]


def node_scatter_add(forces, nodes, node_total):
    channels, count = forces.shape
    high_count = node_total // LANES
    padded_count = -(-count // TILE) * TILE
    nodes = jnp.pad(nodes, (0, padded_count - count))
    forces = jnp.pad(forces, ((0, 0), (0, padded_count - count)))
    summed = pl.pallas_call(
        scatter_kernel,
        grid=(padded_count // TILE,),
        in_specs=[
            pl.BlockSpec((1, TILE), lambda i: (0, i)),
            pl.BlockSpec((channels, TILE), lambda i: (0, i)),
        ],
        out_specs=pl.BlockSpec((channels * LANES, high_count), lambda i: (0, 0)),
        out_shape=jax.ShapeDtypeStruct((channels * LANES, high_count), jnp.float32),
    )(nodes.reshape(1, padded_count), forces)
    return summed.reshape(channels, LANES, high_count).transpose(0, 2, 1).reshape(channels, node_total)


TIME_STEP = 0.25
VISCOUS = 0.5
SOFT_GAP = 0.2
REACH_SQ = 1.0
DAMPING = 0.5


def padded_2(block, sides, width):
    for axis, dim in sides:
        count = lax.axis_size(axis)
        forward = [(i, i + 1) for i in range(count - 1)]
        backward = [(target, source) for source, target in forward]
        low = lax.ppermute(
            lax.index_in_dim(block, block.shape[dim] - 1, axis=dim, keepdims=False), axis, forward
        )
        high = lax.ppermute(lax.index_in_dim(block, 0, axis=dim, keepdims=False), axis, backward)
        block = jnp.concatenate(
            [jnp.expand_dims(low, dim), block, jnp.expand_dims(high, dim)], axis=dim
        )
    return block


def pair_mean(values, along):
    length = values.shape[along]
    return 0.5 * (
        lax.slice_in_dim(values, 0, length - 1, axis=along)
        + lax.slice_in_dim(values, 1, length, axis=along)
    )


def pair_diff(values, along):
    length = values.shape[along]
    return lax.slice_in_dim(values, 1, length, axis=along) - lax.slice_in_dim(
        values, 0, length - 1, axis=along
    )


def pair_prod(values, along):
    length = values.shape[along]
    return lax.slice_in_dim(values, 0, length - 1, axis=along) * lax.slice_in_dim(
        values, 1, length, axis=along
    )


def corner_mean(values):
    return pair_mean(pair_mean(pair_mean(values, 0), 1), 2)


def zone_rate(vel):
    rate_x = pair_diff(pair_mean(pair_mean(vel[0], 0), 2), 1)
    rate_y = pair_diff(pair_mean(pair_mean(vel[1], 0), 1), 2)
    rate_z = pair_diff(pair_mean(pair_mean(vel[2], 1), 2), 0)
    return rate_x + rate_y + rate_z


def stress_forces(padded):
    inside = pair_prod(pair_prod(pair_prod(padded[5], 0), 1), 2)
    strain = TIME_STEP * zone_rate(padded[0:3])
    pressure = inside * (
        corner_mean(padded[4]) + corner_mean(padded[3]) * (VISCOUS * strain * strain - strain)
    )
    framed = jnp.pad(pressure, ((1, 1), (0, 0), (0, 0)))
    force_x = -pair_diff(pair_mean(pair_mean(framed, 0), 2), 1)
    force_y = -pair_diff(pair_mean(pair_mean(framed, 0), 1), 2)
    force_z = -pair_diff(pair_mean(pair_mean(framed, 1), 2), 0)
    return (jnp.stack([force_x, force_y, force_z], axis=0), inside)


def nodal_rate(padded_vel, inside):
    rate = inside * zone_rate(padded_vel)
    framed = jnp.pad(rate, ((1, 1), (0, 0), (0, 0)))
    return pair_mean(pair_mean(pair_mean(framed, 0), 1), 2)


def contact_pairs(slave, master):
    delta_x = slave[:, 0, :, None] - master[:, 0, None, :]
    delta_y = slave[:, 1, :, None] - master[:, 1, None, :]
    delta_z = slave[:, 2, :, None] - master[:, 2, None, :]
    normal_x = master[:, 3, None, :]
    normal_y = master[:, 4, None, :]
    normal_z = master[:, 5, None, :]
    dist_sq = delta_x * delta_x + delta_y * delta_y + delta_z * delta_z
    gap_normal = normal_x * delta_x + normal_y * delta_y + normal_z * delta_z
    master_along = (
        master[:, 3] * master[:, 6] + master[:, 4] * master[:, 7] + master[:, 5] * master[:, 8]
    )
    closing = (
        normal_x * slave[:, 3, :, None]
        + normal_y * slave[:, 4, :, None]
        + normal_z * slave[:, 5, :, None]
    ) - master_along[:, None, :]
    weight = jnp.exp(-dist_sq / REACH_SQ)
    soft = gap_normal * (-1.0 / SOFT_GAP)
    depth_soft = SOFT_GAP * (jnp.maximum(soft, 0.0) + jnp.log1p(jnp.exp(-jnp.abs(soft))))
    push_force = (
        slave[:, 6, :, None]
        * master[:, 9, None, :]
        * weight
        * depth_soft
        * (1.0 + DAMPING * jnp.tanh(-closing))
    )
    slave_force = jnp.einsum(
        "gij,gcj->gci", push_force, master[:, 3:6], precision=lax.Precision.HIGHEST
    )
    reaction = jnp.sum(push_force, axis=1)
    return (slave_force, reaction)


def master_normals(master_tilt):
    scale = lax.rsqrt(
        1.0 + master_tilt[:, 0] * master_tilt[:, 0] + master_tilt[:, 1] * master_tilt[:, 1]
    )
    return jnp.stack([master_tilt[:, 0] * scale, master_tilt[:, 1] * scale, scale], axis=1)


def on_device(
    velocity,
    bulk,
    prestress,
    node_mass,
    slave_pos,
    slave_area,
    seg_count,
    slave_node,
    pair_owner,
    pair_master,
    master_cent,
    master_tilt,
    master_stiff,
    master_node,
):
    count_gx = lax.axis_size("gx")
    count_gy = lax.axis_size("gy")
    devices = count_gx * count_gy
    layers, row_cells, col_cells = bulk.shape
    node_total = layers * row_cells * col_cells
    block_total, _, seg_width = slave_pos.shape
    master_total = master_cent.shape[0]
    slot_depth = (block_total + devices - 1) // devices + 1
    stacked = jnp.concatenate(
        [velocity, bulk[None], prestress[None], jnp.ones_like(bulk)[None]], axis=0
    )
    padded = padded_2(stacked, (("gx", 2), ("gy", 3)), 1)
    stress, inside = stress_forces(padded)
    vel_flat = velocity.reshape(3, node_total)
    slave_count = block_total * seg_width
    slave_vel = (
        node_gather(vel_flat, slave_node.reshape(-1))
        .reshape(3, block_total, seg_width)
        .transpose(1, 0, 2)
    )
    master_vel = (
        node_gather(vel_flat, master_node.reshape(-1))
        .reshape(3, master_total, seg_width)
        .transpose(1, 0, 2)
    )
    live_mask = jnp.arange(seg_width, dtype=jnp.int32)[None, :] < seg_count[:, None]
    area_live = jnp.where(live_mask, slave_area, jnp.zeros_like(slave_area))
    slave = jnp.concatenate(
        [slave_pos + TIME_STEP * slave_vel, slave_vel, area_live[:, None, :]], axis=1
    )
    normals = master_normals(master_tilt)
    master_data = jnp.concatenate(
        [master_cent + TIME_STEP * master_vel, normals, master_vel, master_stiff[:, None, :]],
        axis=1,
    )
    owners = pair_owner[:, 0]
    positions = jnp.arange(block_total, dtype=jnp.int32)
    earlier = (owners[:, None] == owners[None, :]) & (positions[None, :] < positions[:, None])
    slot_index = jnp.sum(earlier.astype(jnp.int32), axis=1)
    target_slot = owners * slot_depth + slot_index
    slot_hit = target_slot[None, :] == jnp.arange(devices * slot_depth, dtype=jnp.int32)[:, None]
    source = jnp.sum(jnp.where(slot_hit, positions[None, :], 0), axis=1)
    filled = jnp.any(slot_hit, axis=1)
    tagged = jnp.concatenate(
        [
            slave,
            jnp.broadcast_to(pair_master.astype(jnp.float32)[:, None, None], (block_total, 1, seg_width)),
        ],
        axis=1,
    )
    outgoing = jnp.where(filled[:, None, None], jnp.take(tagged, source, axis=0), 0.0)
    arrived = lax.all_to_all(
        outgoing.reshape(devices, slot_depth, 8, seg_width),
        ("gx", "gy"),
        split_axis=0,
        concat_axis=0,
        tiled=True,
    )
    item_total = devices * slot_depth
    arrived = arrived.reshape(item_total, 8, seg_width)
    picked = arrived[:, 7, 0].astype(jnp.int32)
    arrived = arrived[:, :7]
    paired = jnp.take(master_data, picked, axis=0)
    group_size = 16 * slot_depth

    def per_group(pairing):
        return contact_pairs(pairing[0], pairing[1])

    forces, reaction = lax.map(
        per_group,
        (
            arrived.reshape(item_total // group_size, group_size, 7, seg_width),
            paired.reshape(item_total // group_size, group_size, 10, seg_width),
        ),
    )
    forces = forces.reshape(item_total, 3, seg_width)
    reaction = reaction.reshape(item_total, seg_width)
    onehot = (picked[:, None] == jnp.arange(master_total, dtype=jnp.int32)[None, :]).astype(
        jnp.float32
    )
    master_sum = jnp.dot(onehot.T, reaction, precision=lax.Precision.HIGHEST)
    master_force = -master_sum[:, None, :] * normals
    master_contact = node_scatter_add(
        master_force.transpose(1, 0, 2).reshape(3, -1), master_node.reshape(-1), node_total
    )
    returned = lax.all_to_all(
        forces.reshape(devices, slot_depth, 3, seg_width),
        ("gx", "gy"),
        split_axis=0,
        concat_axis=0,
        tiled=True,
    )
    slave_force = jnp.take(returned.reshape(item_total, 3, seg_width), target_slot, axis=0)
    contact = master_contact + node_scatter_add(
        slave_force.transpose(1, 0, 2).reshape(3, -1), slave_node.reshape(-1), node_total
    )
    contact_field = contact.reshape(3, layers, row_cells, col_cells)
    velocity_new = velocity + TIME_STEP * (stress + contact_field) / node_mass[None]
    padded_new = padded_2(velocity_new, (("gx", 2), ("gy", 3)), 1)
    node_rate = nodal_rate(padded_new, inside)
    return (velocity_new, node_rate)


def solution(mesh):
    placed = (
        P(None, None, "gx", "gy"),
        P(None, "gx", "gy"),
        P(None, "gx", "gy"),
        P(None, "gx", "gy"),
        P(("gx", "gy"), None, None),
        P(("gx", "gy"), None),
        P(("gx", "gy")),
        P(("gx", "gy"), None),
        P(("gx", "gy"), None),
        P(("gx", "gy")),
        P(("gx", "gy"), None, None),
        P(("gx", "gy"), None, None),
        P(("gx", "gy"), None),
        P(("gx", "gy"), None),
    )
    return jax.shard_map(
        on_device,
        mesh=mesh,
        in_specs=placed,
        out_specs=(P(None, None, "gx", "gy"), P(None, "gx", "gy")),
        check_vma=False,
    )
```

```python
import jax
import jax.numpy as jnp
from jax import lax
from jax.sharding import PartitionSpec as P
from jax.experimental import pallas as pl
from jax.experimental.pallas import tpu as pltpu

LANES = 128
TILE = 2048


def split_pieces(values):
    first = values.astype(jnp.bfloat16)
    rest = values - first.astype(jnp.float32)
    second = rest.astype(jnp.bfloat16)
    third = (rest - second.astype(jnp.float32)).astype(jnp.bfloat16)
    return (first, second, third)


def gather_kernel(index_ref, table_ref, out_ref):
    node = index_ref[...]
    width = node.shape[1]
    high_count = table_ref.shape[1]
    channels = out_ref.shape[0]
    onehot = (
        lax.broadcasted_iota(jnp.int32, (high_count, width), 0) == (node >> 7)
    ).astype(jnp.bfloat16)
    gathered = None
    for piece in split_pieces(table_ref[...])[:2]:
        part = jnp.dot(piece, onehot, preferred_element_type=jnp.float32)
        gathered = part if gathered is None else gathered + part
    low_hit = lax.broadcasted_iota(jnp.int32, (LANES, width), 0) == (node & (LANES - 1))
    for c in range(channels):
        block = gathered[c * LANES : (c + 1) * LANES]
        out_ref[c : c + 1, :] = jnp.sum(jnp.where(low_hit, block, 0.0), axis=0, keepdims=True)


def scatter_kernel(index_ref, force_ref, out_ref):
    @pl.when(pl.program_id(0) == 0)
    def _():
        out_ref[...] = jnp.zeros_like(out_ref)

    node = index_ref[...]
    width = node.shape[1]
    high_count = out_ref.shape[1]
    channels = force_ref.shape[0]
    onehot = (
        lax.broadcasted_iota(jnp.int32, (high_count, width), 0) == (node >> 7)
    ).astype(jnp.bfloat16)
    low_hit = lax.broadcasted_iota(jnp.int32, (LANES, width), 0) == (node & (LANES - 1))
    total = None
    for piece in split_pieces(force_ref[...])[:2]:
        spread = jnp.concatenate(
            [jnp.where(low_hit, piece[c : c + 1, :], jnp.zeros_like(piece[c : c + 1, :])) for c in range(channels)],
            axis=0,
        )
        part = lax.dot_general(
            spread, onehot, (((1,), (1,)), ((), ())), preferred_element_type=jnp.float32
        )
        total = part if total is None else total + part
    out_ref[...] += total


def node_gather(field, nodes):
    channels, node_total = field.shape
    high_count = node_total // LANES
    table = field.reshape(channels, high_count, LANES).transpose(0, 2, 1).reshape(
        channels * LANES, high_count
    )
    count = nodes.shape[0]
    padded_count = -(-count // TILE) * TILE
    nodes = jnp.pad(nodes, (0, padded_count - count))
    return pl.pallas_call(
        gather_kernel,
        grid=(padded_count // TILE,),
        in_specs=[
            pl.BlockSpec((1, TILE), lambda i: (0, i)),
            pl.BlockSpec((channels * LANES, high_count), lambda i: (0, 0)),
        ],
        out_specs=pl.BlockSpec((channels, TILE), lambda i: (0, i)),
        out_shape=jax.ShapeDtypeStruct((channels, padded_count), jnp.float32),
    )(nodes.reshape(1, padded_count), table)[:, :count]


def node_scatter_add(forces, nodes, node_total):
    channels, count = forces.shape
    high_count = node_total // LANES
    padded_count = -(-count // TILE) * TILE
    nodes = jnp.pad(nodes, (0, padded_count - count))
    forces = jnp.pad(forces, ((0, 0), (0, padded_count - count)))
    summed = pl.pallas_call(
        scatter_kernel,
        grid=(padded_count // TILE,),
        in_specs=[
            pl.BlockSpec((1, TILE), lambda i: (0, i)),
            pl.BlockSpec((channels, TILE), lambda i: (0, i)),
        ],
        out_specs=pl.BlockSpec((channels * LANES, high_count), lambda i: (0, 0)),
        out_shape=jax.ShapeDtypeStruct((channels * LANES, high_count), jnp.float32),
    )(nodes.reshape(1, padded_count), forces)
    return summed.reshape(channels, LANES, high_count).transpose(0, 2, 1).reshape(channels, node_total)


TIME_STEP = 0.25
VISCOUS = 0.5
SOFT_GAP = 0.2
REACH_SQ = 1.0
DAMPING = 0.5


def padded_2(block, sides, width):
    for axis, dim in sides:
        count = lax.axis_size(axis)
        forward = [(i, i + 1) for i in range(count - 1)]
        backward = [(target, source) for source, target in forward]
        low = lax.ppermute(
            lax.index_in_dim(block, block.shape[dim] - 1, axis=dim, keepdims=False), axis, forward
        )
        high = lax.ppermute(lax.index_in_dim(block, 0, axis=dim, keepdims=False), axis, backward)
        block = jnp.concatenate(
            [jnp.expand_dims(low, dim), block, jnp.expand_dims(high, dim)], axis=dim
        )
    return block


def pair_mean(values, along):
    length = values.shape[along]
    return 0.5 * (
        lax.slice_in_dim(values, 0, length - 1, axis=along)
        + lax.slice_in_dim(values, 1, length, axis=along)
    )


def pair_diff(values, along):
    length = values.shape[along]
    return lax.slice_in_dim(values, 1, length, axis=along) - lax.slice_in_dim(
        values, 0, length - 1, axis=along
    )


def pair_prod(values, along):
    length = values.shape[along]
    return lax.slice_in_dim(values, 0, length - 1, axis=along) * lax.slice_in_dim(
        values, 1, length, axis=along
    )


def corner_mean(values):
    return pair_mean(pair_mean(pair_mean(values, 0), 1), 2)


def zone_rate(vel):
    rate_x = pair_diff(pair_mean(pair_mean(vel[0], 0), 2), 1)
    rate_y = pair_diff(pair_mean(pair_mean(vel[1], 0), 1), 2)
    rate_z = pair_diff(pair_mean(pair_mean(vel[2], 1), 2), 0)
    return rate_x + rate_y + rate_z


def stress_forces(padded):
    inside = pair_prod(pair_prod(pair_prod(padded[5], 0), 1), 2)
    strain = TIME_STEP * zone_rate(padded[0:3])
    pressure = inside * (
        corner_mean(padded[4]) + corner_mean(padded[3]) * (VISCOUS * strain * strain - strain)
    )
    framed = jnp.pad(pressure, ((1, 1), (0, 0), (0, 0)))
    force_x = -pair_diff(pair_mean(pair_mean(framed, 0), 2), 1)
    force_y = -pair_diff(pair_mean(pair_mean(framed, 0), 1), 2)
    force_z = -pair_diff(pair_mean(pair_mean(framed, 1), 2), 0)
    return (jnp.stack([force_x, force_y, force_z], axis=0), inside)


def nodal_rate(padded_vel, inside):
    rate = inside * zone_rate(padded_vel)
    framed = jnp.pad(rate, ((1, 1), (0, 0), (0, 0)))
    return pair_mean(pair_mean(pair_mean(framed, 0), 1), 2)


def contact_pairs(slave, master):
    delta_x = slave[:, 0, None, :] - master[:, 0, :, None]
    delta_y = slave[:, 1, None, :] - master[:, 1, :, None]
    delta_z = slave[:, 2, None, :] - master[:, 2, :, None]
    normal_x = master[:, 3, :, None]
    normal_y = master[:, 4, :, None]
    normal_z = master[:, 5, :, None]
    dist_sq = delta_x * delta_x + delta_y * delta_y + delta_z * delta_z
    gap_normal = normal_x * delta_x + normal_y * delta_y + normal_z * delta_z
    master_along = (
        master[:, 3] * master[:, 6] + master[:, 4] * master[:, 7] + master[:, 5] * master[:, 8]
    )
    closing = (
        normal_x * slave[:, 3, None, :]
        + normal_y * slave[:, 4, None, :]
        + normal_z * slave[:, 5, None, :]
    ) - master_along[:, :, None]
    weight = jnp.exp(-dist_sq / REACH_SQ)
    soft = gap_normal * (-1.0 / SOFT_GAP)
    depth_soft = SOFT_GAP * (jnp.maximum(soft, 0.0) + jnp.log1p(jnp.exp(-jnp.abs(soft))))
    push_force = (
        slave[:, 6, None, :]
        * master[:, 9, :, None]
        * weight
        * depth_soft
        * (1.0 + DAMPING * jnp.tanh(-closing))
    )
    slave_force = jnp.stack(
        [
            jnp.sum(push_force * normal_x, axis=1),
            jnp.sum(push_force * normal_y, axis=1),
            jnp.sum(push_force * normal_z, axis=1),
        ],
        axis=1,
    )
    reaction = jnp.sum(push_force, axis=2)
    return (slave_force, reaction)


def master_normals(master_tilt):
    scale = lax.rsqrt(
        1.0 + master_tilt[:, 0] * master_tilt[:, 0] + master_tilt[:, 1] * master_tilt[:, 1]
    )
    return jnp.stack([master_tilt[:, 0] * scale, master_tilt[:, 1] * scale, scale], axis=1)


def on_device(
    velocity,
    bulk,
    prestress,
    node_mass,
    slave_pos,
    slave_area,
    seg_count,
    slave_node,
    pair_owner,
    pair_master,
    master_cent,
    master_tilt,
    master_stiff,
    master_node,
):
    count_gx = lax.axis_size("gx")
    count_gy = lax.axis_size("gy")
    devices = count_gx * count_gy
    layers, row_cells, col_cells = bulk.shape
    node_total = layers * row_cells * col_cells
    block_total, _, seg_width = slave_pos.shape
    master_total = master_cent.shape[0]
    slot_depth = (block_total + devices - 1) // devices + 1
    stacked = jnp.concatenate(
        [velocity, bulk[None], prestress[None], jnp.ones_like(bulk)[None]], axis=0
    )
    padded = padded_2(stacked, (("gx", 2), ("gy", 3)), 1)
    stress, inside = stress_forces(padded)
    vel_flat = velocity.reshape(3, node_total)
    slave_count = block_total * seg_width
    slave_vel = (
        node_gather(vel_flat, slave_node.reshape(-1))
        .reshape(3, block_total, seg_width)
        .transpose(1, 0, 2)
    )
    master_vel = (
        node_gather(vel_flat, master_node.reshape(-1))
        .reshape(3, master_total, seg_width)
        .transpose(1, 0, 2)
    )
    live_mask = jnp.arange(seg_width, dtype=jnp.int32)[None, :] < seg_count[:, None]
    area_live = jnp.where(live_mask, slave_area, jnp.zeros_like(slave_area))
    slave = jnp.concatenate(
        [slave_pos + TIME_STEP * slave_vel, slave_vel, area_live[:, None, :]], axis=1
    )
    normals = master_normals(master_tilt)
    master_data = jnp.concatenate(
        [master_cent + TIME_STEP * master_vel, normals, master_vel, master_stiff[:, None, :]],
        axis=1,
    )
    owners = pair_owner[:, 0]
    positions = jnp.arange(block_total, dtype=jnp.int32)
    earlier = (owners[:, None] == owners[None, :]) & (positions[None, :] < positions[:, None])
    slot_index = jnp.sum(earlier.astype(jnp.int32), axis=1)
    target_slot = owners * slot_depth + slot_index
    slot_hit = target_slot[None, :] == jnp.arange(devices * slot_depth, dtype=jnp.int32)[:, None]
    source = jnp.sum(jnp.where(slot_hit, positions[None, :], 0), axis=1)
    filled = jnp.any(slot_hit, axis=1)
    tagged = jnp.concatenate(
        [
            slave,
            jnp.broadcast_to(pair_master.astype(jnp.float32)[:, None, None], (block_total, 1, seg_width)),
        ],
        axis=1,
    )
    outgoing = jnp.where(filled[:, None, None], jnp.take(tagged, source, axis=0), 0.0)
    arrived = lax.all_to_all(
        outgoing.reshape(devices, slot_depth, 8, seg_width),
        ("gx", "gy"),
        split_axis=0,
        concat_axis=0,
        tiled=True,
    )
    item_total = devices * slot_depth
    arrived = arrived.reshape(item_total, 8, seg_width)
    picked = arrived[:, 7, 0].astype(jnp.int32)
    arrived = arrived[:, :7]
    paired = jnp.take(master_data, picked, axis=0)
    group_size = 16 * slot_depth

    def per_group(pairing):
        return contact_pairs(pairing[0], pairing[1])

    forces, reaction = lax.map(
        per_group,
        (
            arrived.reshape(item_total // group_size, group_size, 7, seg_width),
            paired.reshape(item_total // group_size, group_size, 10, seg_width),
        ),
    )
    forces = forces.reshape(item_total, 3, seg_width)
    reaction = reaction.reshape(item_total, seg_width)
    onehot = (picked[:, None] == jnp.arange(master_total, dtype=jnp.int32)[None, :]).astype(
        jnp.float32
    )
    master_sum = jnp.dot(onehot.T, reaction, precision=lax.Precision.HIGHEST)
    master_force = -master_sum[:, None, :] * normals
    master_contact = node_scatter_add(
        master_force.transpose(1, 0, 2).reshape(3, -1), master_node.reshape(-1), node_total
    )
    returned = lax.all_to_all(
        forces.reshape(devices, slot_depth, 3, seg_width),
        ("gx", "gy"),
        split_axis=0,
        concat_axis=0,
        tiled=True,
    )
    slave_force = jnp.take(returned.reshape(item_total, 3, seg_width), target_slot, axis=0)
    contact = master_contact + node_scatter_add(
        slave_force.transpose(1, 0, 2).reshape(3, -1), slave_node.reshape(-1), node_total
    )
    contact_field = contact.reshape(3, layers, row_cells, col_cells)
    velocity_new = velocity + TIME_STEP * (stress + contact_field) / node_mass[None]
    padded_new = padded_2(velocity_new, (("gx", 2), ("gy", 3)), 1)
    node_rate = nodal_rate(padded_new, inside)
    return (velocity_new, node_rate)


def solution(mesh):
    placed = (
        P(None, None, "gx", "gy"),
        P(None, "gx", "gy"),
        P(None, "gx", "gy"),
        P(None, "gx", "gy"),
        P(("gx", "gy"), None, None),
        P(("gx", "gy"), None),
        P(("gx", "gy")),
        P(("gx", "gy"), None),
        P(("gx", "gy"), None),
        P(("gx", "gy")),
        P(("gx", "gy"), None, None),
        P(("gx", "gy"), None, None),
        P(("gx", "gy"), None),
        P(("gx", "gy"), None),
    )
    return jax.shard_map(
        on_device,
        mesh=mesh,
        in_specs=placed,
        out_specs=(P(None, None, "gx", "gy"), P(None, "gx", "gy")),
        check_vma=False,
    )
```

```python
import jax
import jax.numpy as jnp
from jax import lax
from jax.sharding import PartitionSpec as P
from jax.experimental import pallas as pl
from jax.experimental.pallas import tpu as pltpu

LANES = 128
TILE = 2048


def split_pieces(values):
    first = values.astype(jnp.bfloat16)
    rest = values - first.astype(jnp.float32)
    second = rest.astype(jnp.bfloat16)
    third = (rest - second.astype(jnp.float32)).astype(jnp.bfloat16)
    return (first, second, third)


def gather_kernel(index_ref, table_ref, out_ref):
    node = index_ref[...]
    width = node.shape[1]
    high_count = table_ref.shape[1]
    channels = out_ref.shape[0]
    onehot = (
        lax.broadcasted_iota(jnp.int32, (high_count, width), 0) == (node >> 7)
    ).astype(jnp.bfloat16)
    gathered = None
    for piece in split_pieces(table_ref[...])[:2]:
        part = jnp.dot(piece, onehot, preferred_element_type=jnp.float32)
        gathered = part if gathered is None else gathered + part
    low_hit = lax.broadcasted_iota(jnp.int32, (LANES, width), 0) == (node & (LANES - 1))
    for c in range(channels):
        block = gathered[c * LANES : (c + 1) * LANES]
        out_ref[c : c + 1, :] = jnp.sum(jnp.where(low_hit, block, 0.0), axis=0, keepdims=True)


def scatter_kernel(index_ref, force_ref, out_ref):
    @pl.when(pl.program_id(0) == 0)
    def _():
        out_ref[...] = jnp.zeros_like(out_ref)

    node = index_ref[...]
    width = node.shape[1]
    high_count = out_ref.shape[1]
    channels = force_ref.shape[0]
    onehot = (
        lax.broadcasted_iota(jnp.int32, (high_count, width), 0) == (node >> 7)
    ).astype(jnp.bfloat16)
    low_hit = lax.broadcasted_iota(jnp.int32, (LANES, width), 0) == (node & (LANES - 1))
    total = None
    for piece in split_pieces(force_ref[...])[:2]:
        spread = jnp.concatenate(
            [jnp.where(low_hit, piece[c : c + 1, :], jnp.zeros_like(piece[c : c + 1, :])) for c in range(channels)],
            axis=0,
        )
        part = lax.dot_general(
            spread, onehot, (((1,), (1,)), ((), ())), preferred_element_type=jnp.float32
        )
        total = part if total is None else total + part
    out_ref[...] += total


def node_gather(field, nodes):
    channels, node_total = field.shape
    high_count = node_total // LANES
    table = field.reshape(channels, high_count, LANES).transpose(0, 2, 1).reshape(
        channels * LANES, high_count
    )
    count = nodes.shape[0]
    padded_count = -(-count // TILE) * TILE
    nodes = jnp.pad(nodes, (0, padded_count - count))
    return pl.pallas_call(
        gather_kernel,
        grid=(padded_count // TILE,),
        in_specs=[
            pl.BlockSpec((1, TILE), lambda i: (0, i)),
            pl.BlockSpec((channels * LANES, high_count), lambda i: (0, 0)),
        ],
        out_specs=pl.BlockSpec((channels, TILE), lambda i: (0, i)),
        out_shape=jax.ShapeDtypeStruct((channels, padded_count), jnp.float32),
    )(nodes.reshape(1, padded_count), table)[:, :count]


def node_scatter_add(forces, nodes, node_total):
    channels, count = forces.shape
    high_count = node_total // LANES
    padded_count = -(-count // TILE) * TILE
    nodes = jnp.pad(nodes, (0, padded_count - count))
    forces = jnp.pad(forces, ((0, 0), (0, padded_count - count)))
    summed = pl.pallas_call(
        scatter_kernel,
        grid=(padded_count // TILE,),
        in_specs=[
            pl.BlockSpec((1, TILE), lambda i: (0, i)),
            pl.BlockSpec((channels, TILE), lambda i: (0, i)),
        ],
        out_specs=pl.BlockSpec((channels * LANES, high_count), lambda i: (0, 0)),
        out_shape=jax.ShapeDtypeStruct((channels * LANES, high_count), jnp.float32),
    )(nodes.reshape(1, padded_count), forces)
    return summed.reshape(channels, LANES, high_count).transpose(0, 2, 1).reshape(channels, node_total)


TIME_STEP = 0.25
VISCOUS = 0.5
SOFT_GAP = 0.2
REACH_SQ = 1.0
DAMPING = 0.5


def padded_2(block, sides, width):
    for axis, dim in sides:
        count = lax.axis_size(axis)
        forward = [(i, i + 1) for i in range(count - 1)]
        backward = [(target, source) for source, target in forward]
        low = lax.ppermute(
            lax.index_in_dim(block, block.shape[dim] - 1, axis=dim, keepdims=False), axis, forward
        )
        high = lax.ppermute(lax.index_in_dim(block, 0, axis=dim, keepdims=False), axis, backward)
        block = jnp.concatenate(
            [jnp.expand_dims(low, dim), block, jnp.expand_dims(high, dim)], axis=dim
        )
    return block


def pair_mean(values, along):
    length = values.shape[along]
    return 0.5 * (
        lax.slice_in_dim(values, 0, length - 1, axis=along)
        + lax.slice_in_dim(values, 1, length, axis=along)
    )


def pair_diff(values, along):
    length = values.shape[along]
    return lax.slice_in_dim(values, 1, length, axis=along) - lax.slice_in_dim(
        values, 0, length - 1, axis=along
    )


def pair_prod(values, along):
    length = values.shape[along]
    return lax.slice_in_dim(values, 0, length - 1, axis=along) * lax.slice_in_dim(
        values, 1, length, axis=along
    )


def corner_mean(values):
    return pair_mean(pair_mean(pair_mean(values, 0), 1), 2)


def zone_rate(vel):
    rate_x = pair_diff(pair_mean(pair_mean(vel[0], 0), 2), 1)
    rate_y = pair_diff(pair_mean(pair_mean(vel[1], 0), 1), 2)
    rate_z = pair_diff(pair_mean(pair_mean(vel[2], 1), 2), 0)
    return rate_x + rate_y + rate_z


def stress_forces(padded):
    inside = pair_prod(pair_prod(pair_prod(padded[5], 0), 1), 2)
    strain = TIME_STEP * zone_rate(padded[0:3])
    pressure = inside * (
        corner_mean(padded[4]) + corner_mean(padded[3]) * (VISCOUS * strain * strain - strain)
    )
    framed = jnp.pad(pressure, ((1, 1), (0, 0), (0, 0)))
    force_x = -pair_diff(pair_mean(pair_mean(framed, 0), 2), 1)
    force_y = -pair_diff(pair_mean(pair_mean(framed, 0), 1), 2)
    force_z = -pair_diff(pair_mean(pair_mean(framed, 1), 2), 0)
    return (jnp.stack([force_x, force_y, force_z], axis=0), inside)


def nodal_rate(padded_vel, inside):
    rate = inside * zone_rate(padded_vel)
    framed = jnp.pad(rate, ((1, 1), (0, 0), (0, 0)))
    return pair_mean(pair_mean(pair_mean(framed, 0), 1), 2)


def contact_pairs(slave, master):
    delta_x = slave[:, 0, None, :] - master[:, 0, :, None]
    delta_y = slave[:, 1, None, :] - master[:, 1, :, None]
    delta_z = slave[:, 2, None, :] - master[:, 2, :, None]
    normal_x = master[:, 3, :, None]
    normal_y = master[:, 4, :, None]
    normal_z = master[:, 5, :, None]
    dist_sq = delta_x * delta_x + delta_y * delta_y + delta_z * delta_z
    gap_normal = normal_x * delta_x + normal_y * delta_y + normal_z * delta_z
    master_along = (
        master[:, 3] * master[:, 6] + master[:, 4] * master[:, 7] + master[:, 5] * master[:, 8]
    )
    closing = (
        normal_x * slave[:, 3, None, :]
        + normal_y * slave[:, 4, None, :]
        + normal_z * slave[:, 5, None, :]
    ) - master_along[:, :, None]
    weight = jnp.exp(-dist_sq / REACH_SQ)
    soft = gap_normal * (-1.0 / SOFT_GAP)
    depth_soft = SOFT_GAP * (jnp.maximum(soft, 0.0) + jnp.log1p(jnp.exp(-jnp.abs(soft))))
    push_force = (
        slave[:, 6, None, :]
        * master[:, 9, :, None]
        * weight
        * depth_soft
        * (1.0 + DAMPING * jnp.tanh(-closing))
    )
    slave_force = jnp.stack(
        [
            jnp.sum(push_force * normal_x, axis=1),
            jnp.sum(push_force * normal_y, axis=1),
            jnp.sum(push_force * normal_z, axis=1),
        ],
        axis=1,
    )
    reaction = jnp.sum(push_force, axis=2)
    return (slave_force, reaction)


def master_normals(master_tilt):
    scale = lax.rsqrt(
        1.0 + master_tilt[:, 0] * master_tilt[:, 0] + master_tilt[:, 1] * master_tilt[:, 1]
    )
    return jnp.stack([master_tilt[:, 0] * scale, master_tilt[:, 1] * scale, scale], axis=1)


def on_device(
    velocity,
    bulk,
    prestress,
    node_mass,
    slave_pos,
    slave_area,
    seg_count,
    slave_node,
    pair_owner,
    pair_master,
    master_cent,
    master_tilt,
    master_stiff,
    master_node,
):
    count_gx = lax.axis_size("gx")
    count_gy = lax.axis_size("gy")
    devices = count_gx * count_gy
    layers, row_cells, col_cells = bulk.shape
    node_total = layers * row_cells * col_cells
    block_total, _, seg_width = slave_pos.shape
    master_total = master_cent.shape[0]
    slot_depth = (block_total + devices - 1) // devices + 1
    stacked = jnp.concatenate(
        [velocity, bulk[None], prestress[None], jnp.ones_like(bulk)[None]], axis=0
    )
    padded = padded_2(stacked, (("gx", 2), ("gy", 3)), 1)
    stress, inside = stress_forces(padded)
    vel_flat = velocity.reshape(3, node_total)
    slave_count = block_total * seg_width
    slave_vel = (
        node_gather(vel_flat, slave_node.reshape(-1))
        .reshape(3, block_total, seg_width)
        .transpose(1, 0, 2)
    )
    master_vel = (
        node_gather(vel_flat, master_node.reshape(-1))
        .reshape(3, master_total, seg_width)
        .transpose(1, 0, 2)
    )
    live_mask = jnp.arange(seg_width, dtype=jnp.int32)[None, :] < seg_count[:, None]
    area_live = jnp.where(live_mask, slave_area, jnp.zeros_like(slave_area))
    slave = jnp.concatenate(
        [slave_pos + TIME_STEP * slave_vel, slave_vel, area_live[:, None, :]], axis=1
    )
    normals = master_normals(master_tilt)
    master_data = jnp.concatenate(
        [master_cent + TIME_STEP * master_vel, normals, master_vel, master_stiff[:, None, :]],
        axis=1,
    )
    owners = pair_owner[:, 0]
    positions = jnp.arange(block_total, dtype=jnp.int32)
    earlier = (owners[:, None] == owners[None, :]) & (positions[None, :] < positions[:, None])
    slot_index = jnp.sum(earlier.astype(jnp.int32), axis=1)
    target_slot = owners * slot_depth + slot_index
    slot_hit = target_slot[None, :] == jnp.arange(devices * slot_depth, dtype=jnp.int32)[:, None]
    source = jnp.sum(jnp.where(slot_hit, positions[None, :], 0), axis=1)
    filled = jnp.any(slot_hit, axis=1)
    tagged = jnp.concatenate(
        [
            slave,
            jnp.broadcast_to(pair_master.astype(jnp.float32)[:, None, None], (block_total, 1, seg_width)),
        ],
        axis=1,
    )
    outgoing = jnp.where(filled[:, None, None], jnp.take(tagged, source, axis=0), 0.0)
    arrived = lax.all_to_all(
        outgoing.reshape(devices, slot_depth, 8, seg_width),
        ("gx", "gy"),
        split_axis=0,
        concat_axis=0,
        tiled=True,
    )
    item_total = devices * slot_depth
    arrived = arrived.reshape(item_total, 8, seg_width)
    picked = arrived[:, 7, 0].astype(jnp.int32)
    arrived = arrived[:, :7]
    paired = jnp.take(master_data, picked, axis=0)
    forces, reaction = contact_pairs(arrived, paired)
    forces = forces.reshape(item_total, 3, seg_width)
    reaction = reaction.reshape(item_total, seg_width)
    onehot = (picked[:, None] == jnp.arange(master_total, dtype=jnp.int32)[None, :]).astype(
        jnp.float32
    )
    master_sum = jnp.dot(onehot.T, reaction, precision=lax.Precision.HIGHEST)
    master_force = -master_sum[:, None, :] * normals
    master_contact = node_scatter_add(
        master_force.transpose(1, 0, 2).reshape(3, -1), master_node.reshape(-1), node_total
    )
    returned = lax.all_to_all(
        forces.reshape(devices, slot_depth, 3, seg_width),
        ("gx", "gy"),
        split_axis=0,
        concat_axis=0,
        tiled=True,
    )
    slave_force = jnp.take(returned.reshape(item_total, 3, seg_width), target_slot, axis=0)
    contact = master_contact + node_scatter_add(
        slave_force.transpose(1, 0, 2).reshape(3, -1), slave_node.reshape(-1), node_total
    )
    contact_field = contact.reshape(3, layers, row_cells, col_cells)
    velocity_new = velocity + TIME_STEP * (stress + contact_field) / node_mass[None]
    padded_new = padded_2(velocity_new, (("gx", 2), ("gy", 3)), 1)
    node_rate = nodal_rate(padded_new, inside)
    return (velocity_new, node_rate)


def solution(mesh):
    placed = (
        P(None, None, "gx", "gy"),
        P(None, "gx", "gy"),
        P(None, "gx", "gy"),
        P(None, "gx", "gy"),
        P(("gx", "gy"), None, None),
        P(("gx", "gy"), None),
        P(("gx", "gy")),
        P(("gx", "gy"), None),
        P(("gx", "gy"), None),
        P(("gx", "gy")),
        P(("gx", "gy"), None, None),
        P(("gx", "gy"), None, None),
        P(("gx", "gy"), None),
        P(("gx", "gy"), None),
    )
    return jax.shard_map(
        on_device,
        mesh=mesh,
        in_specs=placed,
        out_specs=(P(None, None, "gx", "gy"), P(None, "gx", "gy")),
        check_vma=False,
    )
```

```python
import jax
import jax.numpy as jnp
from jax import lax
from jax.sharding import PartitionSpec as P
from jax.experimental import pallas as pl
from jax.experimental.pallas import tpu as pltpu

LANES = 128
TILE = 4096


def split_pieces(values):
    first = values.astype(jnp.bfloat16)
    rest = values - first.astype(jnp.float32)
    second = rest.astype(jnp.bfloat16)
    third = (rest - second.astype(jnp.float32)).astype(jnp.bfloat16)
    return (first, second, third)


def gather_kernel(index_ref, table_ref, out_ref):
    node = index_ref[...]
    width = node.shape[1]
    high_count = table_ref.shape[1]
    channels = out_ref.shape[0]
    onehot = (
        lax.broadcasted_iota(jnp.int32, (high_count, width), 0) == (node >> 7)
    ).astype(jnp.bfloat16)
    gathered = None
    for piece in split_pieces(table_ref[...])[:2]:
        part = jnp.dot(piece, onehot, preferred_element_type=jnp.float32)
        gathered = part if gathered is None else gathered + part
    low_hit = lax.broadcasted_iota(jnp.int32, (LANES, width), 0) == (node & (LANES - 1))
    for c in range(channels):
        block = gathered[c * LANES : (c + 1) * LANES]
        out_ref[c : c + 1, :] = jnp.sum(jnp.where(low_hit, block, 0.0), axis=0, keepdims=True)


def scatter_kernel(index_ref, force_ref, out_ref):
    @pl.when(pl.program_id(0) == 0)
    def _():
        out_ref[...] = jnp.zeros_like(out_ref)

    node = index_ref[...]
    width = node.shape[1]
    high_count = out_ref.shape[1]
    channels = force_ref.shape[0]
    onehot = (
        lax.broadcasted_iota(jnp.int32, (high_count, width), 0) == (node >> 7)
    ).astype(jnp.bfloat16)
    low_hit = lax.broadcasted_iota(jnp.int32, (LANES, width), 0) == (node & (LANES - 1))
    total = None
    for piece in split_pieces(force_ref[...])[:2]:
        spread = jnp.concatenate(
            [jnp.where(low_hit, piece[c : c + 1, :], jnp.zeros_like(piece[c : c + 1, :])) for c in range(channels)],
            axis=0,
        )
        part = lax.dot_general(
            spread, onehot, (((1,), (1,)), ((), ())), preferred_element_type=jnp.float32
        )
        total = part if total is None else total + part
    out_ref[...] += total


def node_gather(field, nodes):
    channels, node_total = field.shape
    high_count = node_total // LANES
    table = field.reshape(channels, high_count, LANES).transpose(0, 2, 1).reshape(
        channels * LANES, high_count
    )
    count = nodes.shape[0]
    padded_count = -(-count // TILE) * TILE
    nodes = jnp.pad(nodes, (0, padded_count - count))
    return pl.pallas_call(
        gather_kernel,
        grid=(padded_count // TILE,),
        in_specs=[
            pl.BlockSpec((1, TILE), lambda i: (0, i)),
            pl.BlockSpec((channels * LANES, high_count), lambda i: (0, 0)),
        ],
        out_specs=pl.BlockSpec((channels, TILE), lambda i: (0, i)),
        out_shape=jax.ShapeDtypeStruct((channels, padded_count), jnp.float32),
    )(nodes.reshape(1, padded_count), table)[:, :count]


def node_scatter_add(forces, nodes, node_total):
    channels, count = forces.shape
    high_count = node_total // LANES
    padded_count = -(-count // TILE) * TILE
    nodes = jnp.pad(nodes, (0, padded_count - count))
    forces = jnp.pad(forces, ((0, 0), (0, padded_count - count)))
    summed = pl.pallas_call(
        scatter_kernel,
        grid=(padded_count // TILE,),
        in_specs=[
            pl.BlockSpec((1, TILE), lambda i: (0, i)),
            pl.BlockSpec((channels, TILE), lambda i: (0, i)),
        ],
        out_specs=pl.BlockSpec((channels * LANES, high_count), lambda i: (0, 0)),
        out_shape=jax.ShapeDtypeStruct((channels * LANES, high_count), jnp.float32),
    )(nodes.reshape(1, padded_count), forces)
    return summed.reshape(channels, LANES, high_count).transpose(0, 2, 1).reshape(channels, node_total)


TIME_STEP = 0.25
VISCOUS = 0.5
SOFT_GAP = 0.2
REACH_SQ = 1.0
DAMPING = 0.5


def padded_2(block, sides, width):
    for axis, dim in sides:
        count = lax.axis_size(axis)
        forward = [(i, i + 1) for i in range(count - 1)]
        backward = [(target, source) for source, target in forward]
        low = lax.ppermute(
            lax.index_in_dim(block, block.shape[dim] - 1, axis=dim, keepdims=False), axis, forward
        )
        high = lax.ppermute(lax.index_in_dim(block, 0, axis=dim, keepdims=False), axis, backward)
        block = jnp.concatenate(
            [jnp.expand_dims(low, dim), block, jnp.expand_dims(high, dim)], axis=dim
        )
    return block


def pair_mean(values, along):
    length = values.shape[along]
    return 0.5 * (
        lax.slice_in_dim(values, 0, length - 1, axis=along)
        + lax.slice_in_dim(values, 1, length, axis=along)
    )


def pair_diff(values, along):
    length = values.shape[along]
    return lax.slice_in_dim(values, 1, length, axis=along) - lax.slice_in_dim(
        values, 0, length - 1, axis=along
    )


def pair_prod(values, along):
    length = values.shape[along]
    return lax.slice_in_dim(values, 0, length - 1, axis=along) * lax.slice_in_dim(
        values, 1, length, axis=along
    )


def corner_mean(values):
    return pair_mean(pair_mean(pair_mean(values, 0), 1), 2)


def zone_rate(vel):
    rate_x = pair_diff(pair_mean(pair_mean(vel[0], 0), 2), 1)
    rate_y = pair_diff(pair_mean(pair_mean(vel[1], 0), 1), 2)
    rate_z = pair_diff(pair_mean(pair_mean(vel[2], 1), 2), 0)
    return rate_x + rate_y + rate_z


def stress_forces(padded):
    inside = pair_prod(pair_prod(pair_prod(padded[5], 0), 1), 2)
    strain = TIME_STEP * zone_rate(padded[0:3])
    pressure = inside * (
        corner_mean(padded[4]) + corner_mean(padded[3]) * (VISCOUS * strain * strain - strain)
    )
    framed = jnp.pad(pressure, ((1, 1), (0, 0), (0, 0)))
    force_x = -pair_diff(pair_mean(pair_mean(framed, 0), 2), 1)
    force_y = -pair_diff(pair_mean(pair_mean(framed, 0), 1), 2)
    force_z = -pair_diff(pair_mean(pair_mean(framed, 1), 2), 0)
    return (jnp.stack([force_x, force_y, force_z], axis=0), inside)


def nodal_rate(padded_vel, inside):
    rate = inside * zone_rate(padded_vel)
    framed = jnp.pad(rate, ((1, 1), (0, 0), (0, 0)))
    return pair_mean(pair_mean(pair_mean(framed, 0), 1), 2)


def contact_pairs(slave, master):
    delta_x = slave[:, 0, None, :] - master[:, 0, :, None]
    delta_y = slave[:, 1, None, :] - master[:, 1, :, None]
    delta_z = slave[:, 2, None, :] - master[:, 2, :, None]
    normal_x = master[:, 3, :, None]
    normal_y = master[:, 4, :, None]
    normal_z = master[:, 5, :, None]
    dist_sq = delta_x * delta_x + delta_y * delta_y + delta_z * delta_z
    gap_normal = normal_x * delta_x + normal_y * delta_y + normal_z * delta_z
    master_along = (
        master[:, 3] * master[:, 6] + master[:, 4] * master[:, 7] + master[:, 5] * master[:, 8]
    )
    closing = (
        normal_x * slave[:, 3, None, :]
        + normal_y * slave[:, 4, None, :]
        + normal_z * slave[:, 5, None, :]
    ) - master_along[:, :, None]
    weight = jnp.exp(-dist_sq / REACH_SQ)
    soft = gap_normal * (-1.0 / SOFT_GAP)
    depth_soft = SOFT_GAP * (jnp.maximum(soft, 0.0) + jnp.log1p(jnp.exp(-jnp.abs(soft))))
    push_force = (
        slave[:, 6, None, :]
        * master[:, 9, :, None]
        * weight
        * depth_soft
        * (1.0 + DAMPING * jnp.tanh(-closing))
    )
    slave_force = jnp.stack(
        [
            jnp.sum(push_force * normal_x, axis=1),
            jnp.sum(push_force * normal_y, axis=1),
            jnp.sum(push_force * normal_z, axis=1),
        ],
        axis=1,
    )
    reaction = jnp.sum(push_force, axis=2)
    return (slave_force, reaction)


def master_normals(master_tilt):
    scale = lax.rsqrt(
        1.0 + master_tilt[:, 0] * master_tilt[:, 0] + master_tilt[:, 1] * master_tilt[:, 1]
    )
    return jnp.stack([master_tilt[:, 0] * scale, master_tilt[:, 1] * scale, scale], axis=1)


def on_device(
    velocity,
    bulk,
    prestress,
    node_mass,
    slave_pos,
    slave_area,
    seg_count,
    slave_node,
    pair_owner,
    pair_master,
    master_cent,
    master_tilt,
    master_stiff,
    master_node,
):
    count_gx = lax.axis_size("gx")
    count_gy = lax.axis_size("gy")
    devices = count_gx * count_gy
    layers, row_cells, col_cells = bulk.shape
    node_total = layers * row_cells * col_cells
    block_total, _, seg_width = slave_pos.shape
    master_total = master_cent.shape[0]
    slot_depth = (block_total + devices - 1) // devices + 1
    stacked = jnp.concatenate(
        [velocity, bulk[None], prestress[None], jnp.ones_like(bulk)[None]], axis=0
    )
    padded = padded_2(stacked, (("gx", 2), ("gy", 3)), 1)
    stress, inside = stress_forces(padded)
    vel_flat = velocity.reshape(3, node_total)
    slave_count = block_total * seg_width
    slave_vel = (
        node_gather(vel_flat, slave_node.reshape(-1))
        .reshape(3, block_total, seg_width)
        .transpose(1, 0, 2)
    )
    master_vel = (
        node_gather(vel_flat, master_node.reshape(-1))
        .reshape(3, master_total, seg_width)
        .transpose(1, 0, 2)
    )
    live_mask = jnp.arange(seg_width, dtype=jnp.int32)[None, :] < seg_count[:, None]
    area_live = jnp.where(live_mask, slave_area, jnp.zeros_like(slave_area))
    slave = jnp.concatenate(
        [slave_pos + TIME_STEP * slave_vel, slave_vel, area_live[:, None, :]], axis=1
    )
    normals = master_normals(master_tilt)
    master_data = jnp.concatenate(
        [master_cent + TIME_STEP * master_vel, normals, master_vel, master_stiff[:, None, :]],
        axis=1,
    )
    owners = pair_owner[:, 0]
    positions = jnp.arange(block_total, dtype=jnp.int32)
    earlier = (owners[:, None] == owners[None, :]) & (positions[None, :] < positions[:, None])
    slot_index = jnp.sum(earlier.astype(jnp.int32), axis=1)
    target_slot = owners * slot_depth + slot_index
    slot_hit = target_slot[None, :] == jnp.arange(devices * slot_depth, dtype=jnp.int32)[:, None]
    source = jnp.sum(jnp.where(slot_hit, positions[None, :], 0), axis=1)
    filled = jnp.any(slot_hit, axis=1)
    tagged = jnp.concatenate(
        [
            slave,
            jnp.broadcast_to(pair_master.astype(jnp.float32)[:, None, None], (block_total, 1, seg_width)),
        ],
        axis=1,
    )
    outgoing = jnp.where(filled[:, None, None], jnp.take(tagged, source, axis=0), 0.0)
    arrived = lax.all_to_all(
        outgoing.reshape(devices, slot_depth, 8, seg_width),
        ("gx", "gy"),
        split_axis=0,
        concat_axis=0,
        tiled=True,
    )
    item_total = devices * slot_depth
    arrived = arrived.reshape(item_total, 8, seg_width)
    picked = arrived[:, 7, 0].astype(jnp.int32)
    arrived = arrived[:, :7]
    paired = jnp.take(master_data, picked, axis=0)
    forces, reaction = contact_pairs(arrived, paired)
    forces = forces.reshape(item_total, 3, seg_width)
    reaction = reaction.reshape(item_total, seg_width)
    onehot = (picked[:, None] == jnp.arange(master_total, dtype=jnp.int32)[None, :]).astype(
        jnp.float32
    )
    master_sum = jnp.dot(onehot.T, reaction, precision=lax.Precision.HIGHEST)
    master_force = -master_sum[:, None, :] * normals
    master_contact = node_scatter_add(
        master_force.transpose(1, 0, 2).reshape(3, -1), master_node.reshape(-1), node_total
    )
    returned = lax.all_to_all(
        forces.reshape(devices, slot_depth, 3, seg_width),
        ("gx", "gy"),
        split_axis=0,
        concat_axis=0,
        tiled=True,
    )
    slave_force = jnp.take(returned.reshape(item_total, 3, seg_width), target_slot, axis=0)
    contact = master_contact + node_scatter_add(
        slave_force.transpose(1, 0, 2).reshape(3, -1), slave_node.reshape(-1), node_total
    )
    contact_field = contact.reshape(3, layers, row_cells, col_cells)
    velocity_new = velocity + TIME_STEP * (stress + contact_field) / node_mass[None]
    padded_new = padded_2(velocity_new, (("gx", 2), ("gy", 3)), 1)
    node_rate = nodal_rate(padded_new, inside)
    return (velocity_new, node_rate)


def solution(mesh):
    placed = (
        P(None, None, "gx", "gy"),
        P(None, "gx", "gy"),
        P(None, "gx", "gy"),
        P(None, "gx", "gy"),
        P(("gx", "gy"), None, None),
        P(("gx", "gy"), None),
        P(("gx", "gy")),
        P(("gx", "gy"), None),
        P(("gx", "gy"), None),
        P(("gx", "gy")),
        P(("gx", "gy"), None, None),
        P(("gx", "gy"), None, None),
        P(("gx", "gy"), None),
        P(("gx", "gy"), None),
    )
    return jax.shard_map(
        on_device,
        mesh=mesh,
        in_specs=placed,
        out_specs=(P(None, None, "gx", "gy"), P(None, "gx", "gy")),
        check_vma=False,
    )
```

```python
import jax
import jax.numpy as jnp
from jax import lax
from jax.sharding import PartitionSpec as P
from jax.experimental import pallas as pl
from jax.experimental.pallas import tpu as pltpu

LANES = 128
TILE = 4096


def split_pieces(values):
    first = values.astype(jnp.bfloat16)
    rest = values - first.astype(jnp.float32)
    second = rest.astype(jnp.bfloat16)
    third = (rest - second.astype(jnp.float32)).astype(jnp.bfloat16)
    return (first, second, third)


def gather_kernel(index_ref, table_ref, out_ref):
    node = index_ref[...]
    width = node.shape[1]
    high_count = table_ref.shape[1]
    channels = out_ref.shape[0]
    onehot = (
        lax.broadcasted_iota(jnp.int32, (high_count, width), 0) == (node >> 7)
    ).astype(jnp.bfloat16)
    gathered = None
    for piece in split_pieces(table_ref[...])[:2]:
        part = jnp.dot(piece, onehot, preferred_element_type=jnp.float32)
        gathered = part if gathered is None else gathered + part
    low_hit = lax.broadcasted_iota(jnp.int32, (LANES, width), 0) == (node & (LANES - 1))
    for c in range(channels):
        block = gathered[c * LANES : (c + 1) * LANES]
        out_ref[c : c + 1, :] = jnp.sum(jnp.where(low_hit, block, 0.0), axis=0, keepdims=True)


def scatter_kernel(index_ref, force_ref, out_ref):
    @pl.when(pl.program_id(0) == 0)
    def _():
        out_ref[...] = jnp.zeros_like(out_ref)

    node = index_ref[...]
    width = node.shape[1]
    high_count = out_ref.shape[1]
    channels = force_ref.shape[0]
    onehot = (
        lax.broadcasted_iota(jnp.int32, (high_count, width), 0) == (node >> 7)
    ).astype(jnp.bfloat16)
    low_hit = lax.broadcasted_iota(jnp.int32, (LANES, width), 0) == (node & (LANES - 1))
    total = None
    for piece in split_pieces(force_ref[...])[:2]:
        spread = jnp.concatenate(
            [jnp.where(low_hit, piece[c : c + 1, :], jnp.zeros_like(piece[c : c + 1, :])) for c in range(channels)],
            axis=0,
        )
        part = lax.dot_general(
            spread, onehot, (((1,), (1,)), ((), ())), preferred_element_type=jnp.float32
        )
        total = part if total is None else total + part
    out_ref[...] += total


def node_gather(field, nodes):
    channels, node_total = field.shape
    high_count = node_total // LANES
    table = field.reshape(channels, high_count, LANES).transpose(0, 2, 1).reshape(
        channels * LANES, high_count
    )
    count = nodes.shape[0]
    padded_count = -(-count // TILE) * TILE
    nodes = jnp.pad(nodes, (0, padded_count - count))
    return pl.pallas_call(
        gather_kernel,
        grid=(padded_count // TILE,),
        in_specs=[
            pl.BlockSpec((1, TILE), lambda i: (0, i)),
            pl.BlockSpec((channels * LANES, high_count), lambda i: (0, 0)),
        ],
        out_specs=pl.BlockSpec((channels, TILE), lambda i: (0, i)),
        out_shape=jax.ShapeDtypeStruct((channels, padded_count), jnp.float32),
    )(nodes.reshape(1, padded_count), table)[:, :count]


def node_scatter_add(forces, nodes, node_total):
    channels, count = forces.shape
    high_count = node_total // LANES
    padded_count = -(-count // TILE) * TILE
    nodes = jnp.pad(nodes, (0, padded_count - count))
    forces = jnp.pad(forces, ((0, 0), (0, padded_count - count)))
    summed = pl.pallas_call(
        scatter_kernel,
        grid=(padded_count // TILE,),
        in_specs=[
            pl.BlockSpec((1, TILE), lambda i: (0, i)),
            pl.BlockSpec((channels, TILE), lambda i: (0, i)),
        ],
        out_specs=pl.BlockSpec((channels * LANES, high_count), lambda i: (0, 0)),
        out_shape=jax.ShapeDtypeStruct((channels * LANES, high_count), jnp.float32),
    )(nodes.reshape(1, padded_count), forces)
    return summed.reshape(channels, LANES, high_count).transpose(0, 2, 1).reshape(channels, node_total)


TIME_STEP = 0.25
VISCOUS = 0.5
SOFT_GAP = 0.2
REACH_SQ = 1.0
DAMPING = 0.5


def padded_2(block, sides, width):
    for axis, dim in sides:
        count = lax.axis_size(axis)
        forward = [(i, i + 1) for i in range(count - 1)]
        backward = [(target, source) for source, target in forward]
        low = lax.ppermute(
            lax.index_in_dim(block, block.shape[dim] - 1, axis=dim, keepdims=False), axis, forward
        )
        high = lax.ppermute(lax.index_in_dim(block, 0, axis=dim, keepdims=False), axis, backward)
        block = jnp.concatenate(
            [jnp.expand_dims(low, dim), block, jnp.expand_dims(high, dim)], axis=dim
        )
    return block


def pair_mean(values, along):
    length = values.shape[along]
    return 0.5 * (
        lax.slice_in_dim(values, 0, length - 1, axis=along)
        + lax.slice_in_dim(values, 1, length, axis=along)
    )


def pair_diff(values, along):
    length = values.shape[along]
    return lax.slice_in_dim(values, 1, length, axis=along) - lax.slice_in_dim(
        values, 0, length - 1, axis=along
    )


def pair_prod(values, along):
    length = values.shape[along]
    return lax.slice_in_dim(values, 0, length - 1, axis=along) * lax.slice_in_dim(
        values, 1, length, axis=along
    )


def corner_mean(values):
    return pair_mean(pair_mean(pair_mean(values, 0), 1), 2)


def zone_rate(vel):
    rate_x = pair_diff(pair_mean(pair_mean(vel[0], 0), 2), 1)
    rate_y = pair_diff(pair_mean(pair_mean(vel[1], 0), 1), 2)
    rate_z = pair_diff(pair_mean(pair_mean(vel[2], 1), 2), 0)
    return rate_x + rate_y + rate_z


def stress_forces(padded):
    inside = pair_prod(pair_prod(pair_prod(padded[5], 0), 1), 2)
    strain = TIME_STEP * zone_rate(padded[0:3])
    pressure = inside * (
        corner_mean(padded[4]) + corner_mean(padded[3]) * (VISCOUS * strain * strain - strain)
    )
    framed = jnp.pad(pressure, ((1, 1), (0, 0), (0, 0)))
    force_x = -pair_diff(pair_mean(pair_mean(framed, 0), 2), 1)
    force_y = -pair_diff(pair_mean(pair_mean(framed, 0), 1), 2)
    force_z = -pair_diff(pair_mean(pair_mean(framed, 1), 2), 0)
    return (jnp.stack([force_x, force_y, force_z], axis=0), inside)


def nodal_rate(padded_vel, inside):
    rate = inside * zone_rate(padded_vel)
    framed = jnp.pad(rate, ((1, 1), (0, 0), (0, 0)))
    return pair_mean(pair_mean(pair_mean(framed, 0), 1), 2)


def contact_pairs(slave, master):
    delta_x = slave[:, 0, None, :] - master[:, 0, :, None]
    delta_y = slave[:, 1, None, :] - master[:, 1, :, None]
    delta_z = slave[:, 2, None, :] - master[:, 2, :, None]
    normal_x = master[:, 3, :, None]
    normal_y = master[:, 4, :, None]
    normal_z = master[:, 5, :, None]
    dist_sq = delta_x * delta_x + delta_y * delta_y + delta_z * delta_z
    gap_normal = normal_x * delta_x + normal_y * delta_y + normal_z * delta_z
    master_along = (
        master[:, 3] * master[:, 6] + master[:, 4] * master[:, 7] + master[:, 5] * master[:, 8]
    )
    closing = (
        normal_x * slave[:, 3, None, :]
        + normal_y * slave[:, 4, None, :]
        + normal_z * slave[:, 5, None, :]
    ) - master_along[:, :, None]
    weight = jnp.exp(-dist_sq / REACH_SQ)
    soft = gap_normal * (-1.0 / SOFT_GAP)
    depth_soft = SOFT_GAP * (jnp.maximum(soft, 0.0) + jnp.log1p(jnp.exp(-jnp.abs(soft))))
    push_force = (
        slave[:, 6, None, :]
        * master[:, 9, :, None]
        * weight
        * depth_soft
        * (1.0 + DAMPING * jnp.tanh(-closing))
    )
    slave_force = jnp.stack(
        [
            jnp.sum(push_force * normal_x, axis=1),
            jnp.sum(push_force * normal_y, axis=1),
            jnp.sum(push_force * normal_z, axis=1),
        ],
        axis=1,
    )
    reaction = jnp.sum(push_force, axis=2)
    return (slave_force, reaction)


def master_normals(master_tilt):
    scale = lax.rsqrt(
        1.0 + master_tilt[:, 0] * master_tilt[:, 0] + master_tilt[:, 1] * master_tilt[:, 1]
    )
    return jnp.stack([master_tilt[:, 0] * scale, master_tilt[:, 1] * scale, scale], axis=1)


def on_device(
    velocity,
    bulk,
    prestress,
    node_mass,
    slave_pos,
    slave_area,
    seg_count,
    slave_node,
    pair_owner,
    pair_master,
    master_cent,
    master_tilt,
    master_stiff,
    master_node,
):
    count_gx = lax.axis_size("gx")
    count_gy = lax.axis_size("gy")
    devices = count_gx * count_gy
    layers, row_cells, col_cells = bulk.shape
    node_total = layers * row_cells * col_cells
    block_total, _, seg_width = slave_pos.shape
    master_total = master_cent.shape[0]
    slot_depth = (block_total + devices - 1) // devices + 1
    stacked = jnp.concatenate(
        [velocity, bulk[None], prestress[None], jnp.ones_like(bulk)[None]], axis=0
    )
    padded = padded_2(stacked, (("gx", 2), ("gy", 3)), 1)
    stress, inside = stress_forces(padded)
    vel_flat = velocity.reshape(3, node_total)
    slave_count = block_total * seg_width
    slave_vel = (
        node_gather(vel_flat, slave_node.reshape(-1))
        .reshape(3, block_total, seg_width)
        .transpose(1, 0, 2)
    )
    master_vel = (
        node_gather(vel_flat, master_node.reshape(-1))
        .reshape(3, master_total, seg_width)
        .transpose(1, 0, 2)
    )
    live_mask = jnp.arange(seg_width, dtype=jnp.int32)[None, :] < seg_count[:, None]
    area_live = jnp.where(live_mask, slave_area, jnp.zeros_like(slave_area))
    slave = jnp.concatenate(
        [slave_pos + TIME_STEP * slave_vel, slave_vel, area_live[:, None, :]], axis=1
    )
    normals = master_normals(master_tilt)
    master_data = jnp.concatenate(
        [master_cent + TIME_STEP * master_vel, normals, master_vel, master_stiff[:, None, :]],
        axis=1,
    )
    owners = pair_owner[:, 0]
    positions = jnp.arange(block_total, dtype=jnp.int32)
    earlier = (owners[:, None] == owners[None, :]) & (positions[None, :] < positions[:, None])
    slot_index = jnp.sum(earlier.astype(jnp.int32), axis=1)
    target_slot = owners * slot_depth + slot_index
    slot_hit = target_slot[None, :] == jnp.arange(devices * slot_depth, dtype=jnp.int32)[:, None]
    source = jnp.sum(jnp.where(slot_hit, positions[None, :], 0), axis=1)
    filled = jnp.any(slot_hit, axis=1)
    tagged = jnp.concatenate(
        [
            slave,
            jnp.broadcast_to(pair_master.astype(jnp.float32)[:, None, None], (block_total, 1, seg_width)),
        ],
        axis=1,
    )
    outgoing = jnp.where(filled[:, None, None], jnp.take(tagged, source, axis=0), 0.0)
    arrived = lax.all_to_all(
        outgoing.reshape(devices, slot_depth, 8, seg_width),
        ("gx", "gy"),
        split_axis=0,
        concat_axis=0,
        tiled=True,
    )
    item_total = devices * slot_depth
    arrived = arrived.reshape(item_total, 8, seg_width)
    picked = jnp.max(arrived[:, 7, :], axis=1).astype(jnp.int32)
    arrived = arrived[:, :7]
    paired = jnp.take(master_data, picked, axis=0)
    forces, reaction = contact_pairs(arrived, paired)
    forces = forces.reshape(item_total, 3, seg_width)
    reaction = reaction.reshape(item_total, seg_width)
    onehot = (picked[:, None] == jnp.arange(master_total, dtype=jnp.int32)[None, :]).astype(
        jnp.float32
    )
    master_sum = jnp.dot(onehot.T, reaction, precision=lax.Precision.HIGHEST)
    master_force = -master_sum[:, None, :] * normals
    master_contact = node_scatter_add(
        master_force.transpose(1, 0, 2).reshape(3, -1), master_node.reshape(-1), node_total
    )
    returned = lax.all_to_all(
        forces.reshape(devices, slot_depth, 3, seg_width),
        ("gx", "gy"),
        split_axis=0,
        concat_axis=0,
        tiled=True,
    )
    slave_force = jnp.take(returned.reshape(item_total, 3, seg_width), target_slot, axis=0)
    contact = master_contact + node_scatter_add(
        slave_force.transpose(1, 0, 2).reshape(3, -1), slave_node.reshape(-1), node_total
    )
    contact_field = contact.reshape(3, layers, row_cells, col_cells)
    velocity_new = velocity + TIME_STEP * (stress + contact_field) / node_mass[None]
    padded_new = padded_2(velocity_new, (("gx", 2), ("gy", 3)), 1)
    node_rate = nodal_rate(padded_new, inside)
    return (velocity_new, node_rate)


def solution(mesh):
    placed = (
        P(None, None, "gx", "gy"),
        P(None, "gx", "gy"),
        P(None, "gx", "gy"),
        P(None, "gx", "gy"),
        P(("gx", "gy"), None, None),
        P(("gx", "gy"), None),
        P(("gx", "gy")),
        P(("gx", "gy"), None),
        P(("gx", "gy"), None),
        P(("gx", "gy")),
        P(("gx", "gy"), None, None),
        P(("gx", "gy"), None, None),
        P(("gx", "gy"), None),
        P(("gx", "gy"), None),
    )
    return jax.shard_map(
        on_device,
        mesh=mesh,
        in_specs=placed,
        out_specs=(P(None, None, "gx", "gy"), P(None, "gx", "gy")),
        check_vma=False,
    )
```

```python
import jax
import jax.numpy as jnp
from jax import lax
from jax.sharding import PartitionSpec as P
from jax.experimental import pallas as pl
from jax.experimental.pallas import tpu as pltpu

LANES = 128
TILE = 4096


def split_pieces(values):
    first = values.astype(jnp.bfloat16)
    rest = values - first.astype(jnp.float32)
    second = rest.astype(jnp.bfloat16)
    third = (rest - second.astype(jnp.float32)).astype(jnp.bfloat16)
    return (first, second, third)


def gather_kernel(index_ref, table_ref, out_ref):
    node = index_ref[...]
    width = node.shape[1]
    high_count = table_ref.shape[1]
    channels = out_ref.shape[0]
    onehot = (
        lax.broadcasted_iota(jnp.int32, (high_count, width), 0) == (node >> 7)
    ).astype(jnp.bfloat16)
    gathered = None
    for piece in split_pieces(table_ref[...])[:2]:
        part = jnp.dot(piece, onehot, preferred_element_type=jnp.float32)
        gathered = part if gathered is None else gathered + part
    low_hit = lax.broadcasted_iota(jnp.int32, (LANES, width), 0) == (node & (LANES - 1))
    for c in range(channels):
        block = gathered[c * LANES : (c + 1) * LANES]
        out_ref[c : c + 1, :] = jnp.sum(jnp.where(low_hit, block, 0.0), axis=0, keepdims=True)


def scatter_kernel(index_ref, force_ref, init_ref, out_ref):
    @pl.when(pl.program_id(0) == 0)
    def _():
        out_ref[...] = init_ref[...]

    node = index_ref[...]
    width = node.shape[1]
    high_count = out_ref.shape[1]
    channels = force_ref.shape[0]
    onehot = (
        lax.broadcasted_iota(jnp.int32, (high_count, width), 0) == (node >> 7)
    ).astype(jnp.bfloat16)
    low_hit = lax.broadcasted_iota(jnp.int32, (LANES, width), 0) == (node & (LANES - 1))
    total = None
    for piece in split_pieces(force_ref[...])[:2]:
        spread = jnp.concatenate(
            [jnp.where(low_hit, piece[c : c + 1, :], jnp.zeros_like(piece[c : c + 1, :])) for c in range(channels)],
            axis=0,
        )
        part = lax.dot_general(
            spread, onehot, (((1,), (1,)), ((), ())), preferred_element_type=jnp.float32
        )
        total = part if total is None else total + part
    out_ref[...] += total


def node_gather(field, nodes):
    channels, node_total = field.shape
    high_count = node_total // LANES
    table = field.reshape(channels, high_count, LANES).transpose(0, 2, 1).reshape(
        channels * LANES, high_count
    )
    count = nodes.shape[0]
    padded_count = -(-count // TILE) * TILE
    nodes = jnp.pad(nodes, (0, padded_count - count))
    return pl.pallas_call(
        gather_kernel,
        grid=(padded_count // TILE,),
        in_specs=[
            pl.BlockSpec((1, TILE), lambda i: (0, i)),
            pl.BlockSpec((channels * LANES, high_count), lambda i: (0, 0)),
        ],
        out_specs=pl.BlockSpec((channels, TILE), lambda i: (0, i)),
        out_shape=jax.ShapeDtypeStruct((channels, padded_count), jnp.float32),
    )(nodes.reshape(1, padded_count), table)[:, :count]


def node_scatter_add(forces, nodes, start):
    channels, count = forces.shape
    high_count = start.shape[1]
    padded_count = -(-count // TILE) * TILE
    nodes = jnp.pad(nodes, (0, padded_count - count))
    forces = jnp.pad(forces, ((0, 0), (0, padded_count - count)))
    return pl.pallas_call(
        scatter_kernel,
        grid=(padded_count // TILE,),
        in_specs=[
            pl.BlockSpec((1, TILE), lambda i: (0, i)),
            pl.BlockSpec((channels, TILE), lambda i: (0, i)),
            pl.BlockSpec(start.shape, lambda i: (0, 0)),
        ],
        out_specs=pl.BlockSpec(start.shape, lambda i: (0, 0)),
        out_shape=jax.ShapeDtypeStruct(start.shape, jnp.float32),
    )(nodes.reshape(1, padded_count), forces, start)


def sums_to_nodes(summed, channels, node_total):
    high_count = summed.shape[1]
    return summed.reshape(channels, LANES, high_count).transpose(0, 2, 1).reshape(channels, node_total)


TIME_STEP = 0.25
VISCOUS = 0.5
SOFT_GAP = 0.2
REACH_SQ = 1.0
DAMPING = 0.5


def padded_2(block, sides, width):
    for axis, dim in sides:
        count = lax.axis_size(axis)
        forward = [(i, i + 1) for i in range(count - 1)]
        backward = [(target, source) for source, target in forward]
        low = lax.ppermute(
            lax.index_in_dim(block, block.shape[dim] - 1, axis=dim, keepdims=False), axis, forward
        )
        high = lax.ppermute(lax.index_in_dim(block, 0, axis=dim, keepdims=False), axis, backward)
        block = jnp.concatenate(
            [jnp.expand_dims(low, dim), block, jnp.expand_dims(high, dim)], axis=dim
        )
    return block


def pair_mean(values, along):
    length = values.shape[along]
    return 0.5 * (
        lax.slice_in_dim(values, 0, length - 1, axis=along)
        + lax.slice_in_dim(values, 1, length, axis=along)
    )


def pair_diff(values, along):
    length = values.shape[along]
    return lax.slice_in_dim(values, 1, length, axis=along) - lax.slice_in_dim(
        values, 0, length - 1, axis=along
    )


def pair_prod(values, along):
    length = values.shape[along]
    return lax.slice_in_dim(values, 0, length - 1, axis=along) * lax.slice_in_dim(
        values, 1, length, axis=along
    )


def corner_mean(values):
    return pair_mean(pair_mean(pair_mean(values, 0), 1), 2)


def zone_rate(vel):
    rate_x = pair_diff(pair_mean(pair_mean(vel[0], 0), 2), 1)
    rate_y = pair_diff(pair_mean(pair_mean(vel[1], 0), 1), 2)
    rate_z = pair_diff(pair_mean(pair_mean(vel[2], 1), 2), 0)
    return rate_x + rate_y + rate_z


def stress_forces(padded):
    inside = pair_prod(pair_prod(pair_prod(padded[5], 0), 1), 2)
    strain = TIME_STEP * zone_rate(padded[0:3])
    pressure = inside * (
        corner_mean(padded[4]) + corner_mean(padded[3]) * (VISCOUS * strain * strain - strain)
    )
    framed = jnp.pad(pressure, ((1, 1), (0, 0), (0, 0)))
    force_x = -pair_diff(pair_mean(pair_mean(framed, 0), 2), 1)
    force_y = -pair_diff(pair_mean(pair_mean(framed, 0), 1), 2)
    force_z = -pair_diff(pair_mean(pair_mean(framed, 1), 2), 0)
    return (jnp.stack([force_x, force_y, force_z], axis=0), inside)


def nodal_rate(padded_vel, inside):
    rate = inside * zone_rate(padded_vel)
    framed = jnp.pad(rate, ((1, 1), (0, 0), (0, 0)))
    return pair_mean(pair_mean(pair_mean(framed, 0), 1), 2)


def contact_pairs(slave, master):
    delta_x = slave[:, 0, None, :] - master[:, 0, :, None]
    delta_y = slave[:, 1, None, :] - master[:, 1, :, None]
    delta_z = slave[:, 2, None, :] - master[:, 2, :, None]
    normal_x = master[:, 3, :, None]
    normal_y = master[:, 4, :, None]
    normal_z = master[:, 5, :, None]
    dist_sq = delta_x * delta_x + delta_y * delta_y + delta_z * delta_z
    gap_normal = normal_x * delta_x + normal_y * delta_y + normal_z * delta_z
    master_along = (
        master[:, 3] * master[:, 6] + master[:, 4] * master[:, 7] + master[:, 5] * master[:, 8]
    )
    closing = (
        normal_x * slave[:, 3, None, :]
        + normal_y * slave[:, 4, None, :]
        + normal_z * slave[:, 5, None, :]
    ) - master_along[:, :, None]
    weight = jnp.exp(-dist_sq / REACH_SQ)
    soft = gap_normal * (-1.0 / SOFT_GAP)
    depth_soft = SOFT_GAP * (jnp.maximum(soft, 0.0) + jnp.log1p(jnp.exp(-jnp.abs(soft))))
    push_force = (
        slave[:, 6, None, :]
        * master[:, 9, :, None]
        * weight
        * depth_soft
        * (1.0 + DAMPING * jnp.tanh(-closing))
    )
    slave_force = jnp.stack(
        [
            jnp.sum(push_force * normal_x, axis=1),
            jnp.sum(push_force * normal_y, axis=1),
            jnp.sum(push_force * normal_z, axis=1),
        ],
        axis=1,
    )
    reaction = jnp.sum(push_force, axis=2)
    return (slave_force, reaction)


def master_normals(master_tilt):
    scale = lax.rsqrt(
        1.0 + master_tilt[:, 0] * master_tilt[:, 0] + master_tilt[:, 1] * master_tilt[:, 1]
    )
    return jnp.stack([master_tilt[:, 0] * scale, master_tilt[:, 1] * scale, scale], axis=1)


def on_device(
    velocity,
    bulk,
    prestress,
    node_mass,
    slave_pos,
    slave_area,
    seg_count,
    slave_node,
    pair_owner,
    pair_master,
    master_cent,
    master_tilt,
    master_stiff,
    master_node,
):
    count_gx = lax.axis_size("gx")
    count_gy = lax.axis_size("gy")
    devices = count_gx * count_gy
    layers, row_cells, col_cells = bulk.shape
    node_total = layers * row_cells * col_cells
    block_total, _, seg_width = slave_pos.shape
    master_total = master_cent.shape[0]
    slot_depth = (block_total + devices - 1) // devices + 1
    stacked = jnp.concatenate(
        [velocity, bulk[None], prestress[None], jnp.ones_like(bulk)[None]], axis=0
    )
    vel_flat = velocity.reshape(3, node_total)
    slave_count = block_total * seg_width
    slave_vel = (
        node_gather(vel_flat, slave_node.reshape(-1))
        .reshape(3, block_total, seg_width)
        .transpose(1, 0, 2)
    )
    stacked, slave_vel = lax.optimization_barrier((stacked, slave_vel))
    padded = padded_2(stacked, (("gx", 2), ("gy", 3)), 1)
    stress, inside = stress_forces(padded)
    master_vel = (
        node_gather(vel_flat, master_node.reshape(-1))
        .reshape(3, master_total, seg_width)
        .transpose(1, 0, 2)
    )
    live_mask = jnp.arange(seg_width, dtype=jnp.int32)[None, :] < seg_count[:, None]
    area_live = jnp.where(live_mask, slave_area, jnp.zeros_like(slave_area))
    slave = jnp.concatenate(
        [slave_pos + TIME_STEP * slave_vel, slave_vel, area_live[:, None, :]], axis=1
    )
    normals = master_normals(master_tilt)
    master_data = jnp.concatenate(
        [master_cent + TIME_STEP * master_vel, normals, master_vel, master_stiff[:, None, :]],
        axis=1,
    )
    owners = pair_owner[:, 0]
    positions = jnp.arange(block_total, dtype=jnp.int32)
    earlier = (owners[:, None] == owners[None, :]) & (positions[None, :] < positions[:, None])
    slot_index = jnp.sum(earlier.astype(jnp.int32), axis=1)
    target_slot = owners * slot_depth + slot_index
    slot_hit = target_slot[None, :] == jnp.arange(devices * slot_depth, dtype=jnp.int32)[:, None]
    source = jnp.sum(jnp.where(slot_hit, positions[None, :], 0), axis=1)
    filled = jnp.any(slot_hit, axis=1)
    tagged = jnp.concatenate(
        [
            slave,
            jnp.broadcast_to(pair_master.astype(jnp.float32)[:, None, None], (block_total, 1, seg_width)),
        ],
        axis=1,
    )
    outgoing = jnp.where(filled[:, None, None], jnp.take(tagged, source, axis=0), 0.0)
    arrived = lax.all_to_all(
        outgoing.reshape(devices, slot_depth, 8, seg_width),
        ("gx", "gy"),
        split_axis=0,
        concat_axis=0,
        tiled=True,
    )
    item_total = devices * slot_depth
    arrived = arrived.reshape(item_total, 8, seg_width)
    picked = jnp.max(arrived[:, 7, :], axis=1).astype(jnp.int32)
    arrived = arrived[:, :7]
    paired = jnp.take(master_data, picked, axis=0)
    forces, reaction = contact_pairs(arrived, paired)
    forces = forces.reshape(item_total, 3, seg_width)
    reaction = reaction.reshape(item_total, seg_width)
    onehot = (picked[:, None] == jnp.arange(master_total, dtype=jnp.int32)[None, :]).astype(
        jnp.float32
    )
    master_sum = jnp.dot(onehot.T, reaction, precision=lax.Precision.HIGHEST)
    master_force = -master_sum[:, None, :] * normals
    master_contact = node_scatter_add(
        master_force.transpose(1, 0, 2).reshape(3, -1),
        master_node.reshape(-1),
        jnp.zeros((3 * LANES, node_total // LANES), jnp.float32),
    )
    returned = lax.all_to_all(
        forces.reshape(devices, slot_depth, 3, seg_width),
        ("gx", "gy"),
        split_axis=0,
        concat_axis=0,
        tiled=True,
    )
    slave_force = jnp.take(returned.reshape(item_total, 3, seg_width), target_slot, axis=0)
    contact = sums_to_nodes(
        node_scatter_add(
            slave_force.transpose(1, 0, 2).reshape(3, -1), slave_node.reshape(-1), master_contact
        ),
        3,
        node_total,
    )
    contact_field = contact.reshape(3, layers, row_cells, col_cells)
    velocity_new = velocity + TIME_STEP * (stress + contact_field) / node_mass[None]
    padded_new = padded_2(velocity_new, (("gx", 2), ("gy", 3)), 1)
    node_rate = nodal_rate(padded_new, inside)
    return (velocity_new, node_rate)


def solution(mesh):
    placed = (
        P(None, None, "gx", "gy"),
        P(None, "gx", "gy"),
        P(None, "gx", "gy"),
        P(None, "gx", "gy"),
        P(("gx", "gy"), None, None),
        P(("gx", "gy"), None),
        P(("gx", "gy")),
        P(("gx", "gy"), None),
        P(("gx", "gy"), None),
        P(("gx", "gy")),
        P(("gx", "gy"), None, None),
        P(("gx", "gy"), None, None),
        P(("gx", "gy"), None),
        P(("gx", "gy"), None),
    )
    return jax.shard_map(
        on_device,
        mesh=mesh,
        in_specs=placed,
        out_specs=(P(None, None, "gx", "gy"), P(None, "gx", "gy")),
        check_vma=False,
    )
```

```python
import jax
import jax.numpy as jnp
from jax import lax
from jax.sharding import PartitionSpec as P
from jax.experimental import pallas as pl
from jax.experimental.pallas import tpu as pltpu

LANES = 128
TILE = 4096


def split_pieces(values):
    first = values.astype(jnp.bfloat16)
    rest = values - first.astype(jnp.float32)
    second = rest.astype(jnp.bfloat16)
    third = (rest - second.astype(jnp.float32)).astype(jnp.bfloat16)
    return (first, second, third)


def block_swap(values):
    channels = values.shape[0] // LANES if values.ndim == 2 else values.shape[0]
    if values.ndim == 3:
        return jnp.concatenate(
            [
                jnp.concatenate([values[c, :, :LANES].T, values[c, :, LANES:].T], axis=1)
                for c in range(channels)
            ],
            axis=0,
        )
    return jnp.stack(
        [
            jnp.concatenate(
                [
                    values[c * LANES : (c + 1) * LANES, :LANES].T,
                    values[c * LANES : (c + 1) * LANES, LANES:].T,
                ],
                axis=1,
            )
            for c in range(channels)
        ]
    )


def node_parts(node):
    high = ((node & (2 * LANES - 1)) >> 7) * LANES + (node >> 8)
    return high, node & (LANES - 1)


def gather_kernel(index_ref, field_ref, out_ref):
    node = index_ref[...]
    width = node.shape[1]
    table = block_swap(field_ref[...])
    high_count = table.shape[1]
    channels = out_ref.shape[0]
    high, low = node_parts(node)
    onehot = (
        lax.broadcasted_iota(jnp.int32, (high_count, width), 0) == high
    ).astype(jnp.bfloat16)
    gathered = None
    for piece in split_pieces(table)[:2]:
        part = jnp.dot(piece, onehot, preferred_element_type=jnp.float32)
        gathered = part if gathered is None else gathered + part
    low_hit = lax.broadcasted_iota(jnp.int32, (LANES, width), 0) == low
    for c in range(channels):
        block = gathered[c * LANES : (c + 1) * LANES]
        out_ref[c : c + 1, :] = jnp.sum(jnp.where(low_hit, block, 0.0), axis=0, keepdims=True)


def scatter_kernel(index_ref, force_ref, init_ref, out_ref, acc_ref):
    @pl.when(pl.program_id(0) == 0)
    def _():
        acc_ref[...] = block_swap(init_ref[...])

    node = index_ref[...]
    width = node.shape[1]
    high_count = acc_ref.shape[1]
    channels = force_ref.shape[0]
    high, low = node_parts(node)
    onehot = (
        lax.broadcasted_iota(jnp.int32, (high_count, width), 0) == high
    ).astype(jnp.bfloat16)
    low_hit = lax.broadcasted_iota(jnp.int32, (LANES, width), 0) == low
    total = None
    for piece in split_pieces(force_ref[...])[:2]:
        spread = jnp.concatenate(
            [jnp.where(low_hit, piece[c : c + 1, :], jnp.zeros_like(piece[c : c + 1, :])) for c in range(channels)],
            axis=0,
        )
        part = lax.dot_general(
            spread, onehot, (((1,), (1,)), ((), ())), preferred_element_type=jnp.float32
        )
        total = part if total is None else total + part
    acc_ref[...] += total

    @pl.when(pl.program_id(0) == pl.num_programs(0) - 1)
    def _():
        out_ref[...] = block_swap(acc_ref[...])


def node_gather(field, nodes):
    count = nodes.shape[0]
    padded_count = -(-count // TILE) * TILE
    nodes = jnp.pad(nodes, (0, padded_count - count))
    channels = field.shape[0]
    return pl.pallas_call(
        gather_kernel,
        grid=(padded_count // TILE,),
        in_specs=[
            pl.BlockSpec((1, TILE), lambda i: (0, i)),
            pl.BlockSpec(field.shape, lambda i: (0, 0, 0)),
        ],
        out_specs=pl.BlockSpec((channels, TILE), lambda i: (0, i)),
        out_shape=jax.ShapeDtypeStruct((channels, padded_count), jnp.float32),
    )(nodes.reshape(1, padded_count), field)[:, :count]


def node_scatter_add(forces, nodes, start):
    channels, count = forces.shape
    padded_count = -(-count // TILE) * TILE
    nodes = jnp.pad(nodes, (0, padded_count - count))
    forces = jnp.pad(forces, ((0, 0), (0, padded_count - count)))
    return pl.pallas_call(
        scatter_kernel,
        grid=(padded_count // TILE,),
        in_specs=[
            pl.BlockSpec((1, TILE), lambda i: (0, i)),
            pl.BlockSpec((channels, TILE), lambda i: (0, i)),
            pl.BlockSpec(start.shape, lambda i: (0, 0, 0)),
        ],
        out_specs=pl.BlockSpec(start.shape, lambda i: (0, 0, 0)),
        out_shape=jax.ShapeDtypeStruct(start.shape, jnp.float32),
        scratch_shapes=[pltpu.VMEM((channels * LANES, start.shape[2]), jnp.float32)],
    )(nodes.reshape(1, padded_count), forces, start)


TIME_STEP = 0.25
VISCOUS = 0.5
SOFT_GAP = 0.2
REACH_SQ = 1.0
DAMPING = 0.5


def padded_2(block, sides, width):
    for axis, dim in sides:
        count = lax.axis_size(axis)
        forward = [(i, i + 1) for i in range(count - 1)]
        backward = [(target, source) for source, target in forward]
        low = lax.ppermute(
            lax.index_in_dim(block, block.shape[dim] - 1, axis=dim, keepdims=False), axis, forward
        )
        high = lax.ppermute(lax.index_in_dim(block, 0, axis=dim, keepdims=False), axis, backward)
        block = jnp.concatenate(
            [jnp.expand_dims(low, dim), block, jnp.expand_dims(high, dim)], axis=dim
        )
    return block


def pair_mean(values, along):
    length = values.shape[along]
    return 0.5 * (
        lax.slice_in_dim(values, 0, length - 1, axis=along)
        + lax.slice_in_dim(values, 1, length, axis=along)
    )


def pair_diff(values, along):
    length = values.shape[along]
    return lax.slice_in_dim(values, 1, length, axis=along) - lax.slice_in_dim(
        values, 0, length - 1, axis=along
    )


def pair_prod(values, along):
    length = values.shape[along]
    return lax.slice_in_dim(values, 0, length - 1, axis=along) * lax.slice_in_dim(
        values, 1, length, axis=along
    )


def corner_mean(values):
    return pair_mean(pair_mean(pair_mean(values, 0), 1), 2)


def zone_rate(vel):
    rate_x = pair_diff(pair_mean(pair_mean(vel[0], 0), 2), 1)
    rate_y = pair_diff(pair_mean(pair_mean(vel[1], 0), 1), 2)
    rate_z = pair_diff(pair_mean(pair_mean(vel[2], 1), 2), 0)
    return rate_x + rate_y + rate_z


def stress_forces(padded):
    inside = pair_prod(pair_prod(pair_prod(padded[5], 0), 1), 2)
    strain = TIME_STEP * zone_rate(padded[0:3])
    pressure = inside * (
        corner_mean(padded[4]) + corner_mean(padded[3]) * (VISCOUS * strain * strain - strain)
    )
    framed = jnp.pad(pressure, ((1, 1), (0, 0), (0, 0)))
    force_x = -pair_diff(pair_mean(pair_mean(framed, 0), 2), 1)
    force_y = -pair_diff(pair_mean(pair_mean(framed, 0), 1), 2)
    force_z = -pair_diff(pair_mean(pair_mean(framed, 1), 2), 0)
    return (jnp.stack([force_x, force_y, force_z], axis=0), inside)


def nodal_rate(padded_vel, inside):
    rate = inside * zone_rate(padded_vel)
    framed = jnp.pad(rate, ((1, 1), (0, 0), (0, 0)))
    return pair_mean(pair_mean(pair_mean(framed, 0), 1), 2)


def contact_pairs(slave, master):
    delta_x = slave[:, 0, None, :] - master[:, 0, :, None]
    delta_y = slave[:, 1, None, :] - master[:, 1, :, None]
    delta_z = slave[:, 2, None, :] - master[:, 2, :, None]
    normal_x = master[:, 3, :, None]
    normal_y = master[:, 4, :, None]
    normal_z = master[:, 5, :, None]
    dist_sq = delta_x * delta_x + delta_y * delta_y + delta_z * delta_z
    gap_normal = normal_x * delta_x + normal_y * delta_y + normal_z * delta_z
    master_along = (
        master[:, 3] * master[:, 6] + master[:, 4] * master[:, 7] + master[:, 5] * master[:, 8]
    )
    closing = (
        normal_x * slave[:, 3, None, :]
        + normal_y * slave[:, 4, None, :]
        + normal_z * slave[:, 5, None, :]
    ) - master_along[:, :, None]
    weight = jnp.exp(-dist_sq / REACH_SQ)
    soft = gap_normal * (-1.0 / SOFT_GAP)
    depth_soft = SOFT_GAP * (jnp.maximum(soft, 0.0) + jnp.log1p(jnp.exp(-jnp.abs(soft))))
    push_force = (
        slave[:, 6, None, :]
        * master[:, 9, :, None]
        * weight
        * depth_soft
        * (1.0 + DAMPING * jnp.tanh(-closing))
    )
    slave_force = jnp.stack(
        [
            jnp.sum(push_force * normal_x, axis=1),
            jnp.sum(push_force * normal_y, axis=1),
            jnp.sum(push_force * normal_z, axis=1),
        ],
        axis=1,
    )
    reaction = jnp.sum(push_force, axis=2)
    return (slave_force, reaction)


def master_normals(master_tilt):
    scale = lax.rsqrt(
        1.0 + master_tilt[:, 0] * master_tilt[:, 0] + master_tilt[:, 1] * master_tilt[:, 1]
    )
    return jnp.stack([master_tilt[:, 0] * scale, master_tilt[:, 1] * scale, scale], axis=1)


def on_device(
    velocity,
    bulk,
    prestress,
    node_mass,
    slave_pos,
    slave_area,
    seg_count,
    slave_node,
    pair_owner,
    pair_master,
    master_cent,
    master_tilt,
    master_stiff,
    master_node,
):
    count_gx = lax.axis_size("gx")
    count_gy = lax.axis_size("gy")
    devices = count_gx * count_gy
    layers, row_cells, col_cells = bulk.shape
    node_total = layers * row_cells * col_cells
    block_total, _, seg_width = slave_pos.shape
    master_total = master_cent.shape[0]
    slot_depth = (block_total + devices - 1) // devices + 1
    stacked = jnp.concatenate(
        [velocity, bulk[None], prestress[None], jnp.ones_like(bulk)[None]], axis=0
    )
    vel_flat = velocity.reshape(3, layers * row_cells, col_cells)
    slave_count = block_total * seg_width
    slave_vel = (
        node_gather(vel_flat, slave_node.reshape(-1))
        .reshape(3, block_total, seg_width)
        .transpose(1, 0, 2)
    )
    stacked, slave_vel = lax.optimization_barrier((stacked, slave_vel))
    padded = padded_2(stacked, (("gx", 2), ("gy", 3)), 1)
    stress, inside = stress_forces(padded)
    master_vel = (
        node_gather(vel_flat, master_node.reshape(-1))
        .reshape(3, master_total, seg_width)
        .transpose(1, 0, 2)
    )
    live_mask = jnp.arange(seg_width, dtype=jnp.int32)[None, :] < seg_count[:, None]
    area_live = jnp.where(live_mask, slave_area, jnp.zeros_like(slave_area))
    slave = jnp.concatenate(
        [slave_pos + TIME_STEP * slave_vel, slave_vel, area_live[:, None, :]], axis=1
    )
    normals = master_normals(master_tilt)
    master_data = jnp.concatenate(
        [master_cent + TIME_STEP * master_vel, normals, master_vel, master_stiff[:, None, :]],
        axis=1,
    )
    owners = pair_owner[:, 0]
    positions = jnp.arange(block_total, dtype=jnp.int32)
    earlier = (owners[:, None] == owners[None, :]) & (positions[None, :] < positions[:, None])
    slot_index = jnp.sum(earlier.astype(jnp.int32), axis=1)
    target_slot = owners * slot_depth + slot_index
    slot_hit = target_slot[None, :] == jnp.arange(devices * slot_depth, dtype=jnp.int32)[:, None]
    source = jnp.sum(jnp.where(slot_hit, positions[None, :], 0), axis=1)
    filled = jnp.any(slot_hit, axis=1)
    tagged = jnp.concatenate(
        [
            slave,
            jnp.broadcast_to(pair_master.astype(jnp.float32)[:, None, None], (block_total, 1, seg_width)),
        ],
        axis=1,
    )
    outgoing = jnp.where(filled[:, None, None], jnp.take(tagged, source, axis=0), 0.0)
    arrived = lax.all_to_all(
        outgoing.reshape(devices, slot_depth, 8, seg_width),
        ("gx", "gy"),
        split_axis=0,
        concat_axis=0,
        tiled=True,
    )
    item_total = devices * slot_depth
    arrived = arrived.reshape(item_total, 8, seg_width)
    picked = jnp.max(arrived[:, 7, :], axis=1).astype(jnp.int32)
    arrived = arrived[:, :7]
    paired = jnp.take(master_data, picked, axis=0)
    forces, reaction = contact_pairs(arrived, paired)
    forces = forces.reshape(item_total, 3, seg_width)
    reaction = reaction.reshape(item_total, seg_width)
    onehot = (picked[:, None] == jnp.arange(master_total, dtype=jnp.int32)[None, :]).astype(
        jnp.float32
    )
    master_sum = jnp.dot(onehot.T, reaction, precision=lax.Precision.HIGHEST)
    master_force = -master_sum[:, None, :] * normals
    master_contact = node_scatter_add(
        master_force.transpose(1, 0, 2).reshape(3, -1),
        master_node.reshape(-1),
        jnp.zeros((3, layers * row_cells, col_cells), jnp.float32),
    )
    returned = lax.all_to_all(
        forces.reshape(devices, slot_depth, 3, seg_width),
        ("gx", "gy"),
        split_axis=0,
        concat_axis=0,
        tiled=True,
    )
    slave_force = jnp.take(returned.reshape(item_total, 3, seg_width), target_slot, axis=0)
    contact = node_scatter_add(
        slave_force.transpose(1, 0, 2).reshape(3, -1), slave_node.reshape(-1), master_contact
    )
    contact_field = contact.reshape(3, layers, row_cells, col_cells)
    velocity_new = velocity + TIME_STEP * (stress + contact_field) / node_mass[None]
    padded_new = padded_2(velocity_new, (("gx", 2), ("gy", 3)), 1)
    node_rate = nodal_rate(padded_new, inside)
    return (velocity_new, node_rate)


def solution(mesh):
    placed = (
        P(None, None, "gx", "gy"),
        P(None, "gx", "gy"),
        P(None, "gx", "gy"),
        P(None, "gx", "gy"),
        P(("gx", "gy"), None, None),
        P(("gx", "gy"), None),
        P(("gx", "gy")),
        P(("gx", "gy"), None),
        P(("gx", "gy"), None),
        P(("gx", "gy")),
        P(("gx", "gy"), None, None),
        P(("gx", "gy"), None, None),
        P(("gx", "gy"), None),
        P(("gx", "gy"), None),
    )
    return jax.shard_map(
        on_device,
        mesh=mesh,
        in_specs=placed,
        out_specs=(P(None, None, "gx", "gy"), P(None, "gx", "gy")),
        check_vma=False,
    )
```

```python
import jax
import jax.numpy as jnp
from jax import lax
from jax.sharding import PartitionSpec as P
from jax.experimental import pallas as pl
from jax.experimental.pallas import tpu as pltpu

LANES = 128
TILE = 4096


def split_pieces(values):
    first = values.astype(jnp.bfloat16)
    rest = values - first.astype(jnp.float32)
    second = rest.astype(jnp.bfloat16)
    third = (rest - second.astype(jnp.float32)).astype(jnp.bfloat16)
    return (first, second, third)


def block_swap(values):
    channels = values.shape[0] // LANES if values.ndim == 2 else values.shape[0]
    if values.ndim == 3:
        return jnp.concatenate(
            [
                jnp.concatenate([values[c, :, :LANES].T, values[c, :, LANES:].T], axis=1)
                for c in range(channels)
            ],
            axis=0,
        )
    return jnp.stack(
        [
            jnp.concatenate(
                [
                    values[c * LANES : (c + 1) * LANES, :LANES].T,
                    values[c * LANES : (c + 1) * LANES, LANES:].T,
                ],
                axis=1,
            )
            for c in range(channels)
        ]
    )


def node_parts(node):
    high = ((node & (2 * LANES - 1)) >> 7) * LANES + (node >> 8)
    return high, node & (LANES - 1)


def gather_kernel(index_ref, field_ref, out_ref):
    node = index_ref[...]
    width = node.shape[1]
    table = block_swap(field_ref[...])
    high_count = table.shape[1]
    channels = out_ref.shape[0]
    high, low = node_parts(node)
    onehot = (
        lax.broadcasted_iota(jnp.int32, (high_count, width), 0) == high
    ).astype(jnp.bfloat16)
    gathered = None
    for piece in split_pieces(table)[:2]:
        part = jnp.dot(piece, onehot, preferred_element_type=jnp.float32)
        gathered = part if gathered is None else gathered + part
    low_hit = lax.broadcasted_iota(jnp.int32, (LANES, width), 0) == low
    for c in range(channels):
        block = gathered[c * LANES : (c + 1) * LANES]
        out_ref[c : c + 1, :] = jnp.sum(jnp.where(low_hit, block, 0.0), axis=0, keepdims=True)


def scatter_kernel(index_ref, force_ref, init_ref, out_ref, acc_ref):
    @pl.when(pl.program_id(0) == 0)
    def _():
        acc_ref[...] = block_swap(init_ref[...])

    node = index_ref[...]
    width = node.shape[1]
    high_count = acc_ref.shape[1]
    channels = force_ref.shape[0]
    high, low = node_parts(node)
    onehot = (
        lax.broadcasted_iota(jnp.int32, (high_count, width), 0) == high
    ).astype(jnp.bfloat16)
    low_hit = lax.broadcasted_iota(jnp.int32, (LANES, width), 0) == low
    total = None
    for piece in split_pieces(force_ref[...])[:2]:
        spread = jnp.concatenate(
            [jnp.where(low_hit, piece[c : c + 1, :], jnp.zeros_like(piece[c : c + 1, :])) for c in range(channels)],
            axis=0,
        )
        part = lax.dot_general(
            spread, onehot, (((1,), (1,)), ((), ())), preferred_element_type=jnp.float32
        )
        total = part if total is None else total + part
    acc_ref[...] += total

    @pl.when(pl.program_id(0) == pl.num_programs(0) - 1)
    def _():
        out_ref[...] = block_swap(acc_ref[...])


def node_gather(field, nodes):
    count = nodes.shape[0]
    padded_count = -(-count // TILE) * TILE
    nodes = jnp.pad(nodes, (0, padded_count - count))
    channels = field.shape[0]
    return pl.pallas_call(
        gather_kernel,
        grid=(padded_count // TILE,),
        in_specs=[
            pl.BlockSpec((1, TILE), lambda i: (0, i)),
            pl.BlockSpec(field.shape, lambda i: (0, 0, 0)),
        ],
        out_specs=pl.BlockSpec((channels, TILE), lambda i: (0, i)),
        out_shape=jax.ShapeDtypeStruct((channels, padded_count), jnp.float32),
    )(nodes.reshape(1, padded_count), field)[:, :count]


def node_scatter_add(forces, nodes, start):
    channels, count = forces.shape
    padded_count = -(-count // TILE) * TILE
    nodes = jnp.pad(nodes, (0, padded_count - count))
    forces = jnp.pad(forces, ((0, 0), (0, padded_count - count)))
    return pl.pallas_call(
        scatter_kernel,
        grid=(padded_count // TILE,),
        in_specs=[
            pl.BlockSpec((1, TILE), lambda i: (0, i)),
            pl.BlockSpec((channels, TILE), lambda i: (0, i)),
            pl.BlockSpec(start.shape, lambda i: (0, 0, 0)),
        ],
        out_specs=pl.BlockSpec(start.shape, lambda i: (0, 0, 0)),
        out_shape=jax.ShapeDtypeStruct(start.shape, jnp.float32),
        scratch_shapes=[pltpu.VMEM((channels * LANES, start.shape[2]), jnp.float32)],
    )(nodes.reshape(1, padded_count), forces, start)


TIME_STEP = 0.25
VISCOUS = 0.5
SOFT_GAP = 0.2
REACH_SQ = 1.0
DAMPING = 0.5


def padded_2(block, sides, width):
    for axis, dim in sides:
        count = lax.axis_size(axis)
        forward = [(i, i + 1) for i in range(count - 1)]
        backward = [(target, source) for source, target in forward]
        low = lax.ppermute(
            lax.index_in_dim(block, block.shape[dim] - 1, axis=dim, keepdims=False), axis, forward
        )
        high = lax.ppermute(lax.index_in_dim(block, 0, axis=dim, keepdims=False), axis, backward)
        block = jnp.concatenate(
            [jnp.expand_dims(low, dim), block, jnp.expand_dims(high, dim)], axis=dim
        )
    return block


def pair_mean(values, along):
    length = values.shape[along]
    return 0.5 * (
        lax.slice_in_dim(values, 0, length - 1, axis=along)
        + lax.slice_in_dim(values, 1, length, axis=along)
    )


def pair_diff(values, along):
    length = values.shape[along]
    return lax.slice_in_dim(values, 1, length, axis=along) - lax.slice_in_dim(
        values, 0, length - 1, axis=along
    )


def pair_prod(values, along):
    length = values.shape[along]
    return lax.slice_in_dim(values, 0, length - 1, axis=along) * lax.slice_in_dim(
        values, 1, length, axis=along
    )


def corner_mean(values):
    return pair_mean(pair_mean(pair_mean(values, 0), 1), 2)


def zone_rate(vel):
    rate_x = pair_diff(pair_mean(pair_mean(vel[0], 0), 2), 1)
    rate_y = pair_diff(pair_mean(pair_mean(vel[1], 0), 1), 2)
    rate_z = pair_diff(pair_mean(pair_mean(vel[2], 1), 2), 0)
    return rate_x + rate_y + rate_z


def stress_forces(padded):
    inside = pair_prod(pair_prod(pair_prod(padded[5], 0), 1), 2)
    strain = TIME_STEP * zone_rate(padded[0:3])
    pressure = inside * (
        corner_mean(padded[4]) + corner_mean(padded[3]) * (VISCOUS * strain * strain - strain)
    )
    framed = jnp.pad(pressure, ((1, 1), (0, 0), (0, 0)))
    force_x = -pair_diff(pair_mean(pair_mean(framed, 0), 2), 1)
    force_y = -pair_diff(pair_mean(pair_mean(framed, 0), 1), 2)
    force_z = -pair_diff(pair_mean(pair_mean(framed, 1), 2), 0)
    return (jnp.stack([force_x, force_y, force_z], axis=0), inside)


def nodal_rate(padded_vel, inside):
    rate = inside * zone_rate(padded_vel)
    framed = jnp.pad(rate, ((1, 1), (0, 0), (0, 0)))
    return pair_mean(pair_mean(pair_mean(framed, 0), 1), 2)


def contact_pairs(slave, master):
    delta_x = slave[:, 0, None, :] - master[:, 0, :, None]
    delta_y = slave[:, 1, None, :] - master[:, 1, :, None]
    delta_z = slave[:, 2, None, :] - master[:, 2, :, None]
    normal_x = master[:, 3, :, None]
    normal_y = master[:, 4, :, None]
    normal_z = master[:, 5, :, None]
    dist_sq = delta_x * delta_x + delta_y * delta_y + delta_z * delta_z
    gap_normal = normal_x * delta_x + normal_y * delta_y + normal_z * delta_z
    master_along = (
        master[:, 3] * master[:, 6] + master[:, 4] * master[:, 7] + master[:, 5] * master[:, 8]
    )
    closing = (
        normal_x * slave[:, 3, None, :]
        + normal_y * slave[:, 4, None, :]
        + normal_z * slave[:, 5, None, :]
    ) - master_along[:, :, None]
    weight = jnp.exp(-dist_sq / REACH_SQ)
    soft = gap_normal * (-1.0 / SOFT_GAP)
    depth_soft = SOFT_GAP * (jnp.maximum(soft, 0.0) + jnp.log1p(jnp.exp(-jnp.abs(soft))))
    push_force = (
        slave[:, 6, None, :]
        * master[:, 9, :, None]
        * weight
        * depth_soft
        * (1.0 + DAMPING * jnp.tanh(-closing))
    )
    slave_force = jnp.stack(
        [
            jnp.sum(push_force * normal_x, axis=1),
            jnp.sum(push_force * normal_y, axis=1),
            jnp.sum(push_force * normal_z, axis=1),
        ],
        axis=1,
    )
    reaction = jnp.sum(push_force, axis=2)
    return (slave_force, reaction)


def master_normals(master_tilt):
    scale = lax.rsqrt(
        1.0 + master_tilt[:, 0] * master_tilt[:, 0] + master_tilt[:, 1] * master_tilt[:, 1]
    )
    return jnp.stack([master_tilt[:, 0] * scale, master_tilt[:, 1] * scale, scale], axis=1)


def on_device(
    velocity,
    bulk,
    prestress,
    node_mass,
    slave_pos,
    slave_area,
    seg_count,
    slave_node,
    pair_owner,
    pair_master,
    master_cent,
    master_tilt,
    master_stiff,
    master_node,
):
    count_gx = lax.axis_size("gx")
    count_gy = lax.axis_size("gy")
    devices = count_gx * count_gy
    layers, row_cells, col_cells = bulk.shape
    node_total = layers * row_cells * col_cells
    block_total, _, seg_width = slave_pos.shape
    master_total = master_cent.shape[0]
    slot_depth = (block_total + devices - 1) // devices + 1
    vel_flat = velocity.reshape(3, layers * row_cells, col_cells)
    slave_count = block_total * seg_width
    slave_vel = (
        node_gather(vel_flat, slave_node.reshape(-1))
        .reshape(3, block_total, seg_width)
        .transpose(1, 0, 2)
    )
    held_vel, held_bulk, held_pre, slave_vel = lax.optimization_barrier(
        (velocity, bulk, prestress, slave_vel)
    )
    stacked = jnp.concatenate(
        [held_vel, held_bulk[None], held_pre[None], jnp.ones_like(held_bulk)[None]], axis=0
    )
    padded = padded_2(stacked, (("gx", 2), ("gy", 3)), 1)
    stress, inside = stress_forces(padded)
    master_vel = (
        node_gather(vel_flat, master_node.reshape(-1))
        .reshape(3, master_total, seg_width)
        .transpose(1, 0, 2)
    )
    live_mask = jnp.arange(seg_width, dtype=jnp.int32)[None, :] < seg_count[:, None]
    area_live = jnp.where(live_mask, slave_area, jnp.zeros_like(slave_area))
    slave = jnp.concatenate(
        [slave_pos + TIME_STEP * slave_vel, slave_vel, area_live[:, None, :]], axis=1
    )
    normals = master_normals(master_tilt)
    master_data = jnp.concatenate(
        [master_cent + TIME_STEP * master_vel, normals, master_vel, master_stiff[:, None, :]],
        axis=1,
    )
    owners = pair_owner[:, 0]
    positions = jnp.arange(block_total, dtype=jnp.int32)
    earlier = (owners[:, None] == owners[None, :]) & (positions[None, :] < positions[:, None])
    slot_index = jnp.sum(earlier.astype(jnp.int32), axis=1)
    target_slot = owners * slot_depth + slot_index
    slot_hit = target_slot[None, :] == jnp.arange(devices * slot_depth, dtype=jnp.int32)[:, None]
    source = jnp.sum(jnp.where(slot_hit, positions[None, :], 0), axis=1)
    filled = jnp.any(slot_hit, axis=1)
    tagged = jnp.concatenate(
        [
            slave,
            jnp.broadcast_to(pair_master.astype(jnp.float32)[:, None, None], (block_total, 1, seg_width)),
        ],
        axis=1,
    )
    outgoing = jnp.where(filled[:, None, None], jnp.take(tagged, source, axis=0), 0.0)
    arrived = lax.all_to_all(
        outgoing.reshape(devices, slot_depth, 8, seg_width),
        ("gx", "gy"),
        split_axis=0,
        concat_axis=0,
        tiled=True,
    )
    item_total = devices * slot_depth
    arrived = arrived.reshape(item_total, 8, seg_width)
    picked = jnp.max(arrived[:, 7, :], axis=1).astype(jnp.int32)
    arrived = arrived[:, :7]
    paired = jnp.take(master_data, picked, axis=0)
    forces, reaction = contact_pairs(arrived, paired)
    forces = forces.reshape(item_total, 3, seg_width)
    reaction = reaction.reshape(item_total, seg_width)
    onehot = (picked[:, None] == jnp.arange(master_total, dtype=jnp.int32)[None, :]).astype(
        jnp.float32
    )
    master_sum = jnp.dot(onehot.T, reaction, precision=lax.Precision.HIGHEST)
    master_force = -master_sum[:, None, :] * normals
    master_contact = node_scatter_add(
        master_force.transpose(1, 0, 2).reshape(3, -1),
        master_node.reshape(-1),
        jnp.zeros((3, layers * row_cells, col_cells), jnp.float32),
    )
    returned = lax.all_to_all(
        forces.reshape(devices, slot_depth, 3, seg_width),
        ("gx", "gy"),
        split_axis=0,
        concat_axis=0,
        tiled=True,
    )
    slave_force = jnp.take(returned.reshape(item_total, 3, seg_width), target_slot, axis=0)
    contact = node_scatter_add(
        slave_force.transpose(1, 0, 2).reshape(3, -1), slave_node.reshape(-1), master_contact
    )
    contact_field = contact.reshape(3, layers, row_cells, col_cells)
    velocity_new = velocity + TIME_STEP * (stress + contact_field) / node_mass[None]
    padded_new = padded_2(velocity_new, (("gx", 2), ("gy", 3)), 1)
    node_rate = nodal_rate(padded_new, inside)
    return (velocity_new, node_rate)


def solution(mesh):
    placed = (
        P(None, None, "gx", "gy"),
        P(None, "gx", "gy"),
        P(None, "gx", "gy"),
        P(None, "gx", "gy"),
        P(("gx", "gy"), None, None),
        P(("gx", "gy"), None),
        P(("gx", "gy")),
        P(("gx", "gy"), None),
        P(("gx", "gy"), None),
        P(("gx", "gy")),
        P(("gx", "gy"), None, None),
        P(("gx", "gy"), None, None),
        P(("gx", "gy"), None),
        P(("gx", "gy"), None),
    )
    return jax.shard_map(
        on_device,
        mesh=mesh,
        in_specs=placed,
        out_specs=(P(None, None, "gx", "gy"), P(None, "gx", "gy")),
        check_vma=False,
    )
```

```python
import jax
import jax.numpy as jnp
from jax import lax
from jax.sharding import PartitionSpec as P
from jax.experimental import pallas as pl
from jax.experimental.pallas import tpu as pltpu

LANES = 128
TILE = 4096


def split_pieces(values):
    first = values.astype(jnp.bfloat16)
    rest = values - first.astype(jnp.float32)
    second = rest.astype(jnp.bfloat16)
    third = (rest - second.astype(jnp.float32)).astype(jnp.bfloat16)
    return (first, second, third)


def block_swap(values):
    channels = values.shape[0] // LANES if values.ndim == 2 else values.shape[0]
    if values.ndim == 3:
        return jnp.concatenate(
            [
                jnp.concatenate([values[c, :, :LANES].T, values[c, :, LANES:].T], axis=1)
                for c in range(channels)
            ],
            axis=0,
        )
    return jnp.stack(
        [
            jnp.concatenate(
                [
                    values[c * LANES : (c + 1) * LANES, :LANES].T,
                    values[c * LANES : (c + 1) * LANES, LANES:].T,
                ],
                axis=1,
            )
            for c in range(channels)
        ]
    )


def node_parts(node):
    high = ((node & (2 * LANES - 1)) >> 7) * LANES + (node >> 8)
    return high, node & (LANES - 1)


def gather_kernel(index_ref, field_ref, out_ref):
    node = index_ref[...]
    width = node.shape[1]
    table = block_swap(field_ref[...])
    high_count = table.shape[1]
    channels = out_ref.shape[0]
    high, low = node_parts(node)
    onehot = (
        lax.broadcasted_iota(jnp.int32, (high_count, width), 0) == high
    ).astype(jnp.bfloat16)
    gathered = None
    for piece in split_pieces(table)[:2]:
        part = jnp.dot(piece, onehot, preferred_element_type=jnp.float32)
        gathered = part if gathered is None else gathered + part
    low_hit = lax.broadcasted_iota(jnp.int32, (LANES, width), 0) == low
    for c in range(channels):
        block = gathered[c * LANES : (c + 1) * LANES]
        out_ref[c : c + 1, :] = jnp.sum(jnp.where(low_hit, block, 0.0), axis=0, keepdims=True)


def scatter_kernel(index_ref, force_ref, init_ref, out_ref, acc_ref):
    @pl.when(pl.program_id(0) == 0)
    def _():
        acc_ref[...] = block_swap(init_ref[...])

    node = index_ref[...]
    width = node.shape[1]
    high_count = acc_ref.shape[1]
    channels = force_ref.shape[0]
    high, low = node_parts(node)
    onehot = (
        lax.broadcasted_iota(jnp.int32, (high_count, width), 0) == high
    ).astype(jnp.bfloat16)
    low_hit = lax.broadcasted_iota(jnp.int32, (LANES, width), 0) == low
    total = None
    for piece in split_pieces(force_ref[...])[:2]:
        spread = jnp.concatenate(
            [jnp.where(low_hit, piece[c : c + 1, :], jnp.zeros_like(piece[c : c + 1, :])) for c in range(channels)],
            axis=0,
        )
        part = lax.dot_general(
            spread, onehot, (((1,), (1,)), ((), ())), preferred_element_type=jnp.float32
        )
        total = part if total is None else total + part
    acc_ref[...] += total

    @pl.when(pl.program_id(0) == pl.num_programs(0) - 1)
    def _():
        out_ref[...] = block_swap(acc_ref[...])


def node_gather(field, nodes):
    count = nodes.shape[0]
    padded_count = -(-count // TILE) * TILE
    nodes = jnp.pad(nodes, (0, padded_count - count))
    channels = field.shape[0]
    return pl.pallas_call(
        gather_kernel,
        grid=(padded_count // TILE,),
        in_specs=[
            pl.BlockSpec((1, TILE), lambda i: (0, i)),
            pl.BlockSpec(field.shape, lambda i: (0, 0, 0)),
        ],
        out_specs=pl.BlockSpec((channels, TILE), lambda i: (0, i)),
        out_shape=jax.ShapeDtypeStruct((channels, padded_count), jnp.float32),
    )(nodes.reshape(1, padded_count), field)[:, :count]


def node_scatter_add(forces, nodes, start):
    channels, count = forces.shape
    padded_count = -(-count // TILE) * TILE
    nodes = jnp.pad(nodes, (0, padded_count - count))
    forces = jnp.pad(forces, ((0, 0), (0, padded_count - count)))
    return pl.pallas_call(
        scatter_kernel,
        grid=(padded_count // TILE,),
        in_specs=[
            pl.BlockSpec((1, TILE), lambda i: (0, i)),
            pl.BlockSpec((channels, TILE), lambda i: (0, i)),
            pl.BlockSpec(start.shape, lambda i: (0, 0, 0)),
        ],
        out_specs=pl.BlockSpec(start.shape, lambda i: (0, 0, 0)),
        out_shape=jax.ShapeDtypeStruct(start.shape, jnp.float32),
        scratch_shapes=[pltpu.VMEM((channels * LANES, start.shape[2]), jnp.float32)],
    )(nodes.reshape(1, padded_count), forces, start)


TIME_STEP = 0.25
VISCOUS = 0.5
SOFT_GAP = 0.2
REACH_SQ = 1.0
DAMPING = 0.5


def padded_2(block, sides, width):
    for axis, dim in sides:
        count = lax.axis_size(axis)
        forward = [(i, i + 1) for i in range(count - 1)]
        backward = [(target, source) for source, target in forward]
        low = lax.ppermute(
            lax.index_in_dim(block, block.shape[dim] - 1, axis=dim, keepdims=False), axis, forward
        )
        high = lax.ppermute(lax.index_in_dim(block, 0, axis=dim, keepdims=False), axis, backward)
        block = jnp.concatenate(
            [jnp.expand_dims(low, dim), block, jnp.expand_dims(high, dim)], axis=dim
        )
    return block


def pair_mean(values, along):
    length = values.shape[along]
    return 0.5 * (
        lax.slice_in_dim(values, 0, length - 1, axis=along)
        + lax.slice_in_dim(values, 1, length, axis=along)
    )


def pair_diff(values, along):
    length = values.shape[along]
    return lax.slice_in_dim(values, 1, length, axis=along) - lax.slice_in_dim(
        values, 0, length - 1, axis=along
    )


def pair_prod(values, along):
    length = values.shape[along]
    return lax.slice_in_dim(values, 0, length - 1, axis=along) * lax.slice_in_dim(
        values, 1, length, axis=along
    )


def corner_mean(values):
    return pair_mean(pair_mean(pair_mean(values, 0), 1), 2)


def zone_rate(vel):
    rate_x = pair_diff(pair_mean(pair_mean(vel[0], 0), 2), 1)
    rate_y = pair_diff(pair_mean(pair_mean(vel[1], 0), 1), 2)
    rate_z = pair_diff(pair_mean(pair_mean(vel[2], 1), 2), 0)
    return rate_x + rate_y + rate_z


def stress_forces(padded):
    inside = pair_prod(pair_prod(pair_prod(padded[5], 0), 1), 2)
    strain = TIME_STEP * zone_rate(padded[0:3])
    pressure = inside * (
        corner_mean(padded[4]) + corner_mean(padded[3]) * (VISCOUS * strain * strain - strain)
    )
    framed = jnp.pad(pressure, ((1, 1), (0, 0), (0, 0)))
    force_x = -pair_diff(pair_mean(pair_mean(framed, 0), 2), 1)
    force_y = -pair_diff(pair_mean(pair_mean(framed, 0), 1), 2)
    force_z = -pair_diff(pair_mean(pair_mean(framed, 1), 2), 0)
    return (jnp.stack([force_x, force_y, force_z], axis=0), inside)


def nodal_rate(padded_vel, inside):
    rate = inside * zone_rate(padded_vel)
    framed = jnp.pad(rate, ((1, 1), (0, 0), (0, 0)))
    return pair_mean(pair_mean(pair_mean(framed, 0), 1), 2)


def contact_pairs(slave, master):
    delta_x = slave[:, 0, None, :] - master[:, 0, :, None]
    delta_y = slave[:, 1, None, :] - master[:, 1, :, None]
    delta_z = slave[:, 2, None, :] - master[:, 2, :, None]
    normal_x = master[:, 3, :, None]
    normal_y = master[:, 4, :, None]
    normal_z = master[:, 5, :, None]
    dist_sq = delta_x * delta_x + delta_y * delta_y + delta_z * delta_z
    gap_normal = normal_x * delta_x + normal_y * delta_y + normal_z * delta_z
    master_along = (
        master[:, 3] * master[:, 6] + master[:, 4] * master[:, 7] + master[:, 5] * master[:, 8]
    )
    closing = (
        normal_x * slave[:, 3, None, :]
        + normal_y * slave[:, 4, None, :]
        + normal_z * slave[:, 5, None, :]
    ) - master_along[:, :, None]
    weight = jnp.exp(-dist_sq / REACH_SQ)
    soft = gap_normal * (-1.0 / SOFT_GAP)
    depth_soft = SOFT_GAP * (jnp.maximum(soft, 0.0) + jnp.log1p(jnp.exp(-jnp.abs(soft))))
    push_force = (
        slave[:, 6, None, :]
        * master[:, 9, :, None]
        * weight
        * depth_soft
        * (1.0 + DAMPING * jnp.tanh(-closing))
    )
    slave_force = jnp.stack(
        [
            jnp.sum(push_force * normal_x, axis=1),
            jnp.sum(push_force * normal_y, axis=1),
            jnp.sum(push_force * normal_z, axis=1),
        ],
        axis=1,
    )
    reaction = jnp.sum(push_force, axis=2)
    return (slave_force, reaction)


def master_normals(master_tilt):
    scale = lax.rsqrt(
        1.0 + master_tilt[:, 0] * master_tilt[:, 0] + master_tilt[:, 1] * master_tilt[:, 1]
    )
    return jnp.stack([master_tilt[:, 0] * scale, master_tilt[:, 1] * scale, scale], axis=1)


def on_device(
    velocity,
    bulk,
    prestress,
    node_mass,
    slave_pos,
    slave_area,
    seg_count,
    slave_node,
    pair_owner,
    pair_master,
    master_cent,
    master_tilt,
    master_stiff,
    master_node,
):
    count_gx = lax.axis_size("gx")
    count_gy = lax.axis_size("gy")
    devices = count_gx * count_gy
    layers, row_cells, col_cells = bulk.shape
    node_total = layers * row_cells * col_cells
    block_total, _, seg_width = slave_pos.shape
    master_total = master_cent.shape[0]
    slot_depth = (block_total + devices - 1) // devices + 1
    vel_flat = velocity.reshape(3, layers * row_cells, col_cells)
    slave_count = block_total * seg_width
    slave_vel = (
        node_gather(vel_flat, slave_node.reshape(-1))
        .reshape(3, block_total, seg_width)
        .transpose(1, 0, 2)
    )
    master_vel = (
        node_gather(vel_flat, master_node.reshape(-1))
        .reshape(3, master_total, seg_width)
        .transpose(1, 0, 2)
    )
    held_vel, held_bulk, held_pre, master_vel = lax.optimization_barrier(
        (velocity, bulk, prestress, master_vel)
    )
    stacked = jnp.concatenate(
        [held_vel, held_bulk[None], held_pre[None], jnp.ones_like(held_bulk)[None]], axis=0
    )
    padded = padded_2(stacked, (("gx", 2), ("gy", 3)), 1)
    stress, inside = stress_forces(padded)
    live_mask = jnp.arange(seg_width, dtype=jnp.int32)[None, :] < seg_count[:, None]
    area_live = jnp.where(live_mask, slave_area, jnp.zeros_like(slave_area))
    slave = jnp.concatenate(
        [slave_pos + TIME_STEP * slave_vel, slave_vel, area_live[:, None, :]], axis=1
    )
    normals = master_normals(master_tilt)
    master_data = jnp.concatenate(
        [master_cent + TIME_STEP * master_vel, normals, master_vel, master_stiff[:, None, :]],
        axis=1,
    )
    owners = pair_owner[:, 0]
    positions = jnp.arange(block_total, dtype=jnp.int32)
    earlier = (owners[:, None] == owners[None, :]) & (positions[None, :] < positions[:, None])
    slot_index = jnp.sum(earlier.astype(jnp.int32), axis=1)
    target_slot = owners * slot_depth + slot_index
    slot_hit = target_slot[None, :] == jnp.arange(devices * slot_depth, dtype=jnp.int32)[:, None]
    source = jnp.sum(jnp.where(slot_hit, positions[None, :], 0), axis=1)
    filled = jnp.any(slot_hit, axis=1)
    tagged = jnp.concatenate(
        [
            slave,
            jnp.broadcast_to(pair_master.astype(jnp.float32)[:, None, None], (block_total, 1, seg_width)),
        ],
        axis=1,
    )
    outgoing = jnp.where(filled[:, None, None], jnp.take(tagged, source, axis=0), 0.0)
    arrived = lax.all_to_all(
        outgoing.reshape(devices, slot_depth, 8, seg_width),
        ("gx", "gy"),
        split_axis=0,
        concat_axis=0,
        tiled=True,
    )
    item_total = devices * slot_depth
    arrived = arrived.reshape(item_total, 8, seg_width)
    picked = jnp.max(arrived[:, 7, :], axis=1).astype(jnp.int32)
    arrived = arrived[:, :7]
    paired = jnp.take(master_data, picked, axis=0)
    forces, reaction = contact_pairs(arrived, paired)
    forces = forces.reshape(item_total, 3, seg_width)
    reaction = reaction.reshape(item_total, seg_width)
    onehot = (picked[:, None] == jnp.arange(master_total, dtype=jnp.int32)[None, :]).astype(
        jnp.float32
    )
    master_sum = jnp.dot(onehot.T, reaction, precision=lax.Precision.HIGHEST)
    master_force = -master_sum[:, None, :] * normals
    master_contact = node_scatter_add(
        master_force.transpose(1, 0, 2).reshape(3, -1),
        master_node.reshape(-1),
        jnp.zeros((3, layers * row_cells, col_cells), jnp.float32),
    )
    returned = lax.all_to_all(
        forces.reshape(devices, slot_depth, 3, seg_width),
        ("gx", "gy"),
        split_axis=0,
        concat_axis=0,
        tiled=True,
    )
    slave_force = jnp.take(returned.reshape(item_total, 3, seg_width), target_slot, axis=0)
    contact = node_scatter_add(
        slave_force.transpose(1, 0, 2).reshape(3, -1), slave_node.reshape(-1), master_contact
    )
    contact_field = contact.reshape(3, layers, row_cells, col_cells)
    velocity_new = velocity + TIME_STEP * (stress + contact_field) / node_mass[None]
    padded_new = padded_2(velocity_new, (("gx", 2), ("gy", 3)), 1)
    node_rate = nodal_rate(padded_new, inside)
    return (velocity_new, node_rate)


def solution(mesh):
    placed = (
        P(None, None, "gx", "gy"),
        P(None, "gx", "gy"),
        P(None, "gx", "gy"),
        P(None, "gx", "gy"),
        P(("gx", "gy"), None, None),
        P(("gx", "gy"), None),
        P(("gx", "gy")),
        P(("gx", "gy"), None),
        P(("gx", "gy"), None),
        P(("gx", "gy")),
        P(("gx", "gy"), None, None),
        P(("gx", "gy"), None, None),
        P(("gx", "gy"), None),
        P(("gx", "gy"), None),
    )
    return jax.shard_map(
        on_device,
        mesh=mesh,
        in_specs=placed,
        out_specs=(P(None, None, "gx", "gy"), P(None, "gx", "gy")),
        check_vma=False,
    )
```

```python
import jax
import jax.numpy as jnp
from jax import lax
from jax.sharding import PartitionSpec as P
from jax.experimental import pallas as pl
from jax.experimental.pallas import tpu as pltpu

LANES = 128
TILE = 4096


def split_pieces(values):
    first = values.astype(jnp.bfloat16)
    rest = values - first.astype(jnp.float32)
    second = rest.astype(jnp.bfloat16)
    third = (rest - second.astype(jnp.float32)).astype(jnp.bfloat16)
    return (first, second, third)


def block_swap(values):
    channels = values.shape[0] // LANES if values.ndim == 2 else values.shape[0]
    if values.ndim == 3:
        return jnp.concatenate(
            [
                jnp.concatenate([values[c, :, :LANES].T, values[c, :, LANES:].T], axis=1)
                for c in range(channels)
            ],
            axis=0,
        )
    return jnp.stack(
        [
            jnp.concatenate(
                [
                    values[c * LANES : (c + 1) * LANES, :LANES].T,
                    values[c * LANES : (c + 1) * LANES, LANES:].T,
                ],
                axis=1,
            )
            for c in range(channels)
        ]
    )


def node_parts(node):
    high = ((node & (2 * LANES - 1)) >> 7) * LANES + (node >> 8)
    return high, node & (LANES - 1)


def gather_kernel(index_ref, field_ref, out_ref, piece_ref):
    @pl.when(pl.program_id(0) == 0)
    def _():
        first, second, _ = split_pieces(block_swap(field_ref[...]))
        piece_ref[0] = first
        piece_ref[1] = second

    node = index_ref[...]
    width = node.shape[1]
    high_count = piece_ref.shape[2]
    channels = out_ref.shape[0]
    high, low = node_parts(node)
    onehot = (
        lax.broadcasted_iota(jnp.int32, (high_count, width), 0) == high
    ).astype(jnp.bfloat16)
    gathered = None
    for p in range(2):
        part = jnp.dot(piece_ref[p], onehot, preferred_element_type=jnp.float32)
        gathered = part if gathered is None else gathered + part
    low_hit = lax.broadcasted_iota(jnp.int32, (LANES, width), 0) == low
    for c in range(channels):
        block = gathered[c * LANES : (c + 1) * LANES]
        out_ref[c : c + 1, :] = jnp.sum(jnp.where(low_hit, block, 0.0), axis=0, keepdims=True)


def scatter_kernel(index_ref, force_ref, init_ref, out_ref, acc_ref):
    @pl.when(pl.program_id(0) == 0)
    def _():
        acc_ref[...] = block_swap(init_ref[...])

    node = index_ref[...]
    width = node.shape[1]
    high_count = acc_ref.shape[1]
    channels = force_ref.shape[0]
    high, low = node_parts(node)
    onehot = (
        lax.broadcasted_iota(jnp.int32, (high_count, width), 0) == high
    ).astype(jnp.bfloat16)
    low_hit = lax.broadcasted_iota(jnp.int32, (LANES, width), 0) == low
    total = None
    for piece in split_pieces(force_ref[...])[:2]:
        spread = jnp.concatenate(
            [jnp.where(low_hit, piece[c : c + 1, :], jnp.zeros_like(piece[c : c + 1, :])) for c in range(channels)],
            axis=0,
        )
        part = lax.dot_general(
            spread, onehot, (((1,), (1,)), ((), ())), preferred_element_type=jnp.float32
        )
        total = part if total is None else total + part
    acc_ref[...] += total

    @pl.when(pl.program_id(0) == pl.num_programs(0) - 1)
    def _():
        out_ref[...] = block_swap(acc_ref[...])


def node_gather(field, nodes):
    count = nodes.shape[0]
    padded_count = -(-count // TILE) * TILE
    nodes = jnp.pad(nodes, (0, padded_count - count))
    channels = field.shape[0]
    return pl.pallas_call(
        gather_kernel,
        grid=(padded_count // TILE,),
        in_specs=[
            pl.BlockSpec((1, TILE), lambda i: (0, i)),
            pl.BlockSpec(field.shape, lambda i: (0, 0, 0)),
        ],
        out_specs=pl.BlockSpec((channels, TILE), lambda i: (0, i)),
        out_shape=jax.ShapeDtypeStruct((channels, padded_count), jnp.float32),
        scratch_shapes=[pltpu.VMEM((2, channels * LANES, field.shape[2]), jnp.bfloat16)],
    )(nodes.reshape(1, padded_count), field)[:, :count]


def node_scatter_add(forces, nodes, start):
    channels, count = forces.shape
    padded_count = -(-count // TILE) * TILE
    nodes = jnp.pad(nodes, (0, padded_count - count))
    forces = jnp.pad(forces, ((0, 0), (0, padded_count - count)))
    return pl.pallas_call(
        scatter_kernel,
        grid=(padded_count // TILE,),
        in_specs=[
            pl.BlockSpec((1, TILE), lambda i: (0, i)),
            pl.BlockSpec((channels, TILE), lambda i: (0, i)),
            pl.BlockSpec(start.shape, lambda i: (0, 0, 0)),
        ],
        out_specs=pl.BlockSpec(start.shape, lambda i: (0, 0, 0)),
        out_shape=jax.ShapeDtypeStruct(start.shape, jnp.float32),
        scratch_shapes=[pltpu.VMEM((channels * LANES, start.shape[2]), jnp.float32)],
    )(nodes.reshape(1, padded_count), forces, start)


TIME_STEP = 0.25
VISCOUS = 0.5
SOFT_GAP = 0.2
REACH_SQ = 1.0
DAMPING = 0.5


def padded_2(block, sides, width):
    for axis, dim in sides:
        count = lax.axis_size(axis)
        forward = [(i, i + 1) for i in range(count - 1)]
        backward = [(target, source) for source, target in forward]
        low = lax.ppermute(
            lax.index_in_dim(block, block.shape[dim] - 1, axis=dim, keepdims=False), axis, forward
        )
        high = lax.ppermute(lax.index_in_dim(block, 0, axis=dim, keepdims=False), axis, backward)
        block = jnp.concatenate(
            [jnp.expand_dims(low, dim), block, jnp.expand_dims(high, dim)], axis=dim
        )
    return block


def pair_mean(values, along):
    length = values.shape[along]
    return 0.5 * (
        lax.slice_in_dim(values, 0, length - 1, axis=along)
        + lax.slice_in_dim(values, 1, length, axis=along)
    )


def pair_diff(values, along):
    length = values.shape[along]
    return lax.slice_in_dim(values, 1, length, axis=along) - lax.slice_in_dim(
        values, 0, length - 1, axis=along
    )


def pair_prod(values, along):
    length = values.shape[along]
    return lax.slice_in_dim(values, 0, length - 1, axis=along) * lax.slice_in_dim(
        values, 1, length, axis=along
    )


def corner_mean(values):
    return pair_mean(pair_mean(pair_mean(values, 0), 1), 2)


def zone_rate(vel):
    rate_x = pair_diff(pair_mean(pair_mean(vel[0], 0), 2), 1)
    rate_y = pair_diff(pair_mean(pair_mean(vel[1], 0), 1), 2)
    rate_z = pair_diff(pair_mean(pair_mean(vel[2], 1), 2), 0)
    return rate_x + rate_y + rate_z


def stress_forces(padded):
    inside = pair_prod(pair_prod(pair_prod(padded[5], 0), 1), 2)
    strain = TIME_STEP * zone_rate(padded[0:3])
    pressure = inside * (
        corner_mean(padded[4]) + corner_mean(padded[3]) * (VISCOUS * strain * strain - strain)
    )
    framed = jnp.pad(pressure, ((1, 1), (0, 0), (0, 0)))
    force_x = -pair_diff(pair_mean(pair_mean(framed, 0), 2), 1)
    force_y = -pair_diff(pair_mean(pair_mean(framed, 0), 1), 2)
    force_z = -pair_diff(pair_mean(pair_mean(framed, 1), 2), 0)
    return (jnp.stack([force_x, force_y, force_z], axis=0), inside)


def nodal_rate(padded_vel, inside):
    rate = inside * zone_rate(padded_vel)
    framed = jnp.pad(rate, ((1, 1), (0, 0), (0, 0)))
    return pair_mean(pair_mean(pair_mean(framed, 0), 1), 2)


def contact_pairs(slave, master):
    delta_x = slave[:, 0, None, :] - master[:, 0, :, None]
    delta_y = slave[:, 1, None, :] - master[:, 1, :, None]
    delta_z = slave[:, 2, None, :] - master[:, 2, :, None]
    normal_x = master[:, 3, :, None]
    normal_y = master[:, 4, :, None]
    normal_z = master[:, 5, :, None]
    dist_sq = delta_x * delta_x + delta_y * delta_y + delta_z * delta_z
    gap_normal = normal_x * delta_x + normal_y * delta_y + normal_z * delta_z
    master_along = (
        master[:, 3] * master[:, 6] + master[:, 4] * master[:, 7] + master[:, 5] * master[:, 8]
    )
    closing = (
        normal_x * slave[:, 3, None, :]
        + normal_y * slave[:, 4, None, :]
        + normal_z * slave[:, 5, None, :]
    ) - master_along[:, :, None]
    weight = jnp.exp(-dist_sq / REACH_SQ)
    soft = gap_normal * (-1.0 / SOFT_GAP)
    depth_soft = SOFT_GAP * (jnp.maximum(soft, 0.0) + jnp.log1p(jnp.exp(-jnp.abs(soft))))
    push_force = (
        slave[:, 6, None, :]
        * master[:, 9, :, None]
        * weight
        * depth_soft
        * (1.0 + DAMPING * jnp.tanh(-closing))
    )
    slave_force = jnp.stack(
        [
            jnp.sum(push_force * normal_x, axis=1),
            jnp.sum(push_force * normal_y, axis=1),
            jnp.sum(push_force * normal_z, axis=1),
        ],
        axis=1,
    )
    reaction = jnp.sum(push_force, axis=2)
    return (slave_force, reaction)


def master_normals(master_tilt):
    scale = lax.rsqrt(
        1.0 + master_tilt[:, 0] * master_tilt[:, 0] + master_tilt[:, 1] * master_tilt[:, 1]
    )
    return jnp.stack([master_tilt[:, 0] * scale, master_tilt[:, 1] * scale, scale], axis=1)


def on_device(
    velocity,
    bulk,
    prestress,
    node_mass,
    slave_pos,
    slave_area,
    seg_count,
    slave_node,
    pair_owner,
    pair_master,
    master_cent,
    master_tilt,
    master_stiff,
    master_node,
):
    count_gx = lax.axis_size("gx")
    count_gy = lax.axis_size("gy")
    devices = count_gx * count_gy
    layers, row_cells, col_cells = bulk.shape
    node_total = layers * row_cells * col_cells
    block_total, _, seg_width = slave_pos.shape
    master_total = master_cent.shape[0]
    slot_depth = (block_total + devices - 1) // devices + 1
    vel_flat = velocity.reshape(3, layers * row_cells, col_cells)
    slave_count = block_total * seg_width
    slave_vel = (
        node_gather(vel_flat, slave_node.reshape(-1))
        .reshape(3, block_total, seg_width)
        .transpose(1, 0, 2)
    )
    held_vel, held_bulk, held_pre, slave_vel = lax.optimization_barrier(
        (velocity, bulk, prestress, slave_vel)
    )
    stacked = jnp.concatenate(
        [held_vel, held_bulk[None], held_pre[None], jnp.ones_like(held_bulk)[None]], axis=0
    )
    padded = padded_2(stacked, (("gx", 2), ("gy", 3)), 1)
    stress, inside = stress_forces(padded)
    master_vel = (
        node_gather(vel_flat, master_node.reshape(-1))
        .reshape(3, master_total, seg_width)
        .transpose(1, 0, 2)
    )
    live_mask = jnp.arange(seg_width, dtype=jnp.int32)[None, :] < seg_count[:, None]
    area_live = jnp.where(live_mask, slave_area, jnp.zeros_like(slave_area))
    slave = jnp.concatenate(
        [slave_pos + TIME_STEP * slave_vel, slave_vel, area_live[:, None, :]], axis=1
    )
    normals = master_normals(master_tilt)
    master_data = jnp.concatenate(
        [master_cent + TIME_STEP * master_vel, normals, master_vel, master_stiff[:, None, :]],
        axis=1,
    )
    owners = pair_owner[:, 0]
    positions = jnp.arange(block_total, dtype=jnp.int32)
    earlier = (owners[:, None] == owners[None, :]) & (positions[None, :] < positions[:, None])
    slot_index = jnp.sum(earlier.astype(jnp.int32), axis=1)
    target_slot = owners * slot_depth + slot_index
    slot_hit = target_slot[None, :] == jnp.arange(devices * slot_depth, dtype=jnp.int32)[:, None]
    source = jnp.sum(jnp.where(slot_hit, positions[None, :], 0), axis=1)
    filled = jnp.any(slot_hit, axis=1)
    tagged = jnp.concatenate(
        [
            slave,
            jnp.broadcast_to(pair_master.astype(jnp.float32)[:, None, None], (block_total, 1, seg_width)),
        ],
        axis=1,
    )
    outgoing = jnp.where(filled[:, None, None], jnp.take(tagged, source, axis=0), 0.0)
    arrived = lax.all_to_all(
        outgoing.reshape(devices, slot_depth, 8, seg_width),
        ("gx", "gy"),
        split_axis=0,
        concat_axis=0,
        tiled=True,
    )
    item_total = devices * slot_depth
    arrived = arrived.reshape(item_total, 8, seg_width)
    picked = jnp.max(arrived[:, 7, :], axis=1).astype(jnp.int32)
    arrived = arrived[:, :7]
    paired = jnp.take(master_data, picked, axis=0)
    forces, reaction = contact_pairs(arrived, paired)
    forces = forces.reshape(item_total, 3, seg_width)
    reaction = reaction.reshape(item_total, seg_width)
    onehot = (picked[:, None] == jnp.arange(master_total, dtype=jnp.int32)[None, :]).astype(
        jnp.float32
    )
    master_sum = jnp.dot(onehot.T, reaction, precision=lax.Precision.HIGHEST)
    master_force = -master_sum[:, None, :] * normals
    master_contact = node_scatter_add(
        master_force.transpose(1, 0, 2).reshape(3, -1),
        master_node.reshape(-1),
        jnp.zeros((3, layers * row_cells, col_cells), jnp.float32),
    )
    returned = lax.all_to_all(
        forces.reshape(devices, slot_depth, 3, seg_width),
        ("gx", "gy"),
        split_axis=0,
        concat_axis=0,
        tiled=True,
    )
    slave_force = jnp.take(returned.reshape(item_total, 3, seg_width), target_slot, axis=0)
    contact = node_scatter_add(
        slave_force.transpose(1, 0, 2).reshape(3, -1), slave_node.reshape(-1), master_contact
    )
    contact_field = contact.reshape(3, layers, row_cells, col_cells)
    velocity_new = velocity + TIME_STEP * (stress + contact_field) / node_mass[None]
    padded_new = padded_2(velocity_new, (("gx", 2), ("gy", 3)), 1)
    node_rate = nodal_rate(padded_new, inside)
    return (velocity_new, node_rate)


def solution(mesh):
    placed = (
        P(None, None, "gx", "gy"),
        P(None, "gx", "gy"),
        P(None, "gx", "gy"),
        P(None, "gx", "gy"),
        P(("gx", "gy"), None, None),
        P(("gx", "gy"), None),
        P(("gx", "gy")),
        P(("gx", "gy"), None),
        P(("gx", "gy"), None),
        P(("gx", "gy")),
        P(("gx", "gy"), None, None),
        P(("gx", "gy"), None, None),
        P(("gx", "gy"), None),
        P(("gx", "gy"), None),
    )
    return jax.shard_map(
        on_device,
        mesh=mesh,
        in_specs=placed,
        out_specs=(P(None, None, "gx", "gy"), P(None, "gx", "gy")),
        check_vma=False,
    )
```

```python
import jax
import jax.numpy as jnp
from jax import lax
from jax.sharding import PartitionSpec as P
from jax.experimental import pallas as pl
from jax.experimental.pallas import tpu as pltpu

LANES = 128
TILE = 4096


def split_pieces(values):
    first = values.astype(jnp.bfloat16)
    rest = values - first.astype(jnp.float32)
    second = rest.astype(jnp.bfloat16)
    third = (rest - second.astype(jnp.float32)).astype(jnp.bfloat16)
    return (first, second, third)


def block_swap(values):
    channels = values.shape[0] // LANES if values.ndim == 2 else values.shape[0]
    if values.ndim == 3:
        return jnp.concatenate(
            [
                jnp.concatenate([values[c, :, :LANES].T, values[c, :, LANES:].T], axis=1)
                for c in range(channels)
            ],
            axis=0,
        )
    return jnp.stack(
        [
            jnp.concatenate(
                [
                    values[c * LANES : (c + 1) * LANES, :LANES].T,
                    values[c * LANES : (c + 1) * LANES, LANES:].T,
                ],
                axis=1,
            )
            for c in range(channels)
        ]
    )


def node_parts(node):
    high = ((node & (2 * LANES - 1)) >> 7) * LANES + (node >> 8)
    return high, node & (LANES - 1)


def gather_kernel(index_ref, field_ref, out_ref):
    node = index_ref[...]
    width = node.shape[1]
    table = block_swap(field_ref[...])
    high_count = table.shape[1]
    channels = out_ref.shape[0]
    high, low = node_parts(node)
    onehot = (
        lax.broadcasted_iota(jnp.int32, (high_count, width), 0) == high
    ).astype(jnp.bfloat16)
    gathered = None
    for piece in split_pieces(table)[:2]:
        part = jnp.dot(piece, onehot, preferred_element_type=jnp.float32)
        gathered = part if gathered is None else gathered + part
    low_hit = lax.broadcasted_iota(jnp.int32, (LANES, width), 0) == low
    for c in range(channels):
        block = gathered[c * LANES : (c + 1) * LANES]
        out_ref[c : c + 1, :] = jnp.sum(jnp.where(low_hit, block, 0.0), axis=0, keepdims=True)


def scatter_kernel(index_ref, force_ref, init_ref, out_ref, acc_ref):
    @pl.when(pl.program_id(0) == 0)
    def _():
        acc_ref[...] = block_swap(init_ref[...])

    node = index_ref[...]
    width = node.shape[1]
    high_count = acc_ref.shape[1]
    channels = force_ref.shape[0]
    high, low = node_parts(node)
    onehot = (
        lax.broadcasted_iota(jnp.int32, (high_count, width), 0) == high
    ).astype(jnp.bfloat16)
    low_hit = lax.broadcasted_iota(jnp.int32, (LANES, width), 0) == low
    total = None
    for piece in split_pieces(force_ref[...])[:2]:
        spread = jnp.concatenate(
            [jnp.where(low_hit, piece[c : c + 1, :], jnp.zeros_like(piece[c : c + 1, :])) for c in range(channels)],
            axis=0,
        )
        part = lax.dot_general(
            spread, onehot, (((1,), (1,)), ((), ())), preferred_element_type=jnp.float32
        )
        total = part if total is None else total + part
    acc_ref[...] += total

    @pl.when(pl.program_id(0) == pl.num_programs(0) - 1)
    def _():
        out_ref[...] = block_swap(acc_ref[...])


def node_gather(field, nodes):
    count = nodes.shape[0]
    tile = 2 * TILE if count >= 2 * TILE else TILE
    padded_count = -(-count // tile) * tile
    nodes = jnp.pad(nodes, (0, padded_count - count))
    channels = field.shape[0]
    return pl.pallas_call(
        gather_kernel,
        grid=(padded_count // tile,),
        in_specs=[
            pl.BlockSpec((1, tile), lambda i: (0, i)),
            pl.BlockSpec(field.shape, lambda i: (0, 0, 0)),
        ],
        out_specs=pl.BlockSpec((channels, tile), lambda i: (0, i)),
        out_shape=jax.ShapeDtypeStruct((channels, padded_count), jnp.float32),
    )(nodes.reshape(1, padded_count), field)[:, :count]


def node_scatter_add(forces, nodes, start):
    channels, count = forces.shape
    tile = 2 * TILE if count >= 2 * TILE else TILE
    padded_count = -(-count // tile) * tile
    nodes = jnp.pad(nodes, (0, padded_count - count))
    forces = jnp.pad(forces, ((0, 0), (0, padded_count - count)))
    return pl.pallas_call(
        scatter_kernel,
        grid=(padded_count // tile,),
        in_specs=[
            pl.BlockSpec((1, tile), lambda i: (0, i)),
            pl.BlockSpec((channels, tile), lambda i: (0, i)),
            pl.BlockSpec(start.shape, lambda i: (0, 0, 0)),
        ],
        out_specs=pl.BlockSpec(start.shape, lambda i: (0, 0, 0)),
        out_shape=jax.ShapeDtypeStruct(start.shape, jnp.float32),
        scratch_shapes=[pltpu.VMEM((channels * LANES, start.shape[2]), jnp.float32)],
    )(nodes.reshape(1, padded_count), forces, start)


TIME_STEP = 0.25
VISCOUS = 0.5
SOFT_GAP = 0.2
REACH_SQ = 1.0
DAMPING = 0.5


def padded_2(block, sides, width):
    for axis, dim in sides:
        count = lax.axis_size(axis)
        forward = [(i, i + 1) for i in range(count - 1)]
        backward = [(target, source) for source, target in forward]
        low = lax.ppermute(
            lax.index_in_dim(block, block.shape[dim] - 1, axis=dim, keepdims=False), axis, forward
        )
        high = lax.ppermute(lax.index_in_dim(block, 0, axis=dim, keepdims=False), axis, backward)
        block = jnp.concatenate(
            [jnp.expand_dims(low, dim), block, jnp.expand_dims(high, dim)], axis=dim
        )
    return block


def pair_mean(values, along):
    length = values.shape[along]
    return 0.5 * (
        lax.slice_in_dim(values, 0, length - 1, axis=along)
        + lax.slice_in_dim(values, 1, length, axis=along)
    )


def pair_diff(values, along):
    length = values.shape[along]
    return lax.slice_in_dim(values, 1, length, axis=along) - lax.slice_in_dim(
        values, 0, length - 1, axis=along
    )


def pair_prod(values, along):
    length = values.shape[along]
    return lax.slice_in_dim(values, 0, length - 1, axis=along) * lax.slice_in_dim(
        values, 1, length, axis=along
    )


def corner_mean(values):
    return pair_mean(pair_mean(pair_mean(values, 0), 1), 2)


def zone_rate(vel):
    rate_x = pair_diff(pair_mean(pair_mean(vel[0], 0), 2), 1)
    rate_y = pair_diff(pair_mean(pair_mean(vel[1], 0), 1), 2)
    rate_z = pair_diff(pair_mean(pair_mean(vel[2], 1), 2), 0)
    return rate_x + rate_y + rate_z


def stress_forces(padded):
    inside = pair_prod(pair_prod(pair_prod(padded[5], 0), 1), 2)
    strain = TIME_STEP * zone_rate(padded[0:3])
    pressure = inside * (
        corner_mean(padded[4]) + corner_mean(padded[3]) * (VISCOUS * strain * strain - strain)
    )
    framed = jnp.pad(pressure, ((1, 1), (0, 0), (0, 0)))
    force_x = -pair_diff(pair_mean(pair_mean(framed, 0), 2), 1)
    force_y = -pair_diff(pair_mean(pair_mean(framed, 0), 1), 2)
    force_z = -pair_diff(pair_mean(pair_mean(framed, 1), 2), 0)
    return (jnp.stack([force_x, force_y, force_z], axis=0), inside)


def nodal_rate(padded_vel, inside):
    rate = inside * zone_rate(padded_vel)
    framed = jnp.pad(rate, ((1, 1), (0, 0), (0, 0)))
    return pair_mean(pair_mean(pair_mean(framed, 0), 1), 2)


def contact_pairs(slave, master):
    delta_x = slave[:, 0, None, :] - master[:, 0, :, None]
    delta_y = slave[:, 1, None, :] - master[:, 1, :, None]
    delta_z = slave[:, 2, None, :] - master[:, 2, :, None]
    normal_x = master[:, 3, :, None]
    normal_y = master[:, 4, :, None]
    normal_z = master[:, 5, :, None]
    dist_sq = delta_x * delta_x + delta_y * delta_y + delta_z * delta_z
    gap_normal = normal_x * delta_x + normal_y * delta_y + normal_z * delta_z
    master_along = (
        master[:, 3] * master[:, 6] + master[:, 4] * master[:, 7] + master[:, 5] * master[:, 8]
    )
    closing = (
        normal_x * slave[:, 3, None, :]
        + normal_y * slave[:, 4, None, :]
        + normal_z * slave[:, 5, None, :]
    ) - master_along[:, :, None]
    weight = jnp.exp(-dist_sq / REACH_SQ)
    soft = gap_normal * (-1.0 / SOFT_GAP)
    depth_soft = SOFT_GAP * (jnp.maximum(soft, 0.0) + jnp.log1p(jnp.exp(-jnp.abs(soft))))
    push_force = (
        slave[:, 6, None, :]
        * master[:, 9, :, None]
        * weight
        * depth_soft
        * (1.0 + DAMPING * jnp.tanh(-closing))
    )
    slave_force = jnp.stack(
        [
            jnp.sum(push_force * normal_x, axis=1),
            jnp.sum(push_force * normal_y, axis=1),
            jnp.sum(push_force * normal_z, axis=1),
        ],
        axis=1,
    )
    reaction = jnp.sum(push_force, axis=2)
    return (slave_force, reaction)


def master_normals(master_tilt):
    scale = lax.rsqrt(
        1.0 + master_tilt[:, 0] * master_tilt[:, 0] + master_tilt[:, 1] * master_tilt[:, 1]
    )
    return jnp.stack([master_tilt[:, 0] * scale, master_tilt[:, 1] * scale, scale], axis=1)


def on_device(
    velocity,
    bulk,
    prestress,
    node_mass,
    slave_pos,
    slave_area,
    seg_count,
    slave_node,
    pair_owner,
    pair_master,
    master_cent,
    master_tilt,
    master_stiff,
    master_node,
):
    count_gx = lax.axis_size("gx")
    count_gy = lax.axis_size("gy")
    devices = count_gx * count_gy
    layers, row_cells, col_cells = bulk.shape
    node_total = layers * row_cells * col_cells
    block_total, _, seg_width = slave_pos.shape
    master_total = master_cent.shape[0]
    slot_depth = (block_total + devices - 1) // devices + 1
    vel_flat = velocity.reshape(3, layers * row_cells, col_cells)
    slave_count = block_total * seg_width
    slave_vel = (
        node_gather(vel_flat, slave_node.reshape(-1))
        .reshape(3, block_total, seg_width)
        .transpose(1, 0, 2)
    )
    held_vel, held_bulk, held_pre, slave_vel = lax.optimization_barrier(
        (velocity, bulk, prestress, slave_vel)
    )
    stacked = jnp.concatenate(
        [held_vel, held_bulk[None], held_pre[None], jnp.ones_like(held_bulk)[None]], axis=0
    )
    padded = padded_2(stacked, (("gx", 2), ("gy", 3)), 1)
    stress, inside = stress_forces(padded)
    master_vel = (
        node_gather(vel_flat, master_node.reshape(-1))
        .reshape(3, master_total, seg_width)
        .transpose(1, 0, 2)
    )
    live_mask = jnp.arange(seg_width, dtype=jnp.int32)[None, :] < seg_count[:, None]
    area_live = jnp.where(live_mask, slave_area, jnp.zeros_like(slave_area))
    slave = jnp.concatenate(
        [slave_pos + TIME_STEP * slave_vel, slave_vel, area_live[:, None, :]], axis=1
    )
    normals = master_normals(master_tilt)
    master_data = jnp.concatenate(
        [master_cent + TIME_STEP * master_vel, normals, master_vel, master_stiff[:, None, :]],
        axis=1,
    )
    owners = pair_owner[:, 0]
    positions = jnp.arange(block_total, dtype=jnp.int32)
    earlier = (owners[:, None] == owners[None, :]) & (positions[None, :] < positions[:, None])
    slot_index = jnp.sum(earlier.astype(jnp.int32), axis=1)
    target_slot = owners * slot_depth + slot_index
    slot_hit = target_slot[None, :] == jnp.arange(devices * slot_depth, dtype=jnp.int32)[:, None]
    source = jnp.sum(jnp.where(slot_hit, positions[None, :], 0), axis=1)
    filled = jnp.any(slot_hit, axis=1)
    tagged = jnp.concatenate(
        [
            slave,
            jnp.broadcast_to(pair_master.astype(jnp.float32)[:, None, None], (block_total, 1, seg_width)),
        ],
        axis=1,
    )
    outgoing = jnp.where(filled[:, None, None], jnp.take(tagged, source, axis=0), 0.0)
    arrived = lax.all_to_all(
        outgoing.reshape(devices, slot_depth, 8, seg_width),
        ("gx", "gy"),
        split_axis=0,
        concat_axis=0,
        tiled=True,
    )
    item_total = devices * slot_depth
    arrived = arrived.reshape(item_total, 8, seg_width)
    picked = jnp.max(arrived[:, 7, :], axis=1).astype(jnp.int32)
    arrived = arrived[:, :7]
    paired = jnp.take(master_data, picked, axis=0)
    forces, reaction = contact_pairs(arrived, paired)
    forces = forces.reshape(item_total, 3, seg_width)
    reaction = reaction.reshape(item_total, seg_width)
    onehot = (picked[:, None] == jnp.arange(master_total, dtype=jnp.int32)[None, :]).astype(
        jnp.float32
    )
    master_sum = jnp.dot(onehot.T, reaction, precision=lax.Precision.HIGHEST)
    master_force = -master_sum[:, None, :] * normals
    master_contact = node_scatter_add(
        master_force.transpose(1, 0, 2).reshape(3, -1),
        master_node.reshape(-1),
        jnp.zeros((3, layers * row_cells, col_cells), jnp.float32),
    )
    returned = lax.all_to_all(
        forces.reshape(devices, slot_depth, 3, seg_width),
        ("gx", "gy"),
        split_axis=0,
        concat_axis=0,
        tiled=True,
    )
    slave_force = jnp.take(returned.reshape(item_total, 3, seg_width), target_slot, axis=0)
    contact = node_scatter_add(
        slave_force.transpose(1, 0, 2).reshape(3, -1), slave_node.reshape(-1), master_contact
    )
    contact_field = contact.reshape(3, layers, row_cells, col_cells)
    velocity_new = velocity + TIME_STEP * (stress + contact_field) / node_mass[None]
    padded_new = padded_2(velocity_new, (("gx", 2), ("gy", 3)), 1)
    node_rate = nodal_rate(padded_new, inside)
    return (velocity_new, node_rate)


def solution(mesh):
    placed = (
        P(None, None, "gx", "gy"),
        P(None, "gx", "gy"),
        P(None, "gx", "gy"),
        P(None, "gx", "gy"),
        P(("gx", "gy"), None, None),
        P(("gx", "gy"), None),
        P(("gx", "gy")),
        P(("gx", "gy"), None),
        P(("gx", "gy"), None),
        P(("gx", "gy")),
        P(("gx", "gy"), None, None),
        P(("gx", "gy"), None, None),
        P(("gx", "gy"), None),
        P(("gx", "gy"), None),
    )
    return jax.shard_map(
        on_device,
        mesh=mesh,
        in_specs=placed,
        out_specs=(P(None, None, "gx", "gy"), P(None, "gx", "gy")),
        check_vma=False,
    )
```

```python
import jax
import jax.numpy as jnp
from jax import lax
from jax.sharding import PartitionSpec as P
from jax.experimental import pallas as pl
from jax.experimental.pallas import tpu as pltpu

LANES = 128
TILE = 4096


def split_pieces(values):
    first = values.astype(jnp.bfloat16)
    rest = values - first.astype(jnp.float32)
    second = rest.astype(jnp.bfloat16)
    third = (rest - second.astype(jnp.float32)).astype(jnp.bfloat16)
    return (first, second, third)


def block_swap(values):
    channels = values.shape[0] // LANES if values.ndim == 2 else values.shape[0]
    if values.ndim == 3:
        return jnp.concatenate(
            [
                jnp.concatenate([values[c, :, :LANES].T, values[c, :, LANES:].T], axis=1)
                for c in range(channels)
            ],
            axis=0,
        )
    return jnp.stack(
        [
            jnp.concatenate(
                [
                    values[c * LANES : (c + 1) * LANES, :LANES].T,
                    values[c * LANES : (c + 1) * LANES, LANES:].T,
                ],
                axis=1,
            )
            for c in range(channels)
        ]
    )


def node_parts(node):
    high = ((node & (2 * LANES - 1)) >> 7) * LANES + (node >> 8)
    return high, node & (LANES - 1)


def gather_kernel(index_ref, field_ref, out_ref):
    node = index_ref[...]
    width = node.shape[1]
    table = block_swap(field_ref[...])
    high_count = table.shape[1]
    channels = out_ref.shape[0]
    high, low = node_parts(node)
    onehot = (
        lax.broadcasted_iota(jnp.int32, (high_count, width), 0) == high
    ).astype(jnp.bfloat16)
    gathered = None
    for piece in split_pieces(table)[:2]:
        part = jnp.dot(piece, onehot, preferred_element_type=jnp.float32)
        gathered = part if gathered is None else gathered + part
    low_hit = lax.broadcasted_iota(jnp.int32, (LANES, width), 0) == low
    for c in range(channels):
        block = gathered[c * LANES : (c + 1) * LANES]
        out_ref[c : c + 1, :] = jnp.sum(jnp.where(low_hit, block, 0.0), axis=0, keepdims=True)


def scatter_kernel(index_ref, force_ref, init_ref, out_ref, acc_ref):
    @pl.when(pl.program_id(0) == 0)
    def _():
        acc_ref[...] = block_swap(init_ref[...])

    node = index_ref[...]
    width = node.shape[1]
    high_count = acc_ref.shape[1]
    channels = force_ref.shape[0]
    high, low = node_parts(node)
    onehot = (
        lax.broadcasted_iota(jnp.int32, (high_count, width), 0) == high
    ).astype(jnp.bfloat16)
    low_hit = lax.broadcasted_iota(jnp.int32, (LANES, width), 0) == low
    total = None
    for piece in split_pieces(force_ref[...])[:2]:
        spread = jnp.concatenate(
            [jnp.where(low_hit, piece[c : c + 1, :], jnp.zeros_like(piece[c : c + 1, :])) for c in range(channels)],
            axis=0,
        )
        part = lax.dot_general(
            spread, onehot, (((1,), (1,)), ((), ())), preferred_element_type=jnp.float32
        )
        total = part if total is None else total + part
    acc_ref[...] += total

    @pl.when(pl.program_id(0) == pl.num_programs(0) - 1)
    def _():
        out_ref[...] = block_swap(acc_ref[...])


def node_gather(field, nodes):
    count = nodes.shape[0]
    tile = 2 * TILE if count >= 2 * TILE else TILE
    padded_count = -(-count // tile) * tile
    nodes = jnp.pad(nodes, (0, padded_count - count))
    channels = field.shape[0]
    return pl.pallas_call(
        gather_kernel,
        grid=(padded_count // tile,),
        in_specs=[
            pl.BlockSpec((1, tile), lambda i: (0, i)),
            pl.BlockSpec(field.shape, lambda i: (0, 0, 0)),
        ],
        out_specs=pl.BlockSpec((channels, tile), lambda i: (0, i)),
        out_shape=jax.ShapeDtypeStruct((channels, padded_count), jnp.float32),
    )(nodes.reshape(1, padded_count), field)[:, :count]


def node_scatter_add(forces, nodes, start):
    channels, count = forces.shape
    tile = 2 * TILE if count >= 2 * TILE else TILE
    padded_count = -(-count // tile) * tile
    nodes = jnp.pad(nodes, (0, padded_count - count))
    forces = jnp.pad(forces, ((0, 0), (0, padded_count - count)))
    return pl.pallas_call(
        scatter_kernel,
        grid=(padded_count // tile,),
        in_specs=[
            pl.BlockSpec((1, tile), lambda i: (0, i)),
            pl.BlockSpec((channels, tile), lambda i: (0, i)),
            pl.BlockSpec(start.shape, lambda i: (0, 0, 0)),
        ],
        out_specs=pl.BlockSpec(start.shape, lambda i: (0, 0, 0)),
        out_shape=jax.ShapeDtypeStruct(start.shape, jnp.float32),
        scratch_shapes=[pltpu.VMEM((channels * LANES, start.shape[2]), jnp.float32)],
    )(nodes.reshape(1, padded_count), forces, start)


TIME_STEP = 0.25
VISCOUS = 0.5
SOFT_GAP = 0.2
REACH_SQ = 1.0
DAMPING = 0.5


def padded_2(block, sides, width):
    for axis, dim in sides:
        count = lax.axis_size(axis)
        forward = [(i, i + 1) for i in range(count - 1)]
        backward = [(target, source) for source, target in forward]
        low = lax.ppermute(
            lax.index_in_dim(block, block.shape[dim] - 1, axis=dim, keepdims=False), axis, forward
        )
        high = lax.ppermute(lax.index_in_dim(block, 0, axis=dim, keepdims=False), axis, backward)
        block = jnp.concatenate(
            [jnp.expand_dims(low, dim), block, jnp.expand_dims(high, dim)], axis=dim
        )
    return block


def pair_mean(values, along):
    length = values.shape[along]
    return 0.5 * (
        lax.slice_in_dim(values, 0, length - 1, axis=along)
        + lax.slice_in_dim(values, 1, length, axis=along)
    )


def pair_diff(values, along):
    length = values.shape[along]
    return lax.slice_in_dim(values, 1, length, axis=along) - lax.slice_in_dim(
        values, 0, length - 1, axis=along
    )


def pair_prod(values, along):
    length = values.shape[along]
    return lax.slice_in_dim(values, 0, length - 1, axis=along) * lax.slice_in_dim(
        values, 1, length, axis=along
    )


def corner_mean(values):
    return pair_mean(pair_mean(pair_mean(values, 0), 1), 2)


def zone_rate(vel):
    rate_x = pair_diff(pair_mean(pair_mean(vel[0], 0), 2), 1)
    rate_y = pair_diff(pair_mean(pair_mean(vel[1], 0), 1), 2)
    rate_z = pair_diff(pair_mean(pair_mean(vel[2], 1), 2), 0)
    return rate_x + rate_y + rate_z


def stress_forces(padded):
    inside = pair_prod(pair_prod(pair_prod(padded[5], 0), 1), 2)
    strain = TIME_STEP * zone_rate(padded[0:3])
    pressure = inside * (
        corner_mean(padded[4]) + corner_mean(padded[3]) * (VISCOUS * strain * strain - strain)
    )
    framed = jnp.pad(pressure, ((1, 1), (0, 0), (0, 0)))
    force_x = -pair_diff(pair_mean(pair_mean(framed, 0), 2), 1)
    force_y = -pair_diff(pair_mean(pair_mean(framed, 0), 1), 2)
    force_z = -pair_diff(pair_mean(pair_mean(framed, 1), 2), 0)
    return (jnp.stack([force_x, force_y, force_z], axis=0), inside)


def nodal_rate(padded_vel, inside):
    rate = inside * zone_rate(padded_vel)
    framed = jnp.pad(rate, ((1, 1), (0, 0), (0, 0)))
    return pair_mean(pair_mean(pair_mean(framed, 0), 1), 2)


def contact_pairs(slave, master):
    delta_x = slave[:, 0, None, :] - master[:, 0, :, None]
    delta_y = slave[:, 1, None, :] - master[:, 1, :, None]
    delta_z = slave[:, 2, None, :] - master[:, 2, :, None]
    normal_x = master[:, 3, :, None]
    normal_y = master[:, 4, :, None]
    normal_z = master[:, 5, :, None]
    dist_sq = delta_x * delta_x + delta_y * delta_y + delta_z * delta_z
    gap_normal = normal_x * delta_x + normal_y * delta_y + normal_z * delta_z
    master_along = (
        master[:, 3] * master[:, 6] + master[:, 4] * master[:, 7] + master[:, 5] * master[:, 8]
    )
    closing = (
        normal_x * slave[:, 3, None, :]
        + normal_y * slave[:, 4, None, :]
        + normal_z * slave[:, 5, None, :]
    ) - master_along[:, :, None]
    weight = jnp.exp(-dist_sq / REACH_SQ)
    soft = gap_normal * (-1.0 / SOFT_GAP)
    depth_soft = SOFT_GAP * (jnp.maximum(soft, 0.0) + jnp.log1p(jnp.exp(-jnp.abs(soft))))
    push_force = (
        slave[:, 6, None, :]
        * master[:, 9, :, None]
        * weight
        * depth_soft
        * (1.0 + DAMPING * jnp.tanh(-closing))
    )
    slave_force = jnp.stack(
        [
            jnp.sum(push_force * normal_x, axis=1),
            jnp.sum(push_force * normal_y, axis=1),
            jnp.sum(push_force * normal_z, axis=1),
        ],
        axis=1,
    )
    reaction = jnp.sum(push_force, axis=2)
    return (slave_force, reaction)


def master_normals(master_tilt):
    scale = lax.rsqrt(
        1.0 + master_tilt[:, 0] * master_tilt[:, 0] + master_tilt[:, 1] * master_tilt[:, 1]
    )
    return jnp.stack([master_tilt[:, 0] * scale, master_tilt[:, 1] * scale, scale], axis=1)


def on_device(
    velocity,
    bulk,
    prestress,
    node_mass,
    slave_pos,
    slave_area,
    seg_count,
    slave_node,
    pair_owner,
    pair_master,
    master_cent,
    master_tilt,
    master_stiff,
    master_node,
):
    count_gx = lax.axis_size("gx")
    count_gy = lax.axis_size("gy")
    devices = count_gx * count_gy
    layers, row_cells, col_cells = bulk.shape
    node_total = layers * row_cells * col_cells
    block_total, _, seg_width = slave_pos.shape
    master_total = master_cent.shape[0]
    slot_depth = (block_total + devices - 1) // devices + 1
    vel_flat = velocity.reshape(3, layers * row_cells, col_cells)
    slave_count = block_total * seg_width
    slave_vel = (
        node_gather(vel_flat, slave_node.reshape(-1))
        .reshape(3, block_total, seg_width)
        .transpose(1, 0, 2)
    )
    held_vel, held_bulk, held_pre, slave_vel = lax.optimization_barrier(
        (velocity, bulk, prestress, slave_vel)
    )
    stacked = jnp.concatenate(
        [held_vel, held_bulk[None], held_pre[None], jnp.ones_like(held_bulk)[None]], axis=0
    )
    padded = padded_2(stacked, (("gx", 2), ("gy", 3)), 1)
    stress, inside = stress_forces(padded)
    master_vel = (
        node_gather(vel_flat, master_node.reshape(-1))
        .reshape(3, master_total, seg_width)
        .transpose(1, 0, 2)
    )
    live_mask = jnp.arange(seg_width, dtype=jnp.int32)[None, :] < seg_count[:, None]
    area_live = jnp.where(live_mask, slave_area, jnp.zeros_like(slave_area))
    slave = jnp.concatenate(
        [slave_pos + TIME_STEP * slave_vel, slave_vel, area_live[:, None, :]], axis=1
    )
    normals = master_normals(master_tilt)
    master_data = jnp.concatenate(
        [master_cent + TIME_STEP * master_vel, normals, master_vel, master_stiff[:, None, :]],
        axis=1,
    )
    owners = pair_owner[:, 0]
    positions = jnp.arange(block_total, dtype=jnp.int32)
    earlier = (owners[:, None] == owners[None, :]) & (positions[None, :] < positions[:, None])
    slot_index = jnp.sum(earlier.astype(jnp.int32), axis=1)
    target_slot = owners * slot_depth + slot_index
    slot_hit = target_slot[None, :] == jnp.arange(devices * slot_depth, dtype=jnp.int32)[:, None]
    source = jnp.sum(jnp.where(slot_hit, positions[None, :], 0), axis=1)
    filled = jnp.any(slot_hit, axis=1)
    tagged = jnp.concatenate(
        [
            slave,
            jnp.broadcast_to(pair_master.astype(jnp.float32)[:, None, None], (block_total, 1, seg_width)),
        ],
        axis=1,
    )
    outgoing = jnp.where(filled[:, None, None], jnp.take(tagged, source, axis=0), 0.0)
    arrived = lax.all_to_all(
        outgoing.reshape(devices, slot_depth, 8, seg_width),
        ("gx", "gy"),
        split_axis=0,
        concat_axis=0,
        tiled=True,
    )
    item_total = devices * slot_depth
    arrived = arrived.reshape(item_total, 8, seg_width)
    picked = jnp.max(arrived[:, 7, :], axis=1).astype(jnp.int32)
    arrived = arrived[:, :7]
    paired = jnp.take(master_data, picked, axis=0)
    forces, reaction = contact_pairs(arrived, paired)
    forces = forces.reshape(item_total, 3, seg_width)
    reaction = reaction.reshape(item_total, seg_width)
    onehot = (picked[:, None] == jnp.arange(master_total, dtype=jnp.int32)[None, :]).astype(
        jnp.float32
    )
    master_sum = jnp.dot(onehot.T, reaction, precision=lax.Precision.HIGHEST)
    master_force = -master_sum[:, None, :] * normals
    master_contact = node_scatter_add(
        master_force.transpose(1, 0, 2).reshape(3, -1),
        master_node.reshape(-1),
        jnp.zeros((3, layers * row_cells, col_cells), jnp.float32),
    )
    returned = lax.all_to_all(
        forces.reshape(devices, slot_depth, 3, seg_width),
        ("gx", "gy"),
        split_axis=0,
        concat_axis=0,
        tiled=True,
    )
    slave_force = jnp.take(returned.reshape(item_total, 3, seg_width), target_slot, axis=0)
    scale = TIME_STEP / node_mass
    base = velocity + TIME_STEP * stress / node_mass[None]
    base, scale, master_contact = lax.optimization_barrier((base, scale, master_contact))
    contact = node_scatter_add(
        slave_force.transpose(1, 0, 2).reshape(3, -1), slave_node.reshape(-1), master_contact
    )
    contact_field = contact.reshape(3, layers, row_cells, col_cells)
    velocity_new = base + scale[None] * contact_field
    padded_new = padded_2(velocity_new, (("gx", 2), ("gy", 3)), 1)
    node_rate = nodal_rate(padded_new, inside)
    return (velocity_new, node_rate)


def solution(mesh):
    placed = (
        P(None, None, "gx", "gy"),
        P(None, "gx", "gy"),
        P(None, "gx", "gy"),
        P(None, "gx", "gy"),
        P(("gx", "gy"), None, None),
        P(("gx", "gy"), None),
        P(("gx", "gy")),
        P(("gx", "gy"), None),
        P(("gx", "gy"), None),
        P(("gx", "gy")),
        P(("gx", "gy"), None, None),
        P(("gx", "gy"), None, None),
        P(("gx", "gy"), None),
        P(("gx", "gy"), None),
    )
    return jax.shard_map(
        on_device,
        mesh=mesh,
        in_specs=placed,
        out_specs=(P(None, None, "gx", "gy"), P(None, "gx", "gy")),
        check_vma=False,
    )
```
